128 devices in a mesh: blk: 32 (over z, y, core), head: 4 (over x).
Axes of the slice: x: 4, y: 4, z: 4, core: 2. Of those that a mesh axis runs over, the one named last changes fastest.
Arguments:
- query_rows: bfloat16 [32768, 1024], P(('blk', 'head')), may hold values from -8 to 8
- key_rows: bfloat16 [32768, 1024], P(('blk', 'head')), may hold values from -8 to 8
- value_rows: bfloat16 [32768, 1024], P(('blk', 'head')), may hold values from -6 to 6
- out_grad: bfloat16 [32768, 1024], P(('blk', 'head')), may hold values from -6 to 6
- expander_device: int32 [256, 4], P('blk'), may hold values from 0 to 31, all different within a row; in each aligned block of 8 rows (0 to 7, 8 to 15, ...) at most 2 rows name the same one
- expander_block: int32 [256, 4], P('blk'), may hold values from 0 to 7
- local_offset: int32 [256, 11], P('blk'), may hold values from -4 to 4
- live_count: int32 [256], P('blk'), may hold values from 3 to 4
- drop_seed: int32 [16, 256, 16], P('head', 'blk'), may hold values from 0 to 1048575
Outputs:
- attended: bfloat16 [32768, 1024], P(('blk', 'head'))
- query_grad: bfloat16 [32768, 1024], P(('blk', 'head'))
- key_grad: bfloat16 [32768, 1024], P(('blk', 'head'))
- value_grad: bfloat16 [32768, 1024], P(('blk', 'head'))
The draws below stay inside these ranges and needn't reach their ends.
Inputs may be any that keep to these rules, and one draw needn't show every extreme that they name: `expander_device`: each row names 4 different devices. Among the rows of one device (aligned blocks of 8 rows), no device is named by more than 2 rows, and in every draw some device is named exactly 2 times by one device's rows.
All inputs are finite; a program needn't handle non-finite values.
Results may differ from the reference program's by a relative error of at most 0.012.
Values may be sent and summed in bfloat16 or wider, within the bound.
No kernel may reach another device: no remote copies, remote signals or barrier semaphores. Data moves between devices by JAX's collectives and lax.ppermute only.
A program may use at most 128 MiB of HBM per device.

```python
import math
import jax
import jax.numpy as jnp
import numpy as np
from jax import lax

H = 16
DH = 64
BS = 128
QB_DEV = 8
L = 11
E = 4
W = 4
NB = 16
PEERS = 32
CAP = 2
BLOCKS = 256
NODES = 32768
HW = 1024


def drawn_pair(key):
    grid_shape = (BLOCKS, BS, H * DH)
    query_seed = jax.random.fold_in(key, 101)
    key_seed = jax.random.fold_in(key, 102)
    query_gain_seed = jax.random.fold_in(key, 103)
    key_gain_seed = jax.random.fold_in(key, 104)
    query_base = jnp.clip(jax.random.normal(query_seed, grid_shape, jnp.float32), -4.0, 4.0)
    key_base = jnp.clip(jax.random.normal(key_seed, grid_shape, jnp.float32), -4.0, 4.0)
    query_gain = jnp.exp(jax.random.uniform(query_gain_seed, (BLOCKS, BS, 1), jnp.float32, -0.69, 0.69))
    key_gain = jnp.exp(jax.random.uniform(key_gain_seed, (BLOCKS, BS, 1), jnp.float32, -0.69, 0.69))
    query_base = query_base * query_gain
    key_base = key_base * key_gain
    return (query_base.reshape(NODES, H * DH), key_base.reshape(NODES, H * DH))


def draw_query_rows(key, part):
    return drawn_pair(key)[0].astype(jnp.bfloat16)


def draw_key_rows(key, part):
    return drawn_pair(key)[1].astype(jnp.bfloat16)


def with_ends(entries, rng, smallest, high):
    longest = entries.shape.index(max(entries.shape))
    spots = []
    for shift in (0, 1):
        where = [jax.random.randint(jax.random.fold_in(rng, axis), (), 0, length) for axis, length in enumerate(entries.shape)]
        where[longest] = (where[longest] + shift) % entries.shape[longest]
        spots.append(tuple(where))
    return entries.at[spots[0]].set(smallest).at[spots[1]].set(high)


def level_of(key, dims, pieces, least, high):
    loudness = 1.0
    for axis_at, parts in pieces:
        draws = jax.random.uniform(jax.random.fold_in(jax.random.fold_in(key, 6), axis_at), (parts,), jnp.float32, least / len(pieces), high / len(pieces))
        loudness = loudness * jnp.repeat(jnp.exp(draws), dims[axis_at] // parts).reshape((-1,) + (1,) * (len(dims) - 1 - axis_at))
    return loudness


def shared_out(key, own, number, rows, count, top, reach, lean):
    ranking = jax.random.permutation(key, count)
    crowded, usual = shares(count, rows * top, reach, lean, True), shares(count, rows * top, reach, lean, False)
    places = jnp.arange(count)

    def named(sizes, turn):
        used = int((sizes > 0).sum())
        fixed = max(1, used // 4)
        shifted = fixed + (places - fixed + turn * (used - fixed)) % max(1, count - fixed)
        return jnp.zeros((count,), jnp.int32).at[ranking[jnp.where(places < fixed, places, shifted)]].set(jnp.asarray(sizes, jnp.int32))

    sizes = jnp.where(number % 4 == 0, named(crowded, number // 4), named(usual, number - number // 4 - 1))
    mixed = jax.random.permutation(jax.random.fold_in(own, 3), count)
    giver, taker = mixed[0:count // 2 * 2:2], mixed[1:count // 2 * 2:2]
    margin = jnp.minimum(sizes[giver] - 1, reach - sizes[taker]) // 2
    margin = jnp.where((giver == ranking[0]) | (taker == ranking[0]) | (sizes[taker] == 0), 0, jnp.maximum(margin, 0))
    shifted = jax.random.randint(jax.random.fold_in(own, 4), (count // 2,), 0, 1 << 20) % (margin + 1)
    sizes = sizes.at[giver].add(-shifted).at[taker].add(shifted)
    members = jnp.searchsorted(jnp.cumsum(sizes), jnp.arange(rows * top), side="right").astype(jnp.int32)
    listing = members.reshape(top, rows).T
    listing = listing[jax.random.permutation(jax.random.fold_in(own, 1), rows)]
    turn = jax.random.randint(jax.random.fold_in(own, 2), (rows, 1), 0, top)
    return jnp.take_along_axis(listing, (jnp.arange(top)[None, :] + turn) % top, axis=1)


def shares(number_of, total, most, slope, full):
    weights = [(1 << 20) // math.isqrt(rank ** slope) + 1 for rank in range(1, number_of + 1)]
    largest = most if full else min(most, max(-(-total // number_of), total * weights[0] // sum(weights)))
    least = 1 if total - largest >= number_of - 1 else 0
    given, spare = [largest] + [least] * (number_of - 1), total - largest - least * (number_of - 1)
    while spare > 0:
        movable = [i for i in range(1, number_of) if given[i] < largest] or [i for i in range(1, number_of) if given[i] < most]
        whole, left = sum([weights[i] for i in movable]), spare
        for i in movable:
            more = min(most - given[i], max(1, left * weights[i] // whole), spare)
            given[i] = given[i] + more
            spare = spare - more
    return np.array(given)


def bell_draw(key, dims, spread, limit, pieces=(), kind=jnp.bfloat16):
    gain = level_of(key, dims, pieces, -0.22, 0.18) if pieces else 1.0
    result = jax.random.normal(key, dims, jnp.float32) * spread * gain
    return jnp.minimum(jnp.maximum(result, -limit), limit).astype(kind)


def setup_inputs(seed: int = 0) -> dict:
    seeds = jax.random.split(jax.random.key(seed), 10)
    query_rows = draw_query_rows(jax.random.fold_in(seeds[9], 71), 0)
    key_rows = draw_key_rows(jax.random.fold_in(seeds[9], 71), 0)
    value_rows = bell_draw(seeds[2], (NODES, HW), 1.0, 6.0, ((0, 128),))
    out_grad = bell_draw(seeds[3], (NODES, HW), 1.0, 6.0, ((0, 128),))
    expander_device_keys = jax.random.split(jax.random.fold_in(seeds[4], 1), BLOCKS // QB_DEV)
    expander_device_turns = jax.random.permutation(jax.random.fold_in(seeds[4], 3), BLOCKS // QB_DEV)
    expander_device = jax.vmap(lambda own, number: shared_out(jax.random.fold_in(seeds[4], 2), own, number, QB_DEV, PEERS, E, CAP, 2))(expander_device_keys, expander_device_turns).reshape((BLOCKS, E))
    expander_block = with_ends(jax.random.randint(seeds[5], (BLOCKS, E), 0, QB_DEV), jax.random.fold_in(seeds[5], 1), 0, QB_DEV - 1).astype(jnp.int32)
    local_offset = with_ends(jax.random.randint(seeds[6], (BLOCKS, L), 0 - W, W + 1), jax.random.fold_in(seeds[6], 1), 0 - W, W).astype(jnp.int32)
    live_count = with_ends(jax.random.randint(seeds[7], (BLOCKS,), 3, E + 1), jax.random.fold_in(seeds[7], 1), 3, E).astype(jnp.int32)
    drop_seed = with_ends(jax.random.randint(seeds[8], (H, BLOCKS, NB), 0, 1048576), jax.random.fold_in(seeds[8], 1), 0, 1048575).astype(jnp.int32)
    return {"query_rows": query_rows, "key_rows": key_rows, "value_rows": value_rows, "out_grad": out_grad, "expander_device": expander_device, "expander_block": expander_block, "local_offset": local_offset, "live_count": live_count, "drop_seed": drop_seed}


KEEP_LEVEL = 102
KEEP_GAIN = 1024.0 / 922.0
MASKED = -1.0e30


def logical_right(value, amount):
    return lax.shift_right_logical(value, jnp.full(value.shape, amount, jnp.int32))


def keep_weights(seed_row, block_size):
    row_index = jnp.arange(block_size, dtype=jnp.int32)[:, None, None]
    col_index = jnp.arange(block_size, dtype=jnp.int32)[None, None, :]
    offset = (row_index * block_size + col_index).astype(jnp.int32)
    hashed = (seed_row[:, None, :, None] * 40503 + offset[None]).astype(jnp.int32)
    hashed = hashed ^ logical_right(hashed, 15)
    hashed = (hashed * 739982445).astype(jnp.int32)
    hashed = hashed ^ logical_right(hashed, 12)
    hashed = (hashed * 695872825).astype(jnp.int32)
    hashed = hashed ^ logical_right(hashed, 15)
    keep_scale = jnp.where((hashed & 1023) >= KEEP_LEVEL, KEEP_GAIN, 0.0).astype(jnp.float32)
    return keep_scale.reshape(seed_row.shape[0], block_size, -1)


def rounded(value):
    return lax.optimization_barrier(value.astype(jnp.bfloat16)).astype(jnp.float32)


def block_terms(query_block, key_block, value_block, grad_block, live_keys, keep_scale, score_scale):
    query_wide = query_block.astype(jnp.float32)
    key_wide = key_block.astype(jnp.float32)
    value_wide = value_block.astype(jnp.float32)
    grad_wide = grad_block.astype(jnp.float32)
    scores = jnp.einsum("qhd,khd->hqk", query_wide, key_wide) * score_scale
    scores = jnp.where(live_keys[None, None, :], scores, MASKED)
    largest = jnp.max(scores, axis=-1, keepdims=True)
    expterm = jnp.exp(scores - largest)
    attention = expterm / jnp.sum(expterm, axis=-1, keepdims=True)
    dropped_wide = rounded(attention * keep_scale)
    attended_full = jnp.einsum("hqk,khd->qhd", dropped_wide, value_wide)
    row_delta = jnp.einsum("qhd,qhd->hq", grad_wide, attended_full)
    drop_grad = jnp.einsum("qhd,khd->hqk", grad_wide, value_wide)
    score_wide = rounded(attention * (drop_grad * keep_scale - row_delta[:, :, None]) * score_scale)
    query_grad = jnp.einsum("hqk,khd->qhd", score_wide, key_wide).astype(jnp.bfloat16)
    key_part = jnp.einsum("hqk,qhd->khd", score_wide, query_wide)
    value_part = jnp.einsum("hqk,qhd->khd", dropped_wide, grad_wide)
    return attended_full.astype(jnp.bfloat16), query_grad, key_part, value_part


def reference(query_rows, key_rows, value_rows, out_grad, expander_device, expander_block, local_offset, live_count, drop_seed):
    score_scale = DH ** -0.5
    slot_count = 1 + L + E
    block_ids = jnp.arange(BLOCKS, dtype=jnp.int32)[:, None]
    near_ids = ((block_ids + local_offset) % BLOCKS).astype(jnp.int32)
    far_ids = (expander_device * QB_DEV + expander_block).astype(jnp.int32)
    slot_blocks = jnp.concatenate([block_ids, near_ids, far_ids], axis=1).astype(jnp.int32)
    slot_index = jnp.arange(slot_count, dtype=jnp.int32)[None, :]
    live_slots = (slot_index <= L) | (slot_index - 1 - L < live_count[:, None])
    far_slots = (jnp.arange(slot_count, dtype=jnp.int32) > L)[:, None, None, None]
    grid_shape = (BLOCKS, BS, H, DH)
    query_grid = query_rows.reshape(grid_shape)
    key_grid = key_rows.reshape(grid_shape)
    value_grid = value_rows.reshape(grid_shape)
    grad_grid = out_grad.reshape(grid_shape)
    seed_rows = jnp.transpose(drop_seed, (1, 0, 2))

    def block_step(running, inputs):
        key_total, value_total = running
        query_block, grad_block, slot_row, live_row, seed_row = inputs
        key_block = key_grid[slot_row].reshape(slot_count * BS, H, DH)
        value_block = value_grid[slot_row].reshape(slot_count * BS, H, DH)
        live_keys = jnp.repeat(live_row, BS)
        keep_scale = keep_weights(seed_row, BS)
        attended_block, query_block_grad, key_part, value_part = block_terms(
            query_block, key_block, value_block, grad_block, live_keys, keep_scale, score_scale)
        key_part = key_part.reshape(slot_count, BS, H, DH)
        value_part = value_part.reshape(slot_count, BS, H, DH)
        key_part = jnp.where(far_slots, rounded(key_part), key_part)
        value_part = jnp.where(far_slots, rounded(value_part), value_part)
        key_total = key_total.at[slot_row].add(key_part)
        value_total = value_total.at[slot_row].add(value_part)
        return (key_total, value_total), (attended_block, query_block_grad)

    start_totals = (jnp.zeros(grid_shape, jnp.float32), jnp.zeros(grid_shape, jnp.float32))
    totals, outputs = lax.scan(block_step, start_totals, (query_grid, grad_grid, slot_blocks, live_slots, seed_rows))
    attended = outputs[0].reshape(NODES, H * DH)
    query_grad = outputs[1].reshape(NODES, H * DH)
    key_grad = totals[0].astype(jnp.bfloat16).reshape(NODES, H * DH)
    value_grad = totals[1].astype(jnp.bfloat16).reshape(NODES, H * DH)
    return (attended, query_grad, key_grad, value_grad)
```

```python
import functools

import jax
import jax.numpy as jnp
from jax import lax
from jax.experimental import pallas as pl
from jax.experimental.pallas import tpu as pltpu
from jax.sharding import PartitionSpec as P

BS = 128
QB_DEV = 8
L = 11
E = 4
W = 4


KEEP_LEVEL = 102
KEEP_GAIN = 1024.0 / 922.0
MASKED = -1e30


def padded(block, sides, width):
    for axis, dim in sides:
        count = lax.axis_size(axis)
        forward = [(i, i + 1) for i in range(count - 1)]
        forward.append((count - 1, 0))
        backward = [(target, source) for source, target in forward]
        low = lax.ppermute(
            lax.slice_in_dim(block, block.shape[dim] - width, None, axis=dim), axis, forward
        )
        high = lax.ppermute(lax.slice_in_dim(block, 0, width, axis=dim), axis, backward)
        block = jnp.concatenate([low, block, high], axis=dim)
    return block


def shifted(block, axis, distance):
    devices = range(lax.axis_size(axis))
    route = [((i - distance) % len(devices), i) for i in devices]
    return lax.ppermute(block, axis, route)


def logical_right(value, amount):
    return lax.shift_right_logical(value, jnp.full(value.shape, amount, jnp.int32))


def keep_weights(seed_row, block_size):
    row_index = jnp.arange(block_size, dtype=jnp.int32)[:, None, None]
    col_index = jnp.arange(block_size, dtype=jnp.int32)[None, None, :]
    offset = row_index * block_size + col_index
    hashed = seed_row[:, None, :, None] * 40503 + offset[None]
    hashed = hashed ^ logical_right(hashed, 15)
    hashed = hashed * 739982445
    hashed = hashed ^ logical_right(hashed, 12)
    hashed = hashed * 695872825
    hashed = hashed ^ logical_right(hashed, 15)
    keep_scale = jnp.where(hashed & 1023 >= KEEP_LEVEL, KEEP_GAIN, 0.0).astype(jnp.float32)
    return keep_scale.reshape(seed_row.shape[0], block_size, -1)


def srl(value, amount):
    return lax.shift_right_logical(value, jnp.full(value.shape, amount, jnp.int32))


def attention_kernel(
    rows_ref, live_ref, seed_ref, q_ref, g_ref, kt_ref, vt_ref,
    att_ref, qg_ref, nk_ref, nv_ref, fk_ref, fv_ref,
    s_scr, keep_scr, drop_scr,
    *, scale, near_count, slot_count, blocks,
):
    h = pl.program_id(0)
    c = pl.program_id(1)
    head_size = q_ref.shape[-1]

    @pl.when(c == 0)
    def _():
        nk_ref[...] = jnp.zeros_like(nk_ref)
        nv_ref[...] = jnp.zeros_like(nv_ref)
        fk_ref[...] = jnp.zeros_like(fk_ref)
        fv_ref[...] = jnp.zeros_like(fv_ref)

    q = q_ref[0]
    g = g_ref[0]
    base = c * slot_count
    seed_base = (h * blocks + c) * slot_count

    def start_of(j):
        return pl.multiple_of(rows_ref[base + j] * BS, BS)

    def keys(j):
        return kt_ref[0, pl.ds(start_of(j), BS), :]

    def values(j):
        return vt_ref[0, pl.ds(start_of(j), BS), :]

    def score_pass(j, m):
        s = lax.dot_general(
            q, keys(j), (((1,), (1,)), ((), ())), preferred_element_type=jnp.float32
        ) * scale
        s = jnp.where(live_ref[base + j] > 0, s, MASKED)
        s_scr[j] = s
        return jnp.maximum(m, jnp.max(s, axis=1, keepdims=True))

    m = lax.fori_loop(0, slot_count, score_pass, jnp.full((BS, 1), -jnp.inf, jnp.float32))

    def exp_pass(j, total):
        e = jnp.exp(s_scr[j] - m)
        s_scr[j] = e
        return total + jnp.sum(e, axis=1, keepdims=True)

    total = lax.fori_loop(0, slot_count, exp_pass, jnp.zeros((BS, 1), jnp.float32))
    inv = 1.0 / total
    offs = (
        lax.broadcasted_iota(jnp.int32, (BS, BS), 0) * BS
        + lax.broadcasted_iota(jnp.int32, (BS, BS), 1)
    )

    def drop_pass(j, acc):
        att = s_scr[j] * inv
        s_scr[j] = att
        word = seed_ref[seed_base + j] * 40503 + offs
        word = word ^ srl(word, 15)
        word = word * 739982445
        word = word ^ srl(word, 12)
        word = word * 695872825
        word = word ^ srl(word, 15)
        keep = jnp.where((word & 1023) >= KEEP_LEVEL, KEEP_GAIN, 0.0).astype(jnp.float32)
        keep_scr[j] = keep
        dropped = (att * keep).astype(jnp.bfloat16)
        drop_scr[j] = dropped
        return acc + jnp.dot(dropped, values(j), preferred_element_type=jnp.float32)

    acc = lax.fori_loop(0, slot_count, drop_pass, jnp.zeros((BS, head_size), jnp.float32))
    att_ref[0] = acc.astype(att_ref.dtype)
    delta = jnp.sum(g.astype(jnp.float32) * acc, axis=1, keepdims=True)

    def grad_terms(j, qacc):
        k = keys(j)
        dg = lax.dot_general(
            g, values(j), (((1,), (1,)), ((), ())), preferred_element_type=jnp.float32
        )
        sg = (s_scr[j] * (dg * keep_scr[j] - delta) * scale).astype(jnp.bfloat16)
        qacc = qacc + jnp.dot(sg, k, preferred_element_type=jnp.float32)
        kp = lax.dot_general(sg, q, (((0,), (0,)), ((), ())), preferred_element_type=jnp.float32)
        vp = lax.dot_general(
            drop_scr[j], g, (((0,), (0,)), ((), ())), preferred_element_type=jnp.float32
        )
        return qacc, kp, vp

    def near_pass(j, qacc):
        qacc, kp, vp = grad_terms(j, qacc)
        at = pl.ds(start_of(j), BS)
        nk_ref[0, at, :] += kp
        nv_ref[0, at, :] += vp
        return qacc

    def far_pass(j, qacc):
        qacc, kp, vp = grad_terms(j, qacc)
        at = pl.ds(pl.multiple_of(start_of(j) - near_count * BS, BS), BS)
        fk_ref[0, at, :] = kp.astype(fk_ref.dtype)
        fv_ref[0, at, :] = vp.astype(fv_ref.dtype)
        return qacc

    qacc = lax.fori_loop(0, L + 1, near_pass, jnp.zeros((BS, head_size), jnp.float32))
    qacc = lax.fori_loop(L + 1, slot_count, far_pass, qacc)
    qg_ref[0] = qacc.astype(qg_ref.dtype)


def block_attention(rows, live, seeds, q, g, kt, vt, *, near_count, far_count, scale):
    heads, row_count, head_size = q.shape
    blocks = row_count // BS
    slot_count = 1 + L + E
    kernel = functools.partial(
        attention_kernel, scale=scale, near_count=near_count, slot_count=slot_count, blocks=blocks
    )
    q_spec = pl.BlockSpec((1, BS, head_size), lambda h, c, *_: (h, c, 0))
    table_spec = pl.BlockSpec((1, kt.shape[1], head_size), lambda h, c, *_: (h, 0, 0))
    near_spec = pl.BlockSpec((1, near_count * BS, head_size), lambda h, c, *_: (h, 0, 0))
    far_spec = pl.BlockSpec((1, far_count * BS, head_size), lambda h, c, *_: (h, 0, 0))
    grid_spec = pltpu.PrefetchScalarGridSpec(
        num_scalar_prefetch=3,
        grid=(heads, blocks),
        in_specs=[q_spec, q_spec, table_spec, table_spec],
        out_specs=[q_spec, q_spec, near_spec, near_spec, far_spec, far_spec],
        scratch_shapes=[
            pltpu.VMEM((slot_count, BS, BS), jnp.float32),
            pltpu.VMEM((slot_count, BS, BS), jnp.float32),
            pltpu.VMEM((slot_count, BS, BS), jnp.bfloat16),
        ],
    )
    flops = 6 * 2 * heads * blocks * slot_count * BS * BS * head_size
    cost = pl.CostEstimate(
        flops=flops,
        transcendentals=heads * blocks * slot_count * BS * BS,
        bytes_accessed=2 * (q.size * 4 + kt.size * 2) + 4 * heads * (near_count + far_count) * BS * head_size * 2,
    )
    return pl.pallas_call(
        kernel,
        grid_spec=grid_spec,
        out_shape=[
            jax.ShapeDtypeStruct(q.shape, jnp.bfloat16),
            jax.ShapeDtypeStruct(q.shape, jnp.bfloat16),
            jax.ShapeDtypeStruct((heads, near_count * BS, head_size), jnp.float32),
            jax.ShapeDtypeStruct((heads, near_count * BS, head_size), jnp.float32),
            jax.ShapeDtypeStruct((heads, far_count * BS, head_size), jnp.bfloat16),
            jax.ShapeDtypeStruct((heads, far_count * BS, head_size), jnp.bfloat16),
        ],
        compiler_params=pltpu.CompilerParams(
            dimension_semantics=("arbitrary", "arbitrary"), vmem_limit_bytes=48 * 1024 * 1024
        ),
        cost_estimate=cost,
    )(rows, live, seeds, q, g, kt, vt)


def on_device(
    query_rows,
    key_rows,
    value_rows,
    out_grad,
    expander_device,
    expander_block,
    local_offset,
    live_count,
    drop_seed,
):
    head_count = lax.axis_size("head")
    head_index = lax.axis_index("head")
    share_rows = query_rows.shape[0]
    local_width = query_rows.shape[1] // head_count
    local_heads = drop_seed.shape[0]
    head_size = local_width // local_heads
    score_scale = head_size ** (-0.5)
    slot_count = 1 + L + E
    gathered = (
        lax.all_gather(query_rows, "head", axis=0, tiled=True),
        lax.all_gather(key_rows, "head", axis=0, tiled=True),
        lax.all_gather(value_rows, "head", axis=0, tiled=True),
        lax.all_gather(out_grad, "head", axis=0, tiled=True),
    )
    first_col = head_index * local_width
    query_local, key_local, value_local, grad_local = [
        lax.dynamic_slice_in_dim(member, first_col, local_width, 1) for member in gathered
    ]
    peer_count = lax.axis_size("blk")
    capacity = min(QB_DEV, max(2, (2 * QB_DEV * E + peer_count - 1) // peer_count))
    flat_device = expander_device.reshape(-1)
    matches = (flat_device[:, None] == jnp.arange(peer_count, dtype=jnp.int32)[None, :]).astype(
        jnp.int32
    )
    before = jnp.cumsum(matches, axis=0) - matches
    slot_rank = jnp.sum(before * matches, axis=1)
    far_position = flat_device * capacity + slot_rank
    far_live = jnp.arange(E, dtype=jnp.int32)[None, :] < live_count[:, None]
    asked_block = jnp.where(far_live, expander_block, -1)
    wanted = (
        jnp.full((peer_count * capacity,), -1, jnp.int32)
        .at[far_position]
        .set(asked_block.reshape(-1))
    )
    wanted_here = lax.all_to_all(
        wanted.reshape(peer_count, capacity), "blk", split_axis=0, concat_axis=0, tiled=True
    )
    key_blocks = key_local.reshape(QB_DEV, BS, local_width)
    value_blocks = value_local.reshape(QB_DEV, BS, local_width)
    stacked = jnp.stack([key_blocks, value_blocks], axis=1)
    widened = padded(stacked, (("blk", 0),), W)
    wanted_flat = wanted_here.reshape(-1)
    chosen = jnp.clip(wanted_flat, 0, QB_DEV - 1)
    asked_mask = (wanted_flat >= 0)[:, None, None]
    zero_block = jnp.zeros((), jnp.bfloat16)
    reply_shape = (peer_count, capacity, BS, local_width)
    far_key, far_value = (
        lax.all_to_all(
            jnp.where(asked_mask, key_blocks[chosen], zero_block).reshape(reply_shape),
            "blk",
            split_axis=0,
            concat_axis=0,
            tiled=True,
        ),
        lax.all_to_all(
            jnp.where(asked_mask, value_blocks[chosen], zero_block).reshape(reply_shape),
            "blk",
            split_axis=0,
            concat_axis=0,
            tiled=True,
        ),
    )
    near_count = QB_DEV + 2 * W
    far_total_count = peer_count * capacity
    key_table = jnp.concatenate(
        [widened[:, 0], far_key.reshape(far_total_count, BS, local_width)], axis=0
    )
    value_table = jnp.concatenate(
        [widened[:, 1], far_value.reshape(far_total_count, BS, local_width)], axis=0
    )
    local_block = jnp.arange(QB_DEV, dtype=jnp.int32)[:, None]
    self_slot = local_block + W
    near_slot = local_block + W + local_offset
    far_slot = near_count + far_position.reshape(QB_DEV, E)
    table_rows = jnp.concatenate([self_slot, near_slot, far_slot], axis=1)
    slot_number = jnp.arange(slot_count, dtype=jnp.int32)[None, :]
    live_slots = (slot_number <= L) | (slot_number - 1 - L < live_count[:, None])
    slot_rows = table_rows.reshape(-1).astype(jnp.int32)
    live_flat = live_slots.reshape(-1).astype(jnp.int32)
    seed_flat = drop_seed.reshape(-1).astype(jnp.int32)
    table_count = key_table.shape[0]

    def head_major(rows):
        return rows.reshape(-1, local_heads, head_size).transpose(1, 0, 2)

    att_out, qg_out, nk, nv, fk, fv = block_attention(
        slot_rows,
        live_flat,
        seed_flat,
        head_major(query_local),
        head_major(grad_local),
        head_major(key_table.reshape(table_count * BS, local_width)),
        head_major(value_table.reshape(table_count * BS, local_width)),
        near_count=near_count,
        far_count=far_total_count,
        scale=score_scale,
    )

    def row_major(arr, count):
        return arr.reshape(local_heads, count, BS, head_size).transpose(1, 2, 0, 3).reshape(
            count, BS, local_width
        )

    near_total = jnp.stack([row_major(nk, near_count), row_major(nv, near_count)], axis=1)
    far_key_total = row_major(fk, far_total_count)
    far_value_total = row_major(fv, far_total_count)
    outputs = (
        row_major(att_out, QB_DEV),
        row_major(qg_out, QB_DEV),
    )
    back_key, back_value = (
        lax.all_to_all(
            far_key_total.reshape(reply_shape), "blk", split_axis=0, concat_axis=0, tiled=True
        ),
        lax.all_to_all(
            far_value_total.reshape(reply_shape), "blk", split_axis=0, concat_axis=0, tiled=True
        ),
    )
    owner_match = (
        jnp.arange(QB_DEV, dtype=jnp.int32)[:, None] == wanted_here.reshape(1, -1)
    ).astype(jnp.bfloat16)
    far_key_sum = jnp.dot(
        owner_match,
        back_key.reshape(far_total_count, BS * local_width),
        preferred_element_type=jnp.float32,
    )
    far_value_sum = jnp.dot(
        owner_match,
        back_value.reshape(far_total_count, BS * local_width),
        preferred_element_type=jnp.float32,
    )
    from_below = shifted(near_total[QB_DEV + W :].astype(jnp.bfloat16), "blk", 1).astype(
        jnp.float32
    )
    from_above = shifted(near_total[:W].astype(jnp.bfloat16), "blk", -1).astype(jnp.float32)
    own_total = near_total[W : W + QB_DEV]
    own_total = own_total.at[:W].add(from_below)
    own_total = own_total.at[QB_DEV - W :].add(from_above)
    block_rows = QB_DEV * BS
    key_grad = (own_total[:, 0].reshape(QB_DEV, BS * local_width) + far_key_sum).astype(
        jnp.bfloat16
    )
    value_grad = (own_total[:, 1].reshape(QB_DEV, BS * local_width) + far_value_sum).astype(
        jnp.bfloat16
    )
    results = (
        outputs[0].reshape(block_rows, local_width),
        outputs[1].reshape(block_rows, local_width),
        key_grad.reshape(block_rows, local_width),
        value_grad.reshape(block_rows, local_width),
    )
    full_results = (
        lax.all_gather(results[0], "head", axis=1, tiled=True),
        lax.all_gather(results[1], "head", axis=1, tiled=True),
        lax.all_gather(results[2], "head", axis=1, tiled=True),
        lax.all_gather(results[3], "head", axis=1, tiled=True),
    )
    first_row = head_index * share_rows
    return tuple(
        (lax.dynamic_slice_in_dim(member, first_row, share_rows, 0) for member in full_results)
    )


def solution(mesh):
    in_specs = (
        P(("blk", "head"), None),
        P(("blk", "head"), None),
        P(("blk", "head"), None),
        P(("blk", "head"), None),
        P("blk", None),
        P("blk", None),
        P("blk", None),
        P("blk"),
        P("head", "blk", None),
    )
    out_specs = (
        P(("blk", "head"), None),
        P(("blk", "head"), None),
        P(("blk", "head"), None),
        P(("blk", "head"), None),
    )
    return jax.shard_map(
        on_device, mesh=mesh, in_specs=in_specs, out_specs=out_specs, check_vma=False
    )
```

```python
import functools

import jax
import jax.numpy as jnp
from jax import lax
from jax.experimental import pallas as pl
from jax.experimental.pallas import tpu as pltpu
from jax.sharding import PartitionSpec as P

BS = 128
QB_DEV = 8
L = 11
E = 4
W = 4


KEEP_LEVEL = 102
KEEP_GAIN = 1024.0 / 922.0
MASKED = -1e30


def padded(block, sides, width):
    for axis, dim in sides:
        count = lax.axis_size(axis)
        forward = [(i, i + 1) for i in range(count - 1)]
        forward.append((count - 1, 0))
        backward = [(target, source) for source, target in forward]
        low = lax.ppermute(
            lax.slice_in_dim(block, block.shape[dim] - width, None, axis=dim), axis, forward
        )
        high = lax.ppermute(lax.slice_in_dim(block, 0, width, axis=dim), axis, backward)
        block = jnp.concatenate([low, block, high], axis=dim)
    return block


def shifted(block, axis, distance):
    devices = range(lax.axis_size(axis))
    route = [((i - distance) % len(devices), i) for i in devices]
    return lax.ppermute(block, axis, route)


def logical_right(value, amount):
    return lax.shift_right_logical(value, jnp.full(value.shape, amount, jnp.int32))


def keep_weights(seed_row, block_size):
    row_index = jnp.arange(block_size, dtype=jnp.int32)[:, None, None]
    col_index = jnp.arange(block_size, dtype=jnp.int32)[None, None, :]
    offset = row_index * block_size + col_index
    hashed = seed_row[:, None, :, None] * 40503 + offset[None]
    hashed = hashed ^ logical_right(hashed, 15)
    hashed = hashed * 739982445
    hashed = hashed ^ logical_right(hashed, 12)
    hashed = hashed * 695872825
    hashed = hashed ^ logical_right(hashed, 15)
    keep_scale = jnp.where(hashed & 1023 >= KEEP_LEVEL, KEEP_GAIN, 0.0).astype(jnp.float32)
    return keep_scale.reshape(seed_row.shape[0], block_size, -1)


def unrolled(body, carry, first, last):
    for j in range(first, last):
        carry = body(j, carry)
    return carry


def srl(value, amount):
    return lax.shift_right_logical(value, jnp.full(value.shape, amount, jnp.int32))


def attention_kernel(
    rows_ref, count_ref, seed_ref, q_ref, g_ref, kt_ref, vt_ref,
    att_ref, qg_ref, nk_ref, nv_ref, fk_ref, fv_ref,
    s_scr, keep_scr, drop_scr,
    *, scale, near_count, slot_count, blocks, use_hash=True,
):
    h = pl.program_id(0)
    c = pl.program_id(1)
    head_size = q_ref.shape[-1]

    @pl.when(c == 0)
    def _():
        nk_ref[...] = jnp.zeros_like(nk_ref)
        nv_ref[...] = jnp.zeros_like(nv_ref)
        fk_ref[...] = jnp.zeros_like(fk_ref)
        fv_ref[...] = jnp.zeros_like(fv_ref)

    q = q_ref[0] * jnp.asarray(scale, q_ref.dtype)
    g = g_ref[0]
    q_t = q.T
    g_t = g.T
    base = c * slot_count
    seed_base = (h * blocks + c) * slot_count
    live_end = L + 1 + count_ref[c]

    def start_of(j):
        return pl.multiple_of(rows_ref[base + j] * BS, BS)

    def keys(j):
        return kt_ref[0, pl.ds(start_of(j), BS), :]

    def values(j):
        return vt_ref[0, pl.ds(start_of(j), BS), :]

    def score_pass(j, m):
        s = lax.dot_general(
            q, keys(j), (((1,), (1,)), ((), ())), preferred_element_type=jnp.float32
        )
        if j > L:
            s = jnp.where(j < live_end, s, MASKED)
        s_scr[j] = s
        return jnp.maximum(m, s)

    m = unrolled(score_pass, jnp.full((BS, BS), -jnp.inf, jnp.float32), 0, slot_count)
    m = jnp.max(m, axis=1, keepdims=True)

    def exp_pass(j, total):
        e = jnp.exp(s_scr[j] - m)
        s_scr[j] = e
        return total + e

    total = unrolled(exp_pass, jnp.zeros((BS, BS), jnp.float32), 0, slot_count)
    inv = 1.0 / jnp.sum(total, axis=1, keepdims=True)
    offs = (
        lax.broadcasted_iota(jnp.int32, (BS, BS), 0) * BS
        + lax.broadcasted_iota(jnp.int32, (BS, BS), 1)
    )

    def drop_pass(j, acc):
        att = s_scr[j] * inv
        s_scr[j] = att
        if use_hash:
            word = seed_ref[seed_base + j] * 40503 + offs
            word = word ^ srl(word, 15)
            word = word * 739982445
            word = word ^ srl(word, 12)
            word = word * 695872825
            word = word ^ srl(word, 15)
            keep = jnp.where((word & 1023) >= KEEP_LEVEL, KEEP_GAIN, 0.0).astype(jnp.float32)
        else:
            keep = jnp.where(offs >= seed_ref[seed_base + j], KEEP_GAIN, 0.0).astype(jnp.float32)
        keep_scr[j] = keep
        dropped = (att * keep).astype(jnp.bfloat16)
        drop_scr[j] = dropped
        return acc + jnp.dot(dropped, values(j), preferred_element_type=jnp.float32)

    acc = unrolled(drop_pass, jnp.zeros((BS, head_size), jnp.float32), 0, slot_count)
    att_ref[0] = acc.astype(att_ref.dtype)
    delta = jnp.sum(g.astype(jnp.float32) * acc, axis=1, keepdims=True)

    def grad_terms(j, qacc):
        dg = lax.dot_general(
            g, values(j), (((1,), (1,)), ((), ())), preferred_element_type=jnp.float32
        )
        sg = (s_scr[j] * (dg * keep_scr[j] - delta)).astype(jnp.bfloat16)
        qacc = qacc + jnp.dot(sg, keys(j), preferred_element_type=jnp.float32)
        kp = jnp.dot(q_t, sg, preferred_element_type=jnp.float32)
        vp = jnp.dot(g_t, drop_scr[j], preferred_element_type=jnp.float32)
        return qacc, kp, vp

    def near_pass(j, qacc):
        qacc, kp, vp = grad_terms(j, qacc)
        at = rows_ref[base + j]
        nk_ref[0, at] += kp
        nv_ref[0, at] += vp
        return qacc

    def far_pass(j, qacc):
        qacc, kp, vp = grad_terms(j, qacc)
        at = rows_ref[base + j] - near_count
        fk_ref[0, at] = kp.astype(fk_ref.dtype)
        fv_ref[0, at] = vp.astype(fv_ref.dtype)
        return qacc

    qacc = unrolled(near_pass, jnp.zeros((BS, head_size), jnp.float32), 0, L + 1)
    qacc = unrolled(far_pass, qacc, L + 1, slot_count)
    qg_ref[0] = (qacc * scale).astype(qg_ref.dtype)


def block_attention(rows, counts, seeds, q, g, kt, vt, *, near_count, far_count, scale, use_hash=True):
    heads, row_count, head_size = q.shape
    blocks = row_count // BS
    slot_count = 1 + L + E
    kernel = functools.partial(
        attention_kernel, scale=scale, near_count=near_count, slot_count=slot_count,
        blocks=blocks, use_hash=use_hash,
    )
    q_spec = pl.BlockSpec((1, BS, head_size), lambda h, c, *_: (h, c, 0))
    table_spec = pl.BlockSpec((1, kt.shape[1], head_size), lambda h, c, *_: (h, 0, 0))
    near_spec = pl.BlockSpec((1, near_count, head_size, BS), lambda h, c, *_: (h, 0, 0, 0))
    far_spec = pl.BlockSpec((1, far_count, head_size, BS), lambda h, c, *_: (h, 0, 0, 0))
    grid_spec = pltpu.PrefetchScalarGridSpec(
        num_scalar_prefetch=3,
        grid=(heads, blocks),
        in_specs=[q_spec, q_spec, table_spec, table_spec],
        out_specs=[q_spec, q_spec, near_spec, near_spec, far_spec, far_spec],
        scratch_shapes=[
            pltpu.VMEM((slot_count, BS, BS), jnp.float32),
            pltpu.VMEM((slot_count, BS, BS), jnp.float32),
            pltpu.VMEM((slot_count, BS, BS), jnp.bfloat16),
        ],
    )
    flops = 6 * 2 * heads * blocks * slot_count * BS * BS * head_size
    cost = pl.CostEstimate(
        flops=flops,
        transcendentals=heads * blocks * slot_count * BS * BS,
        bytes_accessed=2 * (q.size * 4 + kt.size * 2) + 4 * heads * (near_count + far_count) * BS * head_size * 2,
    )
    return pl.pallas_call(
        kernel,
        grid_spec=grid_spec,
        out_shape=[
            jax.ShapeDtypeStruct(q.shape, jnp.bfloat16),
            jax.ShapeDtypeStruct(q.shape, jnp.bfloat16),
            jax.ShapeDtypeStruct((heads, near_count, head_size, BS), jnp.float32),
            jax.ShapeDtypeStruct((heads, near_count, head_size, BS), jnp.float32),
            jax.ShapeDtypeStruct((heads, far_count, head_size, BS), jnp.bfloat16),
            jax.ShapeDtypeStruct((heads, far_count, head_size, BS), jnp.bfloat16),
        ],
        compiler_params=pltpu.CompilerParams(
            dimension_semantics=("arbitrary", "arbitrary"), vmem_limit_bytes=48 * 1024 * 1024
        ),
        cost_estimate=cost,
    )(rows, counts, seeds, q, g, kt, vt)


def on_device(
    query_rows,
    key_rows,
    value_rows,
    out_grad,
    expander_device,
    expander_block,
    local_offset,
    live_count,
    drop_seed,
):
    head_count = lax.axis_size("head")
    head_index = lax.axis_index("head")
    share_rows = query_rows.shape[0]
    local_width = query_rows.shape[1] // head_count
    local_heads = drop_seed.shape[0]
    head_size = local_width // local_heads
    score_scale = head_size ** (-0.5)
    slot_count = 1 + L + E
    gathered = (
        lax.all_gather(query_rows, "head", axis=0, tiled=True),
        lax.all_gather(key_rows, "head", axis=0, tiled=True),
        lax.all_gather(value_rows, "head", axis=0, tiled=True),
        lax.all_gather(out_grad, "head", axis=0, tiled=True),
    )
    first_col = head_index * local_width
    query_local, key_local, value_local, grad_local = [
        lax.dynamic_slice_in_dim(member, first_col, local_width, 1) for member in gathered
    ]
    peer_count = lax.axis_size("blk")
    capacity = min(QB_DEV, max(2, (2 * QB_DEV * E + peer_count - 1) // peer_count))
    flat_device = expander_device.reshape(-1)
    matches = (flat_device[:, None] == jnp.arange(peer_count, dtype=jnp.int32)[None, :]).astype(
        jnp.int32
    )
    before = jnp.cumsum(matches, axis=0) - matches
    slot_rank = jnp.sum(before * matches, axis=1)
    far_position = flat_device * capacity + slot_rank
    far_live = jnp.arange(E, dtype=jnp.int32)[None, :] < live_count[:, None]
    asked_block = jnp.where(far_live, expander_block, -1)
    wanted = (
        jnp.full((peer_count * capacity,), -1, jnp.int32)
        .at[far_position]
        .set(asked_block.reshape(-1))
    )
    wanted_here = lax.all_to_all(
        wanted.reshape(peer_count, capacity), "blk", split_axis=0, concat_axis=0, tiled=True
    )
    key_blocks = key_local.reshape(QB_DEV, BS, local_width)
    value_blocks = value_local.reshape(QB_DEV, BS, local_width)
    stacked = jnp.stack([key_blocks, value_blocks], axis=1)
    widened = padded(stacked, (("blk", 0),), W)
    wanted_flat = wanted_here.reshape(-1)
    chosen = jnp.clip(wanted_flat, 0, QB_DEV - 1)
    asked_mask = (wanted_flat >= 0)[:, None, None]
    zero_block = jnp.zeros((), jnp.bfloat16)
    reply_shape = (peer_count, capacity, BS, local_width)
    far_key, far_value = (
        lax.all_to_all(
            jnp.where(asked_mask, key_blocks[chosen], zero_block).reshape(reply_shape),
            "blk",
            split_axis=0,
            concat_axis=0,
            tiled=True,
        ),
        lax.all_to_all(
            jnp.where(asked_mask, value_blocks[chosen], zero_block).reshape(reply_shape),
            "blk",
            split_axis=0,
            concat_axis=0,
            tiled=True,
        ),
    )
    near_count = QB_DEV + 2 * W
    far_total_count = peer_count * capacity
    key_table = jnp.concatenate(
        [widened[:, 0], far_key.reshape(far_total_count, BS, local_width)], axis=0
    )
    value_table = jnp.concatenate(
        [widened[:, 1], far_value.reshape(far_total_count, BS, local_width)], axis=0
    )
    local_block = jnp.arange(QB_DEV, dtype=jnp.int32)[:, None]
    self_slot = local_block + W
    near_slot = local_block + W + local_offset
    far_slot = near_count + far_position.reshape(QB_DEV, E)
    table_rows = jnp.concatenate([self_slot, near_slot, far_slot], axis=1)
    slot_number = jnp.arange(slot_count, dtype=jnp.int32)[None, :]
    live_slots = (slot_number <= L) | (slot_number - 1 - L < live_count[:, None])
    slot_rows = table_rows.reshape(-1).astype(jnp.int32)
    seed_flat = drop_seed.reshape(-1).astype(jnp.int32)
    table_count = key_table.shape[0]

    def head_major(rows):
        return rows.reshape(-1, local_heads, head_size).transpose(1, 0, 2)

    att_out, qg_out, nk, nv, fk, fv = block_attention(
        slot_rows,
        live_count.astype(jnp.int32),
        seed_flat,
        head_major(query_local),
        head_major(grad_local),
        head_major(key_table.reshape(table_count * BS, local_width)),
        head_major(value_table.reshape(table_count * BS, local_width)),
        near_count=near_count,
        far_count=far_total_count,
        scale=score_scale,
    )

    def row_major(arr, count):
        return arr.reshape(local_heads, count, BS, head_size).transpose(1, 2, 0, 3).reshape(
            count, BS, local_width
        )

    def from_columns(arr, count):
        return arr.transpose(1, 3, 0, 2).reshape(count, BS, local_width)

    near_total = jnp.stack([from_columns(nk, near_count), from_columns(nv, near_count)], axis=1)
    far_key_total = from_columns(fk, far_total_count)
    far_value_total = from_columns(fv, far_total_count)
    outputs = (
        row_major(att_out, QB_DEV),
        row_major(qg_out, QB_DEV),
    )
    back_key, back_value = (
        lax.all_to_all(
            far_key_total.reshape(reply_shape), "blk", split_axis=0, concat_axis=0, tiled=True
        ),
        lax.all_to_all(
            far_value_total.reshape(reply_shape), "blk", split_axis=0, concat_axis=0, tiled=True
        ),
    )
    owner_match = (
        jnp.arange(QB_DEV, dtype=jnp.int32)[:, None] == wanted_here.reshape(1, -1)
    ).astype(jnp.bfloat16)
    far_key_sum = jnp.dot(
        owner_match,
        back_key.reshape(far_total_count, BS * local_width),
        preferred_element_type=jnp.float32,
    )
    far_value_sum = jnp.dot(
        owner_match,
        back_value.reshape(far_total_count, BS * local_width),
        preferred_element_type=jnp.float32,
    )
    from_below = shifted(near_total[QB_DEV + W :].astype(jnp.bfloat16), "blk", 1).astype(
        jnp.float32
    )
    from_above = shifted(near_total[:W].astype(jnp.bfloat16), "blk", -1).astype(jnp.float32)
    own_total = near_total[W : W + QB_DEV]
    own_total = own_total.at[:W].add(from_below)
    own_total = own_total.at[QB_DEV - W :].add(from_above)
    block_rows = QB_DEV * BS
    key_grad = (own_total[:, 0].reshape(QB_DEV, BS * local_width) + far_key_sum).astype(
        jnp.bfloat16
    )
    value_grad = (own_total[:, 1].reshape(QB_DEV, BS * local_width) + far_value_sum).astype(
        jnp.bfloat16
    )
    results = (
        outputs[0].reshape(block_rows, local_width),
        outputs[1].reshape(block_rows, local_width),
        key_grad.reshape(block_rows, local_width),
        value_grad.reshape(block_rows, local_width),
    )
    full_results = (
        lax.all_gather(results[0], "head", axis=1, tiled=True),
        lax.all_gather(results[1], "head", axis=1, tiled=True),
        lax.all_gather(results[2], "head", axis=1, tiled=True),
        lax.all_gather(results[3], "head", axis=1, tiled=True),
    )
    first_row = head_index * share_rows
    return tuple(
        (lax.dynamic_slice_in_dim(member, first_row, share_rows, 0) for member in full_results)
    )


def solution(mesh):
    in_specs = (
        P(("blk", "head"), None),
        P(("blk", "head"), None),
        P(("blk", "head"), None),
        P(("blk", "head"), None),
        P("blk", None),
        P("blk", None),
        P("blk", None),
        P("blk"),
        P("head", "blk", None),
    )
    out_specs = (
        P(("blk", "head"), None),
        P(("blk", "head"), None),
        P(("blk", "head"), None),
        P(("blk", "head"), None),
    )
    return jax.shard_map(
        on_device, mesh=mesh, in_specs=in_specs, out_specs=out_specs, check_vma=False
    )
```

```python
import functools

import jax
import jax.numpy as jnp
from jax import lax
from jax.experimental import pallas as pl
from jax.experimental.pallas import tpu as pltpu
from jax.sharding import PartitionSpec as P

BS = 128
QB_DEV = 8
L = 11
E = 4
W = 4


KEEP_LEVEL = 102
KEEP_GAIN = 1024.0 / 922.0
MASKED = -1e30


def padded(block, sides, width):
    for axis, dim in sides:
        count = lax.axis_size(axis)
        forward = [(i, i + 1) for i in range(count - 1)]
        forward.append((count - 1, 0))
        backward = [(target, source) for source, target in forward]
        low = lax.ppermute(
            lax.slice_in_dim(block, block.shape[dim] - width, None, axis=dim), axis, forward
        )
        high = lax.ppermute(lax.slice_in_dim(block, 0, width, axis=dim), axis, backward)
        block = jnp.concatenate([low, block, high], axis=dim)
    return block


def shifted(block, axis, distance):
    devices = range(lax.axis_size(axis))
    route = [((i - distance) % len(devices), i) for i in devices]
    return lax.ppermute(block, axis, route)


def logical_right(value, amount):
    return lax.shift_right_logical(value, jnp.full(value.shape, amount, jnp.int32))


def keep_weights(seed_row, block_size):
    row_index = jnp.arange(block_size, dtype=jnp.int32)[:, None, None]
    col_index = jnp.arange(block_size, dtype=jnp.int32)[None, None, :]
    offset = row_index * block_size + col_index
    hashed = seed_row[:, None, :, None] * 40503 + offset[None]
    hashed = hashed ^ logical_right(hashed, 15)
    hashed = hashed * 739982445
    hashed = hashed ^ logical_right(hashed, 12)
    hashed = hashed * 695872825
    hashed = hashed ^ logical_right(hashed, 15)
    keep_scale = jnp.where(hashed & 1023 >= KEEP_LEVEL, KEEP_GAIN, 0.0).astype(jnp.float32)
    return keep_scale.reshape(seed_row.shape[0], block_size, -1)


def unrolled(body, carry, first, last):
    for j in range(first, last):
        carry = body(j, carry)
    return carry


def srl(value, amount):
    return lax.shift_right_logical(value, jnp.full(value.shape, amount, jnp.int32))


def attention_kernel(
    rows_ref, count_ref, seed_ref, q_ref, g_ref, kt_ref, vt_ref,
    att_ref, qg_ref, nk_ref, nv_ref, fk_ref, fv_ref,
    s_scr, keep_scr, drop_scr,
    *, scale, near_count, slot_count, blocks, head_size,
):
    p = pl.program_id(0)
    c = pl.program_id(1)
    width = q_ref.shape[-1]
    pair = width // head_size

    @pl.when(c == 0)
    def _():
        nk_ref[...] = jnp.zeros_like(nk_ref)
        nv_ref[...] = jnp.zeros_like(nv_ref)
        fk_ref[...] = jnp.zeros_like(fk_ref)
        fv_ref[...] = jnp.zeros_like(fv_ref)

    q = q_ref[...] * jnp.asarray(scale, q_ref.dtype)
    g = g_ref[...]
    lane_head = lax.broadcasted_iota(jnp.int32, (BS, width), 1) // head_size
    row_head = lax.broadcasted_iota(jnp.int32, (width, BS), 0) // head_size
    zero = jnp.zeros((), q.dtype)
    q_parts = [jnp.where(lane_head == a, q, zero) for a in range(pair)]
    g_parts = [jnp.where(lane_head == a, g, zero) for a in range(pair)]
    q_t = q.T
    g_t = g.T
    base = c * slot_count
    seed_base = [((p * pair + a) * blocks + c) * slot_count for a in range(pair)]
    live_end = L + 1 + count_ref[c]

    def start_of(j):
        return pl.multiple_of(rows_ref[base + j] * BS, BS)

    def keys(j):
        return kt_ref[pl.ds(start_of(j), BS), :]

    def values(j):
        return vt_ref[pl.ds(start_of(j), BS), :]

    def pick(parts, heads):
        out = parts[-1]
        for a in range(pair - 1):
            out = jnp.where(heads == a, parts[a], out)
        return out

    nt = (((1,), (1,)), ((), ()))
    f32 = jnp.float32
    m = [jnp.full((BS, BS), -jnp.inf, f32) for _ in range(pair)]
    for j in range(slot_count):
        k = keys(j)
        for a in range(pair):
            s = lax.dot_general(q_parts[a], k, nt, preferred_element_type=f32)
            if j > L:
                s = jnp.where(j < live_end, s, MASKED)
            s_scr[a, j] = s
            m[a] = jnp.maximum(m[a], s)
    m = [jnp.max(x, axis=1, keepdims=True) for x in m]
    total = [jnp.zeros((BS, BS), f32) for _ in range(pair)]
    for j in range(slot_count):
        for a in range(pair):
            e = jnp.exp(s_scr[a, j] - m[a])
            s_scr[a, j] = e
            total[a] = total[a] + e
    inv = [1.0 / jnp.sum(x, axis=1, keepdims=True) for x in total]
    offs = (
        lax.broadcasted_iota(jnp.int32, (BS, BS), 0) * BS
        + lax.broadcasted_iota(jnp.int32, (BS, BS), 1)
    )
    acc = [jnp.zeros((BS, width), f32) for _ in range(pair)]
    for j in range(slot_count):
        v = values(j)
        for a in range(pair):
            att = s_scr[a, j] * inv[a]
            s_scr[a, j] = att
            word = seed_ref[seed_base[a] + j] * 40503 + offs
            word = word ^ srl(word, 15)
            word = word * 739982445
            word = word ^ srl(word, 12)
            word = word * 695872825
            word = word ^ srl(word, 15)
            keep = jnp.where((word & 1023) >= KEEP_LEVEL, KEEP_GAIN, 0.0).astype(f32)
            keep_scr[a, j] = keep
            dropped = (att * keep).astype(jnp.bfloat16)
            drop_scr[a, j] = dropped
            acc[a] = acc[a] + jnp.dot(dropped, v, preferred_element_type=f32)
    attended = pick(acc, lane_head)
    att_ref[...] = attended.astype(att_ref.dtype)
    spread = g.astype(f32) * attended
    delta = [
        jnp.sum(jnp.where(lane_head == a, spread, 0.0), axis=1, keepdims=True) for a in range(pair)
    ]
    qacc = [jnp.zeros((BS, width), f32) for _ in range(pair)]
    for j in range(slot_count):
        k = keys(j)
        v = values(j)
        kps, vps = [], []
        for a in range(pair):
            dg = lax.dot_general(g_parts[a], v, nt, preferred_element_type=f32)
            sg = (s_scr[a, j] * (dg * keep_scr[a, j] - delta[a])).astype(jnp.bfloat16)
            qacc[a] = qacc[a] + jnp.dot(sg, k, preferred_element_type=f32)
            kps.append(jnp.dot(q_t, sg, preferred_element_type=f32))
            vps.append(jnp.dot(g_t, drop_scr[a, j], preferred_element_type=f32))
        kp = pick(kps, row_head)
        vp = pick(vps, row_head)
        at = rows_ref[base + j]
        if j <= L:
            nk_ref[at] += kp
            nv_ref[at] += vp
        else:
            fk_ref[at - near_count] = kp.astype(fk_ref.dtype)
            fv_ref[at - near_count] = vp.astype(fv_ref.dtype)
    qg_ref[...] = (pick(qacc, lane_head) * scale).astype(qg_ref.dtype)


def block_attention(rows, counts, seeds, q, g, kt, vt, *, near_count, far_count, scale, head_size):
    row_count, local_width = q.shape
    width = 2 * head_size
    groups = local_width // width
    blocks = row_count // BS
    slot_count = 1 + L + E
    kernel = functools.partial(
        attention_kernel, scale=scale, near_count=near_count, slot_count=slot_count,
        blocks=blocks, head_size=head_size,
    )
    q_spec = pl.BlockSpec((BS, width), lambda p, c, *_: (c, p))
    table_spec = pl.BlockSpec((kt.shape[0], width), lambda p, c, *_: (0, p))
    near_spec = pl.BlockSpec((near_count, width, BS), lambda p, c, *_: (0, p, 0))
    far_spec = pl.BlockSpec((far_count, width, BS), lambda p, c, *_: (0, p, 0))
    grid_spec = pltpu.PrefetchScalarGridSpec(
        num_scalar_prefetch=3,
        grid=(groups, blocks),
        in_specs=[q_spec, q_spec, table_spec, table_spec],
        out_specs=[q_spec, q_spec, near_spec, near_spec, far_spec, far_spec],
        scratch_shapes=[
            pltpu.VMEM((2, slot_count, BS, BS), jnp.float32),
            pltpu.VMEM((2, slot_count, BS, BS), jnp.float32),
            pltpu.VMEM((2, slot_count, BS, BS), jnp.bfloat16),
        ],
    )
    heads = local_width // head_size
    flops = 6 * 2 * heads * blocks * slot_count * BS * BS * width
    cost = pl.CostEstimate(
        flops=flops,
        transcendentals=heads * blocks * slot_count * BS * BS,
        bytes_accessed=2 * (q.size * 4 + kt.size * 2) + 4 * (near_count + far_count) * BS * local_width * 2,
    )
    return pl.pallas_call(
        kernel,
        grid_spec=grid_spec,
        out_shape=[
            jax.ShapeDtypeStruct(q.shape, jnp.bfloat16),
            jax.ShapeDtypeStruct(q.shape, jnp.bfloat16),
            jax.ShapeDtypeStruct((near_count, local_width, BS), jnp.float32),
            jax.ShapeDtypeStruct((near_count, local_width, BS), jnp.float32),
            jax.ShapeDtypeStruct((far_count, local_width, BS), jnp.bfloat16),
            jax.ShapeDtypeStruct((far_count, local_width, BS), jnp.bfloat16),
        ],
        compiler_params=pltpu.CompilerParams(
            dimension_semantics=("arbitrary", "arbitrary"), vmem_limit_bytes=48 * 1024 * 1024
        ),
        cost_estimate=cost,
    )(rows, counts, seeds, q, g, kt, vt)


def on_device(
    query_rows,
    key_rows,
    value_rows,
    out_grad,
    expander_device,
    expander_block,
    local_offset,
    live_count,
    drop_seed,
):
    head_count = lax.axis_size("head")
    head_index = lax.axis_index("head")
    share_rows = query_rows.shape[0]
    local_width = query_rows.shape[1] // head_count
    local_heads = drop_seed.shape[0]
    head_size = local_width // local_heads
    score_scale = head_size ** (-0.5)
    slot_count = 1 + L + E
    gathered = (
        lax.all_gather(query_rows, "head", axis=0, tiled=True),
        lax.all_gather(key_rows, "head", axis=0, tiled=True),
        lax.all_gather(value_rows, "head", axis=0, tiled=True),
        lax.all_gather(out_grad, "head", axis=0, tiled=True),
    )
    first_col = head_index * local_width
    query_local, key_local, value_local, grad_local = [
        lax.dynamic_slice_in_dim(member, first_col, local_width, 1) for member in gathered
    ]
    peer_count = lax.axis_size("blk")
    capacity = min(QB_DEV, max(2, (2 * QB_DEV * E + peer_count - 1) // peer_count))
    flat_device = expander_device.reshape(-1)
    matches = (flat_device[:, None] == jnp.arange(peer_count, dtype=jnp.int32)[None, :]).astype(
        jnp.int32
    )
    before = jnp.cumsum(matches, axis=0) - matches
    slot_rank = jnp.sum(before * matches, axis=1)
    far_position = flat_device * capacity + slot_rank
    far_live = jnp.arange(E, dtype=jnp.int32)[None, :] < live_count[:, None]
    asked_block = jnp.where(far_live, expander_block, -1)
    wanted = (
        jnp.full((peer_count * capacity,), -1, jnp.int32)
        .at[far_position]
        .set(asked_block.reshape(-1))
    )
    wanted_here = lax.all_to_all(
        wanted.reshape(peer_count, capacity), "blk", split_axis=0, concat_axis=0, tiled=True
    )
    key_blocks = key_local.reshape(QB_DEV, BS, local_width)
    value_blocks = value_local.reshape(QB_DEV, BS, local_width)
    stacked = jnp.stack([key_blocks, value_blocks], axis=1)
    widened = padded(stacked, (("blk", 0),), W)
    wanted_flat = wanted_here.reshape(-1)
    chosen = jnp.clip(wanted_flat, 0, QB_DEV - 1)
    asked_mask = (wanted_flat >= 0)[:, None, None]
    zero_block = jnp.zeros((), jnp.bfloat16)
    reply_shape = (peer_count, capacity, BS, local_width)
    far_key, far_value = (
        lax.all_to_all(
            jnp.where(asked_mask, key_blocks[chosen], zero_block).reshape(reply_shape),
            "blk",
            split_axis=0,
            concat_axis=0,
            tiled=True,
        ),
        lax.all_to_all(
            jnp.where(asked_mask, value_blocks[chosen], zero_block).reshape(reply_shape),
            "blk",
            split_axis=0,
            concat_axis=0,
            tiled=True,
        ),
    )
    near_count = QB_DEV + 2 * W
    far_total_count = peer_count * capacity
    key_table = jnp.concatenate(
        [widened[:, 0], far_key.reshape(far_total_count, BS, local_width)], axis=0
    )
    value_table = jnp.concatenate(
        [widened[:, 1], far_value.reshape(far_total_count, BS, local_width)], axis=0
    )
    local_block = jnp.arange(QB_DEV, dtype=jnp.int32)[:, None]
    self_slot = local_block + W
    near_slot = local_block + W + local_offset
    far_slot = near_count + far_position.reshape(QB_DEV, E)
    table_rows = jnp.concatenate([self_slot, near_slot, far_slot], axis=1)
    slot_number = jnp.arange(slot_count, dtype=jnp.int32)[None, :]
    live_slots = (slot_number <= L) | (slot_number - 1 - L < live_count[:, None])
    slot_rows = table_rows.reshape(-1).astype(jnp.int32)
    seed_flat = drop_seed.reshape(-1).astype(jnp.int32)
    table_count = key_table.shape[0]

    att_out, qg_out, nk, nv, fk, fv = block_attention(
        slot_rows,
        live_count.astype(jnp.int32),
        seed_flat,
        query_local,
        grad_local,
        key_table.reshape(table_count * BS, local_width),
        value_table.reshape(table_count * BS, local_width),
        near_count=near_count,
        far_count=far_total_count,
        scale=score_scale,
        head_size=head_size,
    )
    outputs = (att_out, qg_out)
    column_shape = (peer_count, capacity, local_width, BS)
    back_key, back_value = (
        lax.all_to_all(fk.reshape(column_shape), "blk", split_axis=0, concat_axis=0, tiled=True),
        lax.all_to_all(fv.reshape(column_shape), "blk", split_axis=0, concat_axis=0, tiled=True),
    )
    owner_match = (
        jnp.arange(QB_DEV, dtype=jnp.int32)[:, None] == wanted_here.reshape(1, -1)
    ).astype(jnp.bfloat16)
    far_key_sum = jnp.dot(
        owner_match,
        back_key.reshape(far_total_count, BS * local_width),
        preferred_element_type=jnp.float32,
    ).reshape(QB_DEV, local_width, BS)
    far_value_sum = jnp.dot(
        owner_match,
        back_value.reshape(far_total_count, BS * local_width),
        preferred_element_type=jnp.float32,
    ).reshape(QB_DEV, local_width, BS)
    near_total = jnp.stack([nk, nv], axis=1)
    from_below = shifted(near_total[QB_DEV + W :].astype(jnp.bfloat16), "blk", 1).astype(
        jnp.float32
    )
    from_above = shifted(near_total[:W].astype(jnp.bfloat16), "blk", -1).astype(jnp.float32)
    own_total = near_total[W : W + QB_DEV]
    own_total = own_total.at[:W].add(from_below)
    own_total = own_total.at[QB_DEV - W :].add(from_above)
    block_rows = QB_DEV * BS
    key_grad = (own_total[:, 0] + far_key_sum).astype(jnp.bfloat16).transpose(0, 2, 1)
    value_grad = (own_total[:, 1] + far_value_sum).astype(jnp.bfloat16).transpose(0, 2, 1)
    results = (
        outputs[0].reshape(block_rows, local_width),
        outputs[1].reshape(block_rows, local_width),
        key_grad.reshape(block_rows, local_width),
        value_grad.reshape(block_rows, local_width),
    )
    full_results = (
        lax.all_gather(results[0], "head", axis=1, tiled=True),
        lax.all_gather(results[1], "head", axis=1, tiled=True),
        lax.all_gather(results[2], "head", axis=1, tiled=True),
        lax.all_gather(results[3], "head", axis=1, tiled=True),
    )
    first_row = head_index * share_rows
    return tuple(
        (lax.dynamic_slice_in_dim(member, first_row, share_rows, 0) for member in full_results)
    )


def solution(mesh):
    in_specs = (
        P(("blk", "head"), None),
        P(("blk", "head"), None),
        P(("blk", "head"), None),
        P(("blk", "head"), None),
        P("blk", None),
        P("blk", None),
        P("blk", None),
        P("blk"),
        P("head", "blk", None),
    )
    out_specs = (
        P(("blk", "head"), None),
        P(("blk", "head"), None),
        P(("blk", "head"), None),
        P(("blk", "head"), None),
    )
    return jax.shard_map(
        on_device, mesh=mesh, in_specs=in_specs, out_specs=out_specs, check_vma=False
    )
```

```python
import functools

import jax
import jax.numpy as jnp
from jax import lax
from jax.experimental import pallas as pl
from jax.experimental.pallas import tpu as pltpu
from jax.sharding import PartitionSpec as P

BS = 128
QB_DEV = 8
L = 11
E = 4
W = 4


KEEP_LEVEL = 102
KEEP_GAIN = 1024.0 / 922.0
MASKED = -1e30


def padded(block, sides, width):
    for axis, dim in sides:
        count = lax.axis_size(axis)
        forward = [(i, i + 1) for i in range(count - 1)]
        forward.append((count - 1, 0))
        backward = [(target, source) for source, target in forward]
        low = lax.ppermute(
            lax.slice_in_dim(block, block.shape[dim] - width, None, axis=dim), axis, forward
        )
        high = lax.ppermute(lax.slice_in_dim(block, 0, width, axis=dim), axis, backward)
        block = jnp.concatenate([low, block, high], axis=dim)
    return block


def shifted(block, axis, distance):
    devices = range(lax.axis_size(axis))
    route = [((i - distance) % len(devices), i) for i in devices]
    return lax.ppermute(block, axis, route)


def logical_right(value, amount):
    return lax.shift_right_logical(value, jnp.full(value.shape, amount, jnp.int32))


def keep_weights(seed_row, block_size):
    row_index = jnp.arange(block_size, dtype=jnp.int32)[:, None, None]
    col_index = jnp.arange(block_size, dtype=jnp.int32)[None, None, :]
    offset = row_index * block_size + col_index
    hashed = seed_row[:, None, :, None] * 40503 + offset[None]
    hashed = hashed ^ logical_right(hashed, 15)
    hashed = hashed * 739982445
    hashed = hashed ^ logical_right(hashed, 12)
    hashed = hashed * 695872825
    hashed = hashed ^ logical_right(hashed, 15)
    keep_scale = jnp.where(hashed & 1023 >= KEEP_LEVEL, KEEP_GAIN, 0.0).astype(jnp.float32)
    return keep_scale.reshape(seed_row.shape[0], block_size, -1)


def unrolled(body, carry, first, last):
    for j in range(first, last):
        carry = body(j, carry)
    return carry


def srl(value, amount):
    return lax.shift_right_logical(value, jnp.full(value.shape, amount, jnp.int32))


def attention_kernel(
    rows_ref, count_ref, seed_ref, q_ref, g_ref, kt_ref, vt_ref,
    att_ref, qg_ref, nk_ref, nv_ref, fk_ref, fv_ref,
    s_scr, keep_scr, drop_scr,
    *, scale, near_count, slot_count, blocks, head_size,
):
    p = pl.program_id(0)
    c = pl.program_id(1)
    width = q_ref.shape[-1]
    pair = width // head_size

    @pl.when(c == 0)
    def _():
        nk_ref[...] = jnp.zeros_like(nk_ref)
        nv_ref[...] = jnp.zeros_like(nv_ref)
        fk_ref[...] = jnp.zeros_like(fk_ref)
        fv_ref[...] = jnp.zeros_like(fv_ref)

    q = q_ref[...] * jnp.asarray(scale, q_ref.dtype)
    g = g_ref[...]
    lane_head = lax.broadcasted_iota(jnp.int32, (BS, width), 1) // head_size
    row_head = lax.broadcasted_iota(jnp.int32, (width, BS), 0) // head_size
    zero = jnp.zeros((), q.dtype)
    q_parts = [jnp.where(lane_head == a, q, zero) for a in range(pair)]
    g_parts = [jnp.where(lane_head == a, g, zero) for a in range(pair)]
    q_t = q.T
    g_t = g.T
    base = c * slot_count
    seed_base = [((p * pair + a) * blocks + c) * slot_count for a in range(pair)]
    live_end = L + 1 + count_ref[c]

    def start_of(j):
        return pl.multiple_of(rows_ref[base + j] * BS, BS)

    def keys(j):
        return kt_ref[pl.ds(start_of(j), BS), :]

    def values(j):
        return vt_ref[pl.ds(start_of(j), BS), :]

    def pick(parts, heads):
        out = parts[-1]
        for a in range(pair - 1):
            out = jnp.where(heads == a, parts[a], out)
        return out

    nt = (((1,), (1,)), ((), ()))
    f32 = jnp.float32
    m = [jnp.full((BS, BS), -jnp.inf, f32) for _ in range(pair)]
    for j in range(slot_count):
        k = keys(j)
        for a in range(pair):
            s = lax.dot_general(q_parts[a], k, nt, preferred_element_type=f32)
            if j > L:
                s = jnp.where(j < live_end, s, MASKED)
            s_scr[a, j] = s
            m[a] = jnp.maximum(m[a], s)
    m = [jnp.max(x, axis=1, keepdims=True) for x in m]
    total = [jnp.zeros((BS, BS), f32) for _ in range(pair)]
    for j in range(slot_count):
        for a in range(pair):
            e = jnp.exp(s_scr[a, j] - m[a])
            s_scr[a, j] = e
            total[a] = total[a] + e
    inv = [1.0 / jnp.sum(x, axis=1, keepdims=True) for x in total]
    offs = (
        lax.broadcasted_iota(jnp.int32, (BS, BS), 0) * BS
        + lax.broadcasted_iota(jnp.int32, (BS, BS), 1)
    )
    acc = [jnp.zeros((BS, width), f32) for _ in range(pair)]
    for j in range(slot_count):
        v = values(j)
        for a in range(pair):
            att = s_scr[a, j] * inv[a]
            s_scr[a, j] = att
            word = seed_ref[seed_base[a] + j] * 40503 + offs
            word = word ^ srl(word, 15)
            word = word * 739982445
            word = word ^ srl(word, 12)
            word = word * 695872825
            word = word ^ srl(word, 15)
            keep = jnp.where((word & 1023) >= KEEP_LEVEL, KEEP_GAIN, 0.0).astype(f32)
            keep_scr[a, j] = keep
            dropped = (att * keep).astype(jnp.bfloat16)
            drop_scr[a, j] = dropped
            acc[a] = acc[a] + jnp.dot(dropped, v, preferred_element_type=f32)
    attended = pick(acc, lane_head)
    att_ref[...] = attended.astype(att_ref.dtype)
    spread = g.astype(f32) * attended
    delta = [
        jnp.sum(jnp.where(lane_head == a, spread, 0.0), axis=1, keepdims=True) for a in range(pair)
    ]
    qacc = [jnp.zeros((BS, width), f32) for _ in range(pair)]
    for j in range(slot_count):
        k = keys(j)
        v = values(j)
        kps, vps = [], []
        for a in range(pair):
            dg = lax.dot_general(g_parts[a], v, nt, preferred_element_type=f32)
            sg = (s_scr[a, j] * (dg * keep_scr[a, j] - delta[a])).astype(jnp.bfloat16)
            qacc[a] = qacc[a] + jnp.dot(sg, k, preferred_element_type=f32)
            kps.append(jnp.dot(q_t, sg, preferred_element_type=f32))
            vps.append(jnp.dot(g_t, drop_scr[a, j], preferred_element_type=f32))
        kp = pick(kps, row_head)
        vp = pick(vps, row_head)
        at = rows_ref[base + j]
        if j <= L:
            nk_ref[at] += kp
            nv_ref[at] += vp
        else:
            fk_ref[at - near_count] = kp.astype(fk_ref.dtype)
            fv_ref[at - near_count] = vp.astype(fv_ref.dtype)
    qg_ref[...] = (pick(qacc, lane_head) * scale).astype(qg_ref.dtype)


def block_attention(rows, counts, seeds, q, g, kt, vt, *, near_count, far_count, scale, head_size):
    row_count, local_width = q.shape
    width = 2 * head_size
    groups = local_width // width
    blocks = row_count // BS
    slot_count = 1 + L + E
    kernel = functools.partial(
        attention_kernel, scale=scale, near_count=near_count, slot_count=slot_count,
        blocks=blocks, head_size=head_size,
    )
    q_spec = pl.BlockSpec((BS, width), lambda p, c, *_: (c, p))
    table_spec = pl.BlockSpec((kt.shape[0], width), lambda p, c, *_: (0, p))
    near_spec = pl.BlockSpec((near_count, width, BS), lambda p, c, *_: (0, p, 0))
    far_spec = pl.BlockSpec((far_count, width, BS), lambda p, c, *_: (0, p, 0))
    grid_spec = pltpu.PrefetchScalarGridSpec(
        num_scalar_prefetch=3,
        grid=(groups, blocks),
        in_specs=[q_spec, q_spec, table_spec, table_spec],
        out_specs=[q_spec, q_spec, near_spec, near_spec, far_spec, far_spec],
        scratch_shapes=[
            pltpu.VMEM((2, slot_count, BS, BS), jnp.float32),
            pltpu.VMEM((2, slot_count, BS, BS), jnp.float32),
            pltpu.VMEM((2, slot_count, BS, BS), jnp.bfloat16),
        ],
    )
    heads = local_width // head_size
    flops = 6 * 2 * heads * blocks * slot_count * BS * BS * width
    cost = pl.CostEstimate(
        flops=flops,
        transcendentals=heads * blocks * slot_count * BS * BS,
        bytes_accessed=2 * (q.size * 4 + kt.size * 2) + 4 * (near_count + far_count) * BS * local_width * 2,
    )
    return pl.pallas_call(
        kernel,
        grid_spec=grid_spec,
        out_shape=[
            jax.ShapeDtypeStruct(q.shape, jnp.bfloat16),
            jax.ShapeDtypeStruct(q.shape, jnp.bfloat16),
            jax.ShapeDtypeStruct((near_count, local_width, BS), jnp.float32),
            jax.ShapeDtypeStruct((near_count, local_width, BS), jnp.float32),
            jax.ShapeDtypeStruct((far_count, local_width, BS), jnp.bfloat16),
            jax.ShapeDtypeStruct((far_count, local_width, BS), jnp.bfloat16),
        ],
        compiler_params=pltpu.CompilerParams(
            dimension_semantics=("arbitrary", "arbitrary"), vmem_limit_bytes=48 * 1024 * 1024
        ),
        cost_estimate=cost,
    )(rows, counts, seeds, q, g, kt, vt)


def on_device(
    query_rows,
    key_rows,
    value_rows,
    out_grad,
    expander_device,
    expander_block,
    local_offset,
    live_count,
    drop_seed,
):
    head_count = lax.axis_size("head")
    head_index = lax.axis_index("head")
    share_rows = query_rows.shape[0]
    local_width = query_rows.shape[1] // head_count
    local_heads = drop_seed.shape[0]
    head_size = local_width // local_heads
    score_scale = head_size ** (-0.5)
    slot_count = 1 + L + E
    exchanged = lax.all_to_all(
        jnp.stack([query_rows, key_rows, value_rows, out_grad]),
        "head",
        split_axis=2,
        concat_axis=1,
        tiled=True,
    )
    query_local, key_local, value_local, grad_local = (
        exchanged[0], exchanged[1], exchanged[2], exchanged[3]
    )
    peer_count = lax.axis_size("blk")
    capacity = min(QB_DEV, max(2, (2 * QB_DEV * E + peer_count - 1) // peer_count))
    flat_device = expander_device.reshape(-1)
    matches = (flat_device[:, None] == jnp.arange(peer_count, dtype=jnp.int32)[None, :]).astype(
        jnp.int32
    )
    before = jnp.cumsum(matches, axis=0) - matches
    slot_rank = jnp.sum(before * matches, axis=1)
    far_position = flat_device * capacity + slot_rank
    far_live = jnp.arange(E, dtype=jnp.int32)[None, :] < live_count[:, None]
    asked_block = jnp.where(far_live, expander_block, -1)
    wanted = (
        jnp.full((peer_count * capacity,), -1, jnp.int32)
        .at[far_position]
        .set(asked_block.reshape(-1))
    )
    wanted_here = lax.all_to_all(
        wanted.reshape(peer_count, capacity), "blk", split_axis=0, concat_axis=0, tiled=True
    )
    key_blocks = key_local.reshape(QB_DEV, BS, local_width)
    value_blocks = value_local.reshape(QB_DEV, BS, local_width)
    stacked = jnp.stack([key_blocks, value_blocks], axis=1)
    widened = padded(stacked, (("blk", 0),), W)
    wanted_flat = wanted_here.reshape(-1)
    chosen = jnp.clip(wanted_flat, 0, QB_DEV - 1)
    asked_mask = (wanted_flat >= 0)[:, None, None]
    zero_block = jnp.zeros((), jnp.bfloat16)
    reply_shape = (peer_count, capacity, BS, local_width)
    far_key, far_value = (
        lax.all_to_all(
            jnp.where(asked_mask, key_blocks[chosen], zero_block).reshape(reply_shape),
            "blk",
            split_axis=0,
            concat_axis=0,
            tiled=True,
        ),
        lax.all_to_all(
            jnp.where(asked_mask, value_blocks[chosen], zero_block).reshape(reply_shape),
            "blk",
            split_axis=0,
            concat_axis=0,
            tiled=True,
        ),
    )
    near_count = QB_DEV + 2 * W
    far_total_count = peer_count * capacity
    key_table = jnp.concatenate(
        [widened[:, 0], far_key.reshape(far_total_count, BS, local_width)], axis=0
    )
    value_table = jnp.concatenate(
        [widened[:, 1], far_value.reshape(far_total_count, BS, local_width)], axis=0
    )
    local_block = jnp.arange(QB_DEV, dtype=jnp.int32)[:, None]
    self_slot = local_block + W
    near_slot = local_block + W + local_offset
    far_slot = near_count + far_position.reshape(QB_DEV, E)
    table_rows = jnp.concatenate([self_slot, near_slot, far_slot], axis=1)
    slot_number = jnp.arange(slot_count, dtype=jnp.int32)[None, :]
    live_slots = (slot_number <= L) | (slot_number - 1 - L < live_count[:, None])
    slot_rows = table_rows.reshape(-1).astype(jnp.int32)
    seed_flat = drop_seed.reshape(-1).astype(jnp.int32)
    table_count = key_table.shape[0]

    att_out, qg_out, nk, nv, fk, fv = block_attention(
        slot_rows,
        live_count.astype(jnp.int32),
        seed_flat,
        query_local,
        grad_local,
        key_table.reshape(table_count * BS, local_width),
        value_table.reshape(table_count * BS, local_width),
        near_count=near_count,
        far_count=far_total_count,
        scale=score_scale,
        head_size=head_size,
    )
    outputs = (att_out, qg_out)
    column_shape = (peer_count, capacity, local_width, BS)
    back_key, back_value = (
        lax.all_to_all(fk.reshape(column_shape), "blk", split_axis=0, concat_axis=0, tiled=True),
        lax.all_to_all(fv.reshape(column_shape), "blk", split_axis=0, concat_axis=0, tiled=True),
    )
    owner_match = (
        jnp.arange(QB_DEV, dtype=jnp.int32)[:, None] == wanted_here.reshape(1, -1)
    ).astype(jnp.bfloat16)
    far_key_sum = jnp.dot(
        owner_match,
        back_key.reshape(far_total_count, BS * local_width),
        preferred_element_type=jnp.float32,
    ).reshape(QB_DEV, local_width, BS)
    far_value_sum = jnp.dot(
        owner_match,
        back_value.reshape(far_total_count, BS * local_width),
        preferred_element_type=jnp.float32,
    ).reshape(QB_DEV, local_width, BS)
    near_total = jnp.stack([nk, nv], axis=1)
    from_below = shifted(near_total[QB_DEV + W :].astype(jnp.bfloat16), "blk", 1).astype(
        jnp.float32
    )
    from_above = shifted(near_total[:W].astype(jnp.bfloat16), "blk", -1).astype(jnp.float32)
    own_total = near_total[W : W + QB_DEV]
    own_total = own_total.at[:W].add(from_below)
    own_total = own_total.at[QB_DEV - W :].add(from_above)
    block_rows = QB_DEV * BS
    key_grad = (own_total[:, 0] + far_key_sum).astype(jnp.bfloat16).transpose(0, 2, 1)
    value_grad = (own_total[:, 1] + far_value_sum).astype(jnp.bfloat16).transpose(0, 2, 1)
    results = (
        outputs[0].reshape(block_rows, local_width),
        outputs[1].reshape(block_rows, local_width),
        key_grad.reshape(block_rows, local_width),
        value_grad.reshape(block_rows, local_width),
    )
    returned = lax.all_to_all(jnp.stack(results), "head", split_axis=1, concat_axis=2, tiled=True)
    return tuple(returned[i] for i in range(len(results)))


def solution(mesh):
    in_specs = (
        P(("blk", "head"), None),
        P(("blk", "head"), None),
        P(("blk", "head"), None),
        P(("blk", "head"), None),
        P("blk", None),
        P("blk", None),
        P("blk", None),
        P("blk"),
        P("head", "blk", None),
    )
    out_specs = (
        P(("blk", "head"), None),
        P(("blk", "head"), None),
        P(("blk", "head"), None),
        P(("blk", "head"), None),
    )
    return jax.shard_map(
        on_device, mesh=mesh, in_specs=in_specs, out_specs=out_specs, check_vma=False
    )
```

```python
import functools

import jax
import jax.numpy as jnp
from jax import lax
from jax.experimental import pallas as pl
from jax.experimental.pallas import tpu as pltpu
from jax.sharding import PartitionSpec as P

BS = 128
QB_DEV = 8
L = 11
E = 4
W = 4


KEEP_LEVEL = 102
KEEP_GAIN = 1024.0 / 922.0
MASKED = -1e30


def padded(block, sides, width):
    for axis, dim in sides:
        count = lax.axis_size(axis)
        forward = [(i, i + 1) for i in range(count - 1)]
        forward.append((count - 1, 0))
        backward = [(target, source) for source, target in forward]
        low = lax.ppermute(
            lax.slice_in_dim(block, block.shape[dim] - width, None, axis=dim), axis, forward
        )
        high = lax.ppermute(lax.slice_in_dim(block, 0, width, axis=dim), axis, backward)
        block = jnp.concatenate([low, block, high], axis=dim)
    return block


def shifted(block, axis, distance):
    devices = range(lax.axis_size(axis))
    route = [((i - distance) % len(devices), i) for i in devices]
    return lax.ppermute(block, axis, route)


def logical_right(value, amount):
    return lax.shift_right_logical(value, jnp.full(value.shape, amount, jnp.int32))


def keep_weights(seed_row, block_size):
    row_index = jnp.arange(block_size, dtype=jnp.int32)[:, None, None]
    col_index = jnp.arange(block_size, dtype=jnp.int32)[None, None, :]
    offset = row_index * block_size + col_index
    hashed = seed_row[:, None, :, None] * 40503 + offset[None]
    hashed = hashed ^ logical_right(hashed, 15)
    hashed = hashed * 739982445
    hashed = hashed ^ logical_right(hashed, 12)
    hashed = hashed * 695872825
    hashed = hashed ^ logical_right(hashed, 15)
    keep_scale = jnp.where(hashed & 1023 >= KEEP_LEVEL, KEEP_GAIN, 0.0).astype(jnp.float32)
    return keep_scale.reshape(seed_row.shape[0], block_size, -1)


def unrolled(body, carry, first, last):
    for j in range(first, last):
        carry = body(j, carry)
    return carry


def srl(value, amount):
    return lax.shift_right_logical(value, jnp.full(value.shape, amount, jnp.int32))


def attention_kernel(
    rows_ref, count_ref, seed_ref, q_ref, g_ref, kt_ref, vt_ref,
    att_ref, qg_ref, nk_ref, nv_ref, fk_ref, fv_ref,
    s_scr, keep_scr, drop_scr,
    *, scale, near_count, slot_count, blocks, head_size, group,
):
    p = group
    c = pl.program_id(0)
    width = q_ref.shape[-1]
    pair = width // head_size

    @pl.when(c == 0)
    def _():
        nk_ref[...] = jnp.zeros_like(nk_ref)
        nv_ref[...] = jnp.zeros_like(nv_ref)
        fk_ref[...] = jnp.zeros_like(fk_ref)
        fv_ref[...] = jnp.zeros_like(fv_ref)

    q = q_ref[...] * jnp.asarray(scale, q_ref.dtype)
    g = g_ref[...]
    lane_head = lax.broadcasted_iota(jnp.int32, (BS, width), 1) // head_size
    row_head = lax.broadcasted_iota(jnp.int32, (width, BS), 0) // head_size
    zero = jnp.zeros((), q.dtype)
    q_parts = [jnp.where(lane_head == a, q, zero) for a in range(pair)]
    g_parts = [jnp.where(lane_head == a, g, zero) for a in range(pair)]
    q_t = q.T
    g_t = g.T
    base = c * slot_count
    seed_base = [((p * pair + a) * blocks + c) * slot_count for a in range(pair)]
    live_end = L + 1 + count_ref[c]

    def start_of(j):
        return pl.multiple_of(rows_ref[base + j] * BS, BS)

    def keys(j):
        return kt_ref[pl.ds(start_of(j), BS), :]

    def values(j):
        return vt_ref[pl.ds(start_of(j), BS), :]

    def pick(parts, heads):
        out = parts[-1]
        for a in range(pair - 1):
            out = jnp.where(heads == a, parts[a], out)
        return out

    nt = (((1,), (1,)), ((), ()))
    f32 = jnp.float32
    m = [jnp.full((BS, BS), -jnp.inf, f32) for _ in range(pair)]
    for j in range(slot_count):
        k = keys(j)
        for a in range(pair):
            s = lax.dot_general(q_parts[a], k, nt, preferred_element_type=f32)
            if j > L:
                s = jnp.where(j < live_end, s, MASKED)
            s_scr[a, j] = s
            m[a] = jnp.maximum(m[a], s)
    m = [jnp.max(x, axis=1, keepdims=True) for x in m]
    total = [jnp.zeros((BS, BS), f32) for _ in range(pair)]
    for j in range(slot_count):
        for a in range(pair):
            e = jnp.exp(s_scr[a, j] - m[a])
            s_scr[a, j] = e
            total[a] = total[a] + e
    inv = [1.0 / jnp.sum(x, axis=1, keepdims=True) for x in total]
    offs = (
        lax.broadcasted_iota(jnp.int32, (BS, BS), 0) * BS
        + lax.broadcasted_iota(jnp.int32, (BS, BS), 1)
    )
    acc = [jnp.zeros((BS, width), f32) for _ in range(pair)]
    for j in range(slot_count):
        v = values(j)
        for a in range(pair):
            att = s_scr[a, j] * inv[a]
            s_scr[a, j] = att
            word = seed_ref[seed_base[a] + j] * 40503 + offs
            word = word ^ srl(word, 15)
            word = word * 739982445
            word = word ^ srl(word, 12)
            word = word * 695872825
            word = word ^ srl(word, 15)
            keep = jnp.where((word & 1023) >= KEEP_LEVEL, KEEP_GAIN, 0.0).astype(f32)
            keep_scr[a, j] = keep
            dropped = (att * keep).astype(jnp.bfloat16)
            drop_scr[a, j] = dropped
            acc[a] = acc[a] + jnp.dot(dropped, v, preferred_element_type=f32)
    attended = pick(acc, lane_head)
    att_ref[...] = attended.astype(att_ref.dtype)
    spread = g.astype(f32) * attended
    delta = [
        jnp.sum(jnp.where(lane_head == a, spread, 0.0), axis=1, keepdims=True) for a in range(pair)
    ]
    qacc = [jnp.zeros((BS, width), f32) for _ in range(pair)]
    for j in range(slot_count):
        k = keys(j)
        v = values(j)
        kps, vps = [], []
        for a in range(pair):
            dg = lax.dot_general(g_parts[a], v, nt, preferred_element_type=f32)
            sg = (s_scr[a, j] * (dg * keep_scr[a, j] - delta[a])).astype(jnp.bfloat16)
            qacc[a] = qacc[a] + jnp.dot(sg, k, preferred_element_type=f32)
            kps.append(jnp.dot(q_t, sg, preferred_element_type=f32))
            vps.append(jnp.dot(g_t, drop_scr[a, j], preferred_element_type=f32))
        kp = pick(kps, row_head)
        vp = pick(vps, row_head)
        at = rows_ref[base + j]
        if j <= L:
            nk_ref[at] += kp
            nv_ref[at] += vp
        else:
            fk_ref[at - near_count] = kp.astype(fk_ref.dtype)
            fv_ref[at - near_count] = vp.astype(fv_ref.dtype)
    qg_ref[...] = (pick(qacc, lane_head) * scale).astype(qg_ref.dtype)


def block_attention(rows, counts, seeds, q, g, kt, vt, *, near_count, far_count, scale, head_size, group):
    row_count = q.shape[0]
    width = 2 * head_size
    blocks = row_count // BS
    slot_count = 1 + L + E
    kernel = functools.partial(
        attention_kernel, scale=scale, near_count=near_count, slot_count=slot_count,
        blocks=blocks, head_size=head_size, group=group,
    )
    q_spec = pl.BlockSpec((BS, width), lambda c, *_: (c, group))
    out_spec = pl.BlockSpec((BS, width), lambda c, *_: (c, 0))
    table_spec = pl.BlockSpec((kt.shape[0], width), lambda c, *_: (0, 0))
    near_spec = pl.BlockSpec((near_count, width, BS), lambda c, *_: (0, 0, 0))
    far_spec = pl.BlockSpec((far_count, width, BS), lambda c, *_: (0, 0, 0))
    grid_spec = pltpu.PrefetchScalarGridSpec(
        num_scalar_prefetch=3,
        grid=(blocks,),
        in_specs=[q_spec, q_spec, table_spec, table_spec],
        out_specs=[out_spec, out_spec, near_spec, near_spec, far_spec, far_spec],
        scratch_shapes=[
            pltpu.VMEM((2, slot_count, BS, BS), jnp.float32),
            pltpu.VMEM((2, slot_count, BS, BS), jnp.float32),
            pltpu.VMEM((2, slot_count, BS, BS), jnp.bfloat16),
        ],
    )
    heads = width // head_size
    flops = 6 * 2 * heads * blocks * slot_count * BS * BS * width
    cost = pl.CostEstimate(
        flops=flops,
        transcendentals=heads * blocks * slot_count * BS * BS,
        bytes_accessed=2 * (row_count * width * 4 + kt.size * 2) + 4 * (near_count + far_count) * BS * width * 2,
    )
    return pl.pallas_call(
        kernel,
        grid_spec=grid_spec,
        out_shape=[
            jax.ShapeDtypeStruct((row_count, width), jnp.bfloat16),
            jax.ShapeDtypeStruct((row_count, width), jnp.bfloat16),
            jax.ShapeDtypeStruct((near_count, width, BS), jnp.float32),
            jax.ShapeDtypeStruct((near_count, width, BS), jnp.float32),
            jax.ShapeDtypeStruct((far_count, width, BS), jnp.bfloat16),
            jax.ShapeDtypeStruct((far_count, width, BS), jnp.bfloat16),
        ],
        compiler_params=pltpu.CompilerParams(
            dimension_semantics=("arbitrary",), vmem_limit_bytes=48 * 1024 * 1024
        ),
        cost_estimate=cost,
    )(rows, counts, seeds, q, g, kt, vt)


def on_device(
    query_rows,
    key_rows,
    value_rows,
    out_grad,
    expander_device,
    expander_block,
    local_offset,
    live_count,
    drop_seed,
):
    head_count = lax.axis_size("head")
    head_index = lax.axis_index("head")
    share_rows = query_rows.shape[0]
    local_width = query_rows.shape[1] // head_count
    local_heads = drop_seed.shape[0]
    head_size = local_width // local_heads
    score_scale = head_size ** (-0.5)
    slot_count = 1 + L + E
    exchanged = lax.all_to_all(
        jnp.stack([query_rows, key_rows, value_rows, out_grad]),
        "head",
        split_axis=2,
        concat_axis=1,
        tiled=True,
    )
    query_local, key_local, value_local, grad_local = (
        exchanged[0], exchanged[1], exchanged[2], exchanged[3]
    )
    peer_count = lax.axis_size("blk")
    capacity = min(QB_DEV, max(2, (2 * QB_DEV * E + peer_count - 1) // peer_count))
    flat_device = expander_device.reshape(-1)
    matches = (flat_device[:, None] == jnp.arange(peer_count, dtype=jnp.int32)[None, :]).astype(
        jnp.int32
    )
    before = jnp.cumsum(matches, axis=0) - matches
    slot_rank = jnp.sum(before * matches, axis=1)
    far_position = flat_device * capacity + slot_rank
    far_live = jnp.arange(E, dtype=jnp.int32)[None, :] < live_count[:, None]
    asked_block = jnp.where(far_live, expander_block, -1)
    wanted = (
        jnp.full((peer_count * capacity,), -1, jnp.int32)
        .at[far_position]
        .set(asked_block.reshape(-1))
    )
    wanted_here = lax.all_to_all(
        wanted.reshape(peer_count, capacity), "blk", split_axis=0, concat_axis=0, tiled=True
    )
    key_blocks = key_local.reshape(QB_DEV, BS, local_width)
    value_blocks = value_local.reshape(QB_DEV, BS, local_width)
    stacked = jnp.stack([key_blocks, value_blocks], axis=1)
    widened = padded(stacked, (("blk", 0),), W)
    wanted_flat = wanted_here.reshape(-1)
    chosen = jnp.clip(wanted_flat, 0, QB_DEV - 1)
    asked_mask = (wanted_flat >= 0)[:, None, None]
    zero_block = jnp.zeros((), jnp.bfloat16)
    reply_shape = (peer_count, capacity, BS, local_width)
    near_count = QB_DEV + 2 * W
    far_total_count = peer_count * capacity
    key_asked = jnp.where(asked_mask, key_blocks[chosen], zero_block)
    value_asked = jnp.where(asked_mask, value_blocks[chosen], zero_block)
    local_block = jnp.arange(QB_DEV, dtype=jnp.int32)[:, None]
    self_slot = local_block + W
    near_slot = local_block + W + local_offset
    far_slot = near_count + far_position.reshape(QB_DEV, E)
    table_rows = jnp.concatenate([self_slot, near_slot, far_slot], axis=1)
    slot_number = jnp.arange(slot_count, dtype=jnp.int32)[None, :]
    live_slots = (slot_number <= L) | (slot_number - 1 - L < live_count[:, None])
    slot_rows = table_rows.reshape(-1).astype(jnp.int32)
    seed_flat = drop_seed.reshape(-1).astype(jnp.int32)
    width = 2 * head_size
    pair_shape = (peer_count, capacity, BS, width)
    column_shape = (peer_count, capacity, width, BS)
    owner_match = (
        jnp.arange(QB_DEV, dtype=jnp.int32)[:, None] == wanted_here.reshape(1, -1)
    ).astype(jnp.bfloat16)

    def owner_sum(back):
        return jnp.dot(
            owner_match,
            back.reshape(far_total_count, width * BS),
            preferred_element_type=jnp.float32,
        ).reshape(QB_DEV, width, BS)

    pieces = []
    for group in range(local_width // width):
        cols = slice(group * width, (group + 1) * width)
        far_key, far_value = (
            lax.all_to_all(
                key_asked[:, :, cols].reshape(pair_shape), "blk", split_axis=0, concat_axis=0, tiled=True
            ),
            lax.all_to_all(
                value_asked[:, :, cols].reshape(pair_shape), "blk", split_axis=0, concat_axis=0, tiled=True
            ),
        )
        key_table = jnp.concatenate(
            [widened[:, 0, :, cols], far_key.reshape(far_total_count, BS, width)], axis=0
        )
        value_table = jnp.concatenate(
            [widened[:, 1, :, cols], far_value.reshape(far_total_count, BS, width)], axis=0
        )
        table_count = key_table.shape[0]
        att_p, qg_p, nk_p, nv_p, fk_p, fv_p = block_attention(
            slot_rows,
            live_count.astype(jnp.int32),
            seed_flat,
            query_local,
            grad_local,
            key_table.reshape(table_count * BS, width),
            value_table.reshape(table_count * BS, width),
            near_count=near_count,
            far_count=far_total_count,
            scale=score_scale,
            head_size=head_size,
            group=group,
        )
        back_key, back_value = (
            lax.all_to_all(fk_p.reshape(column_shape), "blk", split_axis=0, concat_axis=0, tiled=True),
            lax.all_to_all(fv_p.reshape(column_shape), "blk", split_axis=0, concat_axis=0, tiled=True),
        )
        pieces.append((att_p, qg_p, nk_p, nv_p, owner_sum(back_key), owner_sum(back_value)))
    att_out, qg_out, nk, nv, far_key_sum, far_value_sum = [
        jnp.concatenate([piece[i] for piece in pieces], axis=1) for i in range(6)
    ]
    outputs = (att_out, qg_out)
    near_total = jnp.stack([nk, nv], axis=1)
    from_below = shifted(near_total[QB_DEV + W :].astype(jnp.bfloat16), "blk", 1).astype(
        jnp.float32
    )
    from_above = shifted(near_total[:W].astype(jnp.bfloat16), "blk", -1).astype(jnp.float32)
    own_total = near_total[W : W + QB_DEV]
    own_total = own_total.at[:W].add(from_below)
    own_total = own_total.at[QB_DEV - W :].add(from_above)
    block_rows = QB_DEV * BS
    key_grad = (own_total[:, 0] + far_key_sum).astype(jnp.bfloat16).transpose(0, 2, 1)
    value_grad = (own_total[:, 1] + far_value_sum).astype(jnp.bfloat16).transpose(0, 2, 1)
    results = (
        outputs[0].reshape(block_rows, local_width),
        outputs[1].reshape(block_rows, local_width),
        key_grad.reshape(block_rows, local_width),
        value_grad.reshape(block_rows, local_width),
    )
    returned = lax.all_to_all(jnp.stack(results), "head", split_axis=1, concat_axis=2, tiled=True)
    return tuple(returned[i] for i in range(len(results)))


def solution(mesh):
    in_specs = (
        P(("blk", "head"), None),
        P(("blk", "head"), None),
        P(("blk", "head"), None),
        P(("blk", "head"), None),
        P("blk", None),
        P("blk", None),
        P("blk", None),
        P("blk"),
        P("head", "blk", None),
    )
    out_specs = (
        P(("blk", "head"), None),
        P(("blk", "head"), None),
        P(("blk", "head"), None),
        P(("blk", "head"), None),
    )
    return jax.shard_map(
        on_device, mesh=mesh, in_specs=in_specs, out_specs=out_specs, check_vma=False
    )
```

```python
import functools

import jax
import jax.numpy as jnp
from jax import lax
from jax.experimental import pallas as pl
from jax.experimental.pallas import tpu as pltpu
from jax.sharding import PartitionSpec as P

BS = 128
QB_DEV = 8
L = 11
E = 4
W = 4


KEEP_LEVEL = 102
KEEP_GAIN = 1024.0 / 922.0
MASKED = -1e30


def padded(block, sides, width):
    for axis, dim in sides:
        count = lax.axis_size(axis)
        forward = [(i, i + 1) for i in range(count - 1)]
        forward.append((count - 1, 0))
        backward = [(target, source) for source, target in forward]
        low = lax.ppermute(
            lax.slice_in_dim(block, block.shape[dim] - width, None, axis=dim), axis, forward
        )
        high = lax.ppermute(lax.slice_in_dim(block, 0, width, axis=dim), axis, backward)
        block = jnp.concatenate([low, block, high], axis=dim)
    return block


def shifted(block, axis, distance):
    devices = range(lax.axis_size(axis))
    route = [((i - distance) % len(devices), i) for i in devices]
    return lax.ppermute(block, axis, route)


def logical_right(value, amount):
    return lax.shift_right_logical(value, jnp.full(value.shape, amount, jnp.int32))


def keep_weights(seed_row, block_size):
    row_index = jnp.arange(block_size, dtype=jnp.int32)[:, None, None]
    col_index = jnp.arange(block_size, dtype=jnp.int32)[None, None, :]
    offset = row_index * block_size + col_index
    hashed = seed_row[:, None, :, None] * 40503 + offset[None]
    hashed = hashed ^ logical_right(hashed, 15)
    hashed = hashed * 739982445
    hashed = hashed ^ logical_right(hashed, 12)
    hashed = hashed * 695872825
    hashed = hashed ^ logical_right(hashed, 15)
    keep_scale = jnp.where(hashed & 1023 >= KEEP_LEVEL, KEEP_GAIN, 0.0).astype(jnp.float32)
    return keep_scale.reshape(seed_row.shape[0], block_size, -1)


def unrolled(body, carry, first, last):
    for j in range(first, last):
        carry = body(j, carry)
    return carry


def srl(value, amount):
    return lax.shift_right_logical(value, jnp.full(value.shape, amount, jnp.int32))


def attention_kernel(
    rows_ref, count_ref, seed_ref, q_ref, g_ref, kt_ref, vt_ref,
    att_ref, qg_ref, nk_ref, nv_ref, fk_ref, fv_ref,
    s_scr, keep_scr, drop_scr,
    *, scale, near_count, slot_count, blocks, head_size,
):
    p = pl.program_id(0)
    c = pl.program_id(1)
    width = q_ref.shape[-1]
    pair = width // head_size

    @pl.when(c == 0)
    def _():
        nk_ref[...] = jnp.zeros_like(nk_ref)
        nv_ref[...] = jnp.zeros_like(nv_ref)
        fk_ref[...] = jnp.zeros_like(fk_ref)
        fv_ref[...] = jnp.zeros_like(fv_ref)

    q = q_ref[...] * jnp.asarray(scale, q_ref.dtype)
    g = g_ref[...]
    lane_head = lax.broadcasted_iota(jnp.int32, (BS, width), 1) // head_size
    row_head = lax.broadcasted_iota(jnp.int32, (width, BS), 0) // head_size
    zero = jnp.zeros((), q.dtype)
    q_parts = [jnp.where(lane_head == a, q, zero) for a in range(pair)]
    g_parts = [jnp.where(lane_head == a, g, zero) for a in range(pair)]
    q_t = q.T
    g_t = g.T
    base = c * slot_count
    seed_base = [((p * pair + a) * blocks + c) * slot_count for a in range(pair)]
    live_end = L + 1 + count_ref[c]

    def start_of(j):
        return pl.multiple_of(rows_ref[base + j] * BS, BS)

    def keys(j):
        return kt_ref[pl.ds(start_of(j), BS), :]

    def values(j):
        return vt_ref[pl.ds(start_of(j), BS), :]

    def pick(parts, heads):
        out = parts[-1]
        for a in range(pair - 1):
            out = jnp.where(heads == a, parts[a], out)
        return out

    nt = (((1,), (1,)), ((), ()))
    f32 = jnp.float32
    m = [jnp.full((BS, BS), -jnp.inf, f32) for _ in range(pair)]
    for j in range(slot_count):
        k = keys(j)
        for a in range(pair):
            s = lax.dot_general(q_parts[a], k, nt, preferred_element_type=f32)
            if j > L:
                s = jnp.where(j < live_end, s, MASKED)
            s_scr[a, j] = s
            m[a] = jnp.maximum(m[a], s)
    m = [jnp.max(x, axis=1, keepdims=True) for x in m]
    total = [jnp.zeros((BS, BS), f32) for _ in range(pair)]
    for j in range(slot_count):
        for a in range(pair):
            e = jnp.exp(s_scr[a, j] - m[a])
            s_scr[a, j] = e
            total[a] = total[a] + e
    inv = [1.0 / jnp.sum(x, axis=1, keepdims=True) for x in total]
    offs = (
        lax.broadcasted_iota(jnp.int32, (BS, BS), 0) * BS
        + lax.broadcasted_iota(jnp.int32, (BS, BS), 1)
    )
    acc = [jnp.zeros((BS, width), f32) for _ in range(pair)]
    for j in range(slot_count):
        v = values(j)
        for a in range(pair):
            att = s_scr[a, j] * inv[a]
            s_scr[a, j] = att
            word = seed_ref[seed_base[a] + j] * 40503 + offs
            word = word ^ srl(word, 15)
            word = word * 739982445
            word = word ^ srl(word, 12)
            word = word * 695872825
            word = word ^ srl(word, 15)
            keep = jnp.where((word & 1023) >= KEEP_LEVEL, KEEP_GAIN, 0.0).astype(f32)
            keep_scr[a, j] = keep
            dropped = (att * keep).astype(jnp.bfloat16)
            drop_scr[a, j] = dropped
            acc[a] = acc[a] + jnp.dot(dropped, v, preferred_element_type=f32)
    attended = pick(acc, lane_head)
    att_ref[...] = attended.astype(att_ref.dtype)
    spread = g.astype(f32) * attended
    delta = [
        jnp.sum(jnp.where(lane_head == a, spread, 0.0), axis=1, keepdims=True) for a in range(pair)
    ]
    qacc = [jnp.zeros((BS, width), f32) for _ in range(pair)]
    for j in range(slot_count):
        k = keys(j)
        v = values(j)
        kps, vps = [], []
        for a in range(pair):
            dg = lax.dot_general(g_parts[a], v, nt, preferred_element_type=f32)
            sg = (s_scr[a, j] * (dg * keep_scr[a, j] - delta[a])).astype(jnp.bfloat16)
            qacc[a] = qacc[a] + jnp.dot(sg, k, preferred_element_type=f32)
            kps.append(jnp.dot(q_t, sg, preferred_element_type=f32))
            vps.append(jnp.dot(g_t, drop_scr[a, j], preferred_element_type=f32))
        kp = pick(kps, row_head)
        vp = pick(vps, row_head)
        at = rows_ref[base + j]
        if j <= L:
            nk_ref[at] += kp
            nv_ref[at] += vp
        else:
            fk_ref[at - near_count] = kp.astype(fk_ref.dtype)
            fv_ref[at - near_count] = vp.astype(fv_ref.dtype)
    qg_ref[...] = (pick(qacc, lane_head) * scale).astype(qg_ref.dtype)


def block_attention(rows, counts, seeds, q, g, kt, vt, *, near_count, far_count, scale, head_size):
    row_count, local_width = q.shape
    width = 2 * head_size
    groups = local_width // width
    blocks = row_count // BS
    slot_count = 1 + L + E
    kernel = functools.partial(
        attention_kernel, scale=scale, near_count=near_count, slot_count=slot_count,
        blocks=blocks, head_size=head_size,
    )
    q_spec = pl.BlockSpec((BS, width), lambda p, c, *_: (c, p))
    table_spec = pl.BlockSpec((kt.shape[0], width), lambda p, c, *_: (0, p))
    near_spec = pl.BlockSpec((near_count, width, BS), lambda p, c, *_: (0, p, 0))
    far_spec = pl.BlockSpec((far_count, width, BS), lambda p, c, *_: (0, p, 0))
    grid_spec = pltpu.PrefetchScalarGridSpec(
        num_scalar_prefetch=3,
        grid=(groups, blocks),
        in_specs=[q_spec, q_spec, table_spec, table_spec],
        out_specs=[q_spec, q_spec, near_spec, near_spec, far_spec, far_spec],
        scratch_shapes=[
            pltpu.VMEM((2, slot_count, BS, BS), jnp.float32),
            pltpu.VMEM((2, slot_count, BS, BS), jnp.float32),
            pltpu.VMEM((2, slot_count, BS, BS), jnp.bfloat16),
        ],
    )
    heads = local_width // head_size
    flops = 6 * 2 * heads * blocks * slot_count * BS * BS * width
    cost = pl.CostEstimate(
        flops=flops,
        transcendentals=heads * blocks * slot_count * BS * BS,
        bytes_accessed=2 * (q.size * 4 + kt.size * 2) + 4 * (near_count + far_count) * BS * local_width * 2,
    )
    return pl.pallas_call(
        kernel,
        grid_spec=grid_spec,
        out_shape=[
            jax.ShapeDtypeStruct(q.shape, jnp.bfloat16),
            jax.ShapeDtypeStruct(q.shape, jnp.bfloat16),
            jax.ShapeDtypeStruct((near_count, local_width, BS), jnp.float32),
            jax.ShapeDtypeStruct((near_count, local_width, BS), jnp.float32),
            jax.ShapeDtypeStruct((far_count, local_width, BS), jnp.bfloat16),
            jax.ShapeDtypeStruct((far_count, local_width, BS), jnp.bfloat16),
        ],
        compiler_params=pltpu.CompilerParams(
            dimension_semantics=("arbitrary", "arbitrary"), vmem_limit_bytes=48 * 1024 * 1024
        ),
        cost_estimate=cost,
    )(rows, counts, seeds, q, g, kt, vt)


def on_device(
    query_rows,
    key_rows,
    value_rows,
    out_grad,
    expander_device,
    expander_block,
    local_offset,
    live_count,
    drop_seed,
):
    head_count = lax.axis_size("head")
    head_index = lax.axis_index("head")
    share_rows = query_rows.shape[0]
    local_width = query_rows.shape[1] // head_count
    local_heads = drop_seed.shape[0]
    head_size = local_width // local_heads
    score_scale = head_size ** (-0.5)
    slot_count = 1 + L + E
    exchanged = lax.all_to_all(
        jnp.stack([query_rows, key_rows, value_rows, out_grad]),
        "head",
        split_axis=2,
        concat_axis=1,
        tiled=True,
    )
    query_local, key_local, value_local, grad_local = (
        exchanged[0], exchanged[1], exchanged[2], exchanged[3]
    )
    peer_count = lax.axis_size("blk")
    capacity = min(QB_DEV, max(2, (2 * QB_DEV * E + peer_count - 1) // peer_count))
    flat_device = expander_device.reshape(-1)
    matches = (flat_device[:, None] == jnp.arange(peer_count, dtype=jnp.int32)[None, :]).astype(
        jnp.int32
    )
    before = jnp.cumsum(matches, axis=0) - matches
    slot_rank = jnp.sum(before * matches, axis=1)
    far_position = flat_device * capacity + slot_rank
    far_live = jnp.arange(E, dtype=jnp.int32)[None, :] < live_count[:, None]
    asked_block = jnp.where(far_live, expander_block, -1)
    wanted = (
        jnp.full((peer_count * capacity,), -1, jnp.int32)
        .at[far_position]
        .set(asked_block.reshape(-1))
    )
    wanted_here = lax.all_to_all(
        wanted.reshape(peer_count, capacity), "blk", split_axis=0, concat_axis=0, tiled=True
    )
    key_blocks = key_local.reshape(QB_DEV, BS, local_width)
    value_blocks = value_local.reshape(QB_DEV, BS, local_width)
    stacked = jnp.stack([key_blocks, value_blocks], axis=1)
    widened = padded(stacked, (("blk", 0),), W)
    wanted_flat = wanted_here.reshape(-1)
    chosen = jnp.clip(wanted_flat, 0, QB_DEV - 1)
    asked_mask = (wanted_flat >= 0)[:, None, None]
    zero_block = jnp.zeros((), jnp.bfloat16)
    reply_shape = (peer_count, capacity, BS, local_width)
    far_both = lax.all_to_all(
        jnp.stack(
            [
                jnp.where(asked_mask, key_blocks[chosen], zero_block),
                jnp.where(asked_mask, value_blocks[chosen], zero_block),
            ],
            axis=1,
        ).reshape((peer_count, capacity, 2, BS, local_width)),
        "blk",
        split_axis=0,
        concat_axis=0,
        tiled=True,
    )
    far_key, far_value = far_both[:, :, 0], far_both[:, :, 1]
    near_count = QB_DEV + 2 * W
    far_total_count = peer_count * capacity
    key_table = jnp.concatenate(
        [widened[:, 0], far_key.reshape(far_total_count, BS, local_width)], axis=0
    )
    value_table = jnp.concatenate(
        [widened[:, 1], far_value.reshape(far_total_count, BS, local_width)], axis=0
    )
    local_block = jnp.arange(QB_DEV, dtype=jnp.int32)[:, None]
    self_slot = local_block + W
    near_slot = local_block + W + local_offset
    far_slot = near_count + far_position.reshape(QB_DEV, E)
    table_rows = jnp.concatenate([self_slot, near_slot, far_slot], axis=1)
    slot_number = jnp.arange(slot_count, dtype=jnp.int32)[None, :]
    live_slots = (slot_number <= L) | (slot_number - 1 - L < live_count[:, None])
    slot_rows = table_rows.reshape(-1).astype(jnp.int32)
    seed_flat = drop_seed.reshape(-1).astype(jnp.int32)
    table_count = key_table.shape[0]

    att_out, qg_out, nk, nv, fk, fv = block_attention(
        slot_rows,
        live_count.astype(jnp.int32),
        seed_flat,
        query_local,
        grad_local,
        key_table.reshape(table_count * BS, local_width),
        value_table.reshape(table_count * BS, local_width),
        near_count=near_count,
        far_count=far_total_count,
        scale=score_scale,
        head_size=head_size,
    )
    outputs = (att_out, qg_out)
    column_shape = (peer_count, capacity, local_width, BS)
    back_both = lax.all_to_all(
        jnp.stack([fk, fv], axis=1).reshape((peer_count, capacity, 2, local_width, BS)),
        "blk",
        split_axis=0,
        concat_axis=0,
        tiled=True,
    )
    back_key, back_value = back_both[:, :, 0], back_both[:, :, 1]
    owner_match = (
        jnp.arange(QB_DEV, dtype=jnp.int32)[:, None] == wanted_here.reshape(1, -1)
    ).astype(jnp.bfloat16)
    far_key_sum = jnp.dot(
        owner_match,
        back_key.reshape(far_total_count, BS * local_width),
        preferred_element_type=jnp.float32,
    ).reshape(QB_DEV, local_width, BS)
    far_value_sum = jnp.dot(
        owner_match,
        back_value.reshape(far_total_count, BS * local_width),
        preferred_element_type=jnp.float32,
    ).reshape(QB_DEV, local_width, BS)
    near_total = jnp.stack([nk, nv], axis=1)
    from_below = shifted(near_total[QB_DEV + W :].astype(jnp.bfloat16), "blk", 1).astype(
        jnp.float32
    )
    from_above = shifted(near_total[:W].astype(jnp.bfloat16), "blk", -1).astype(jnp.float32)
    own_total = near_total[W : W + QB_DEV]
    own_total = own_total.at[:W].add(from_below)
    own_total = own_total.at[QB_DEV - W :].add(from_above)
    block_rows = QB_DEV * BS
    key_grad = (own_total[:, 0] + far_key_sum).astype(jnp.bfloat16).transpose(0, 2, 1)
    value_grad = (own_total[:, 1] + far_value_sum).astype(jnp.bfloat16).transpose(0, 2, 1)
    results = (
        outputs[0].reshape(block_rows, local_width),
        outputs[1].reshape(block_rows, local_width),
        key_grad.reshape(block_rows, local_width),
        value_grad.reshape(block_rows, local_width),
    )
    returned = lax.all_to_all(jnp.stack(results), "head", split_axis=1, concat_axis=2, tiled=True)
    return tuple(returned[i] for i in range(len(results)))


def solution(mesh):
    in_specs = (
        P(("blk", "head"), None),
        P(("blk", "head"), None),
        P(("blk", "head"), None),
        P(("blk", "head"), None),
        P("blk", None),
        P("blk", None),
        P("blk", None),
        P("blk"),
        P("head", "blk", None),
    )
    out_specs = (
        P(("blk", "head"), None),
        P(("blk", "head"), None),
        P(("blk", "head"), None),
        P(("blk", "head"), None),
    )
    return jax.shard_map(
        on_device, mesh=mesh, in_specs=in_specs, out_specs=out_specs, check_vma=False
    )
```

```python
import functools

import jax
import jax.numpy as jnp
from jax import lax
from jax.experimental import pallas as pl
from jax.experimental.pallas import tpu as pltpu
from jax.sharding import PartitionSpec as P

BS = 128
QB_DEV = 8
L = 11
E = 4
W = 4


KEEP_LEVEL = 102
KEEP_GAIN = 1024.0 / 922.0
MASKED = -1e30


def padded(block, sides, width):
    for axis, dim in sides:
        count = lax.axis_size(axis)
        forward = [(i, i + 1) for i in range(count - 1)]
        forward.append((count - 1, 0))
        backward = [(target, source) for source, target in forward]
        low = lax.ppermute(
            lax.slice_in_dim(block, block.shape[dim] - width, None, axis=dim), axis, forward
        )
        high = lax.ppermute(lax.slice_in_dim(block, 0, width, axis=dim), axis, backward)
        block = jnp.concatenate([low, block, high], axis=dim)
    return block


def shifted(block, axis, distance):
    devices = range(lax.axis_size(axis))
    route = [((i - distance) % len(devices), i) for i in devices]
    return lax.ppermute(block, axis, route)


def logical_right(value, amount):
    return lax.shift_right_logical(value, jnp.full(value.shape, amount, jnp.int32))


def keep_weights(seed_row, block_size):
    row_index = jnp.arange(block_size, dtype=jnp.int32)[:, None, None]
    col_index = jnp.arange(block_size, dtype=jnp.int32)[None, None, :]
    offset = row_index * block_size + col_index
    hashed = seed_row[:, None, :, None] * 40503 + offset[None]
    hashed = hashed ^ logical_right(hashed, 15)
    hashed = hashed * 739982445
    hashed = hashed ^ logical_right(hashed, 12)
    hashed = hashed * 695872825
    hashed = hashed ^ logical_right(hashed, 15)
    keep_scale = jnp.where(hashed & 1023 >= KEEP_LEVEL, KEEP_GAIN, 0.0).astype(jnp.float32)
    return keep_scale.reshape(seed_row.shape[0], block_size, -1)


def unrolled(body, carry, first, last):
    for j in range(first, last):
        carry = body(j, carry)
    return carry


def srl(value, amount):
    return lax.shift_right_logical(value, jnp.full(value.shape, amount, jnp.int32))


def attention_kernel(
    rows_ref, count_ref, seed_ref, q_ref, g_ref, kt_ref, vt_ref,
    att_ref, qg_ref, nk_ref, nv_ref, fk_ref, fv_ref,
    s_scr, keep_scr, drop_scr,
    *, scale, near_count, slot_count, blocks, head_size,
):
    p = pl.program_id(0)
    c = pl.program_id(1)
    width = q_ref.shape[-1]
    pair = width // head_size

    @pl.when(c == 0)
    def _():
        nk_ref[...] = jnp.zeros_like(nk_ref)
        nv_ref[...] = jnp.zeros_like(nv_ref)
        fk_ref[...] = jnp.zeros_like(fk_ref)
        fv_ref[...] = jnp.zeros_like(fv_ref)

    q = q_ref[...] * jnp.asarray(scale, q_ref.dtype)
    g = g_ref[...]
    lane_head = lax.broadcasted_iota(jnp.int32, (BS, width), 1) // head_size
    row_head = lax.broadcasted_iota(jnp.int32, (width, BS), 0) // head_size
    zero = jnp.zeros((), q.dtype)
    q_parts = [jnp.where(lane_head == a, q, zero) for a in range(pair)]
    g_parts = [jnp.where(lane_head == a, g, zero) for a in range(pair)]
    q_t = q.T
    g_t = g.T
    base = c * slot_count
    seed_base = [((p * pair + a) * blocks + c) * slot_count for a in range(pair)]
    live_end = L + 1 + count_ref[c]

    def start_of(j):
        return pl.multiple_of(rows_ref[base + j] * BS, BS)

    def keys(j):
        return kt_ref[pl.ds(start_of(j), BS), :]

    def values(j):
        return vt_ref[pl.ds(start_of(j), BS), :]

    def pick(parts, heads):
        out = parts[-1]
        for a in range(pair - 1):
            out = jnp.where(heads == a, parts[a], out)
        return out

    nt = (((1,), (1,)), ((), ()))
    f32 = jnp.float32
    m = [jnp.full((BS, BS), -jnp.inf, f32) for _ in range(pair)]
    for j in range(slot_count):
        k = keys(j)
        for a in range(pair):
            s = lax.dot_general(q_parts[a], k, nt, preferred_element_type=f32)
            if j > L:
                s = jnp.where(j < live_end, s, MASKED)
            s_scr[a, j] = s
            m[a] = jnp.maximum(m[a], s)
    m = [jnp.max(x, axis=1, keepdims=True) for x in m]
    total = [jnp.zeros((BS, BS), f32) for _ in range(pair)]
    for j in range(slot_count):
        for a in range(pair):
            e = jnp.exp(s_scr[a, j] - m[a])
            s_scr[a, j] = e
            total[a] = total[a] + e
    inv = [1.0 / jnp.sum(x, axis=1, keepdims=True) for x in total]
    offs = (
        lax.broadcasted_iota(jnp.int32, (BS, BS), 0) * BS
        + lax.broadcasted_iota(jnp.int32, (BS, BS), 1)
    )
    acc = [jnp.zeros((BS, width), f32) for _ in range(pair)]
    for j in range(slot_count):
        v = values(j)
        for a in range(pair):
            att = s_scr[a, j] * inv[a]
            s_scr[a, j] = att
            word = seed_ref[seed_base[a] + j] * 40503 + offs
            word = word ^ srl(word, 15)
            word = word * 739982445
            word = word ^ srl(word, 12)
            word = word * 695872825
            word = word ^ srl(word, 15)
            keep = jnp.where((word & 1023) >= KEEP_LEVEL, KEEP_GAIN, 0.0).astype(f32)
            keep_scr[a, j] = keep
            dropped = (att * keep).astype(jnp.bfloat16)
            drop_scr[a, j] = dropped
            acc[a] = acc[a] + jnp.dot(dropped, v, preferred_element_type=f32)
    attended = pick(acc, lane_head)
    att_ref[...] = attended.astype(att_ref.dtype)
    spread = g.astype(f32) * attended
    delta = [
        jnp.sum(jnp.where(lane_head == a, spread, 0.0), axis=1, keepdims=True) for a in range(pair)
    ]
    qacc = [jnp.zeros((BS, width), f32) for _ in range(pair)]
    for j in range(slot_count):
        k = keys(j)
        v = values(j)
        kps, vps = [], []
        for a in range(pair):
            dg = lax.dot_general(g_parts[a], v, nt, preferred_element_type=f32)
            sg = (s_scr[a, j] * (dg * keep_scr[a, j] - delta[a])).astype(jnp.bfloat16)
            qacc[a] = qacc[a] + jnp.dot(sg, k, preferred_element_type=f32)
            kps.append(jnp.dot(q_t, sg, preferred_element_type=f32))
            vps.append(jnp.dot(g_t, drop_scr[a, j], preferred_element_type=f32))
        kp = pick(kps, row_head)
        vp = pick(vps, row_head)
        at = rows_ref[base + j]
        if j <= L:
            nk_ref[at] += kp
            nv_ref[at] += vp
        else:
            fk_ref[at - near_count] = kp.astype(fk_ref.dtype)
            fv_ref[at - near_count] = vp.astype(fv_ref.dtype)
    qg_ref[...] = (pick(qacc, lane_head) * scale).astype(qg_ref.dtype)


def block_attention(rows, counts, seeds, q, g, kt, vt, *, near_count, far_count, scale, head_size):
    row_count, local_width = q.shape
    width = 2 * head_size
    groups = local_width // width
    blocks = row_count // BS
    slot_count = 1 + L + E
    kernel = functools.partial(
        attention_kernel, scale=scale, near_count=near_count, slot_count=slot_count,
        blocks=blocks, head_size=head_size,
    )
    q_spec = pl.BlockSpec((BS, width), lambda p, c, *_: (c, p))
    table_spec = pl.BlockSpec((kt.shape[0], width), lambda p, c, *_: (0, p))
    near_spec = pl.BlockSpec((near_count, width, BS), lambda p, c, *_: (0, p, 0))
    far_spec = pl.BlockSpec((far_count, width, BS), lambda p, c, *_: (0, p, 0))
    grid_spec = pltpu.PrefetchScalarGridSpec(
        num_scalar_prefetch=3,
        grid=(groups, blocks),
        in_specs=[q_spec, q_spec, table_spec, table_spec],
        out_specs=[q_spec, q_spec, near_spec, near_spec, far_spec, far_spec],
        scratch_shapes=[
            pltpu.VMEM((2, slot_count, BS, BS), jnp.float32),
            pltpu.VMEM((2, slot_count, BS, BS), jnp.float32),
            pltpu.VMEM((2, slot_count, BS, BS), jnp.bfloat16),
        ],
    )
    heads = local_width // head_size
    flops = 6 * 2 * heads * blocks * slot_count * BS * BS * width
    cost = pl.CostEstimate(
        flops=flops,
        transcendentals=heads * blocks * slot_count * BS * BS,
        bytes_accessed=2 * (q.size * 4 + kt.size * 2) + 4 * (near_count + far_count) * BS * local_width * 2,
    )
    return pl.pallas_call(
        kernel,
        grid_spec=grid_spec,
        out_shape=[
            jax.ShapeDtypeStruct(q.shape, jnp.bfloat16),
            jax.ShapeDtypeStruct(q.shape, jnp.bfloat16),
            jax.ShapeDtypeStruct((near_count, local_width, BS), jnp.float32),
            jax.ShapeDtypeStruct((near_count, local_width, BS), jnp.float32),
            jax.ShapeDtypeStruct((far_count, local_width, BS), jnp.bfloat16),
            jax.ShapeDtypeStruct((far_count, local_width, BS), jnp.bfloat16),
        ],
        compiler_params=pltpu.CompilerParams(
            dimension_semantics=("arbitrary", "arbitrary"), vmem_limit_bytes=48 * 1024 * 1024
        ),
        cost_estimate=cost,
    )(rows, counts, seeds, q, g, kt, vt)


def on_device(
    query_rows,
    key_rows,
    value_rows,
    out_grad,
    expander_device,
    expander_block,
    local_offset,
    live_count,
    drop_seed,
):
    head_count = lax.axis_size("head")
    head_index = lax.axis_index("head")
    share_rows = query_rows.shape[0]
    local_width = query_rows.shape[1] // head_count
    local_heads = drop_seed.shape[0]
    head_size = local_width // local_heads
    score_scale = head_size ** (-0.5)
    slot_count = 1 + L + E
    def to_columns(arrays):
        return lax.all_to_all(jnp.stack(arrays), "head", split_axis=2, concat_axis=1, tiled=True)

    key_local, value_local = to_columns([key_rows, value_rows])
    query_local, grad_local = to_columns([query_rows, out_grad])
    peer_count = lax.axis_size("blk")
    capacity = min(QB_DEV, max(2, (2 * QB_DEV * E + peer_count - 1) // peer_count))
    flat_device = expander_device.reshape(-1)
    matches = (flat_device[:, None] == jnp.arange(peer_count, dtype=jnp.int32)[None, :]).astype(
        jnp.int32
    )
    before = jnp.cumsum(matches, axis=0) - matches
    slot_rank = jnp.sum(before * matches, axis=1)
    far_position = flat_device * capacity + slot_rank
    far_live = jnp.arange(E, dtype=jnp.int32)[None, :] < live_count[:, None]
    asked_block = jnp.where(far_live, expander_block, -1)
    listing = lax.all_gather(
        jnp.stack([flat_device, asked_block.reshape(-1)]), "blk", axis=0, tiled=False
    )
    hit = (listing[:, 0] == lax.axis_index("blk")).astype(jnp.int32)
    hit_rank = jnp.cumsum(hit, axis=1) - hit
    wanted_here = jnp.stack(
        [
            jnp.sum(jnp.where((hit > 0) & (hit_rank == r), listing[:, 1] + 1, 0), axis=1) - 1
            for r in range(capacity)
        ],
        axis=1,
    )
    key_blocks = key_local.reshape(QB_DEV, BS, local_width)
    value_blocks = value_local.reshape(QB_DEV, BS, local_width)
    stacked = jnp.stack([key_blocks, value_blocks], axis=1)
    widened = padded(stacked, (("blk", 0),), W)
    wanted_flat = wanted_here.reshape(-1)
    chosen = jnp.clip(wanted_flat, 0, QB_DEV - 1)
    asked_mask = (wanted_flat >= 0)[:, None, None]
    zero_block = jnp.zeros((), jnp.bfloat16)
    reply_shape = (peer_count, capacity, BS, local_width)
    far_key, far_value = (
        lax.all_to_all(
            jnp.where(asked_mask, key_blocks[chosen], zero_block).reshape(reply_shape),
            "blk",
            split_axis=0,
            concat_axis=0,
            tiled=True,
        ),
        lax.all_to_all(
            jnp.where(asked_mask, value_blocks[chosen], zero_block).reshape(reply_shape),
            "blk",
            split_axis=0,
            concat_axis=0,
            tiled=True,
        ),
    )
    near_count = QB_DEV + 2 * W
    far_total_count = peer_count * capacity
    key_table = jnp.concatenate(
        [widened[:, 0], far_key.reshape(far_total_count, BS, local_width)], axis=0
    )
    value_table = jnp.concatenate(
        [widened[:, 1], far_value.reshape(far_total_count, BS, local_width)], axis=0
    )
    local_block = jnp.arange(QB_DEV, dtype=jnp.int32)[:, None]
    self_slot = local_block + W
    near_slot = local_block + W + local_offset
    far_slot = near_count + far_position.reshape(QB_DEV, E)
    table_rows = jnp.concatenate([self_slot, near_slot, far_slot], axis=1)
    slot_number = jnp.arange(slot_count, dtype=jnp.int32)[None, :]
    live_slots = (slot_number <= L) | (slot_number - 1 - L < live_count[:, None])
    slot_rows = table_rows.reshape(-1).astype(jnp.int32)
    seed_flat = drop_seed.reshape(-1).astype(jnp.int32)
    table_count = key_table.shape[0]

    att_out, qg_out, nk, nv, fk, fv = block_attention(
        slot_rows,
        live_count.astype(jnp.int32),
        seed_flat,
        query_local,
        grad_local,
        key_table.reshape(table_count * BS, local_width),
        value_table.reshape(table_count * BS, local_width),
        near_count=near_count,
        far_count=far_total_count,
        scale=score_scale,
        head_size=head_size,
    )
    outputs = (att_out, qg_out)
    column_shape = (peer_count, capacity, local_width, BS)
    back_key, back_value = (
        lax.all_to_all(fk.reshape(column_shape), "blk", split_axis=0, concat_axis=0, tiled=True),
        lax.all_to_all(fv.reshape(column_shape), "blk", split_axis=0, concat_axis=0, tiled=True),
    )
    owner_match = (
        jnp.arange(QB_DEV, dtype=jnp.int32)[:, None] == wanted_here.reshape(1, -1)
    ).astype(jnp.bfloat16)
    far_key_sum = jnp.dot(
        owner_match,
        back_key.reshape(far_total_count, BS * local_width),
        preferred_element_type=jnp.float32,
    ).reshape(QB_DEV, local_width, BS)
    far_value_sum = jnp.dot(
        owner_match,
        back_value.reshape(far_total_count, BS * local_width),
        preferred_element_type=jnp.float32,
    ).reshape(QB_DEV, local_width, BS)
    near_total = jnp.stack([nk, nv], axis=1)
    from_below = shifted(near_total[QB_DEV + W :].astype(jnp.bfloat16), "blk", 1).astype(
        jnp.float32
    )
    from_above = shifted(near_total[:W].astype(jnp.bfloat16), "blk", -1).astype(jnp.float32)
    own_total = near_total[W : W + QB_DEV]
    own_total = own_total.at[:W].add(from_below)
    own_total = own_total.at[QB_DEV - W :].add(from_above)
    block_rows = QB_DEV * BS
    key_grad = (own_total[:, 0] + far_key_sum).astype(jnp.bfloat16).transpose(0, 2, 1)
    value_grad = (own_total[:, 1] + far_value_sum).astype(jnp.bfloat16).transpose(0, 2, 1)
    def to_rows(arrays):
        return lax.all_to_all(jnp.stack(arrays), "head", split_axis=1, concat_axis=2, tiled=True)

    attended, query_grad = to_rows([
        outputs[0].reshape(block_rows, local_width),
        outputs[1].reshape(block_rows, local_width),
    ])
    key_grad, value_grad = to_rows([
        key_grad.reshape(block_rows, local_width),
        value_grad.reshape(block_rows, local_width),
    ])
    return attended, query_grad, key_grad, value_grad


def solution(mesh):
    in_specs = (
        P(("blk", "head"), None),
        P(("blk", "head"), None),
        P(("blk", "head"), None),
        P(("blk", "head"), None),
        P("blk", None),
        P("blk", None),
        P("blk", None),
        P("blk"),
        P("head", "blk", None),
    )
    out_specs = (
        P(("blk", "head"), None),
        P(("blk", "head"), None),
        P(("blk", "head"), None),
        P(("blk", "head"), None),
    )
    return jax.shard_map(
        on_device, mesh=mesh, in_specs=in_specs, out_specs=out_specs, check_vma=False
    )
```

```python
import functools

import jax
import jax.numpy as jnp
from jax import lax
from jax.experimental import pallas as pl
from jax.experimental.pallas import tpu as pltpu
from jax.sharding import PartitionSpec as P

BS = 128
QB_DEV = 8
L = 11
E = 4
W = 4


KEEP_LEVEL = 102
KEEP_GAIN = 1024.0 / 922.0
MASKED = -1e30


def padded(block, sides, width):
    for axis, dim in sides:
        count = lax.axis_size(axis)
        forward = [(i, i + 1) for i in range(count - 1)]
        forward.append((count - 1, 0))
        backward = [(target, source) for source, target in forward]
        low = lax.ppermute(
            lax.slice_in_dim(block, block.shape[dim] - width, None, axis=dim), axis, forward
        )
        high = lax.ppermute(lax.slice_in_dim(block, 0, width, axis=dim), axis, backward)
        block = jnp.concatenate([low, block, high], axis=dim)
    return block


def shifted(block, axis, distance):
    devices = range(lax.axis_size(axis))
    route = [((i - distance) % len(devices), i) for i in devices]
    return lax.ppermute(block, axis, route)


def logical_right(value, amount):
    return lax.shift_right_logical(value, jnp.full(value.shape, amount, jnp.int32))


def keep_weights(seed_row, block_size):
    row_index = jnp.arange(block_size, dtype=jnp.int32)[:, None, None]
    col_index = jnp.arange(block_size, dtype=jnp.int32)[None, None, :]
    offset = row_index * block_size + col_index
    hashed = seed_row[:, None, :, None] * 40503 + offset[None]
    hashed = hashed ^ logical_right(hashed, 15)
    hashed = hashed * 739982445
    hashed = hashed ^ logical_right(hashed, 12)
    hashed = hashed * 695872825
    hashed = hashed ^ logical_right(hashed, 15)
    keep_scale = jnp.where(hashed & 1023 >= KEEP_LEVEL, KEEP_GAIN, 0.0).astype(jnp.float32)
    return keep_scale.reshape(seed_row.shape[0], block_size, -1)


def unrolled(body, carry, first, last):
    for j in range(first, last):
        carry = body(j, carry)
    return carry


def srl(value, amount):
    return lax.shift_right_logical(value, jnp.full(value.shape, amount, jnp.int32))


def attention_kernel(
    rows_ref, count_ref, seed_ref, q_ref, g_ref, kt_ref, vt_ref,
    att_ref, qg_ref, nk_ref, nv_ref, fk_ref, fv_ref,
    s_scr, keep_scr, drop_scr,
    *, scale, near_count, slot_count, blocks, head_size,
):
    p = pl.program_id(0)
    c = pl.program_id(1)
    width = q_ref.shape[-1]
    pair = width // head_size

    @pl.when(c == 0)
    def _():
        nk_ref[...] = jnp.zeros_like(nk_ref)
        nv_ref[...] = jnp.zeros_like(nv_ref)
        fk_ref[...] = jnp.zeros_like(fk_ref)
        fv_ref[...] = jnp.zeros_like(fv_ref)

    q = q_ref[...] * jnp.asarray(scale, q_ref.dtype)
    g = g_ref[...]
    lane_head = lax.broadcasted_iota(jnp.int32, (BS, width), 1) // head_size
    row_head = lax.broadcasted_iota(jnp.int32, (width, BS), 0) // head_size
    zero = jnp.zeros((), q.dtype)
    q_parts = [jnp.where(lane_head == a, q, zero) for a in range(pair)]
    g_parts = [jnp.where(lane_head == a, g, zero) for a in range(pair)]
    q_t = q.T
    g_t = g.T
    base = c * slot_count
    seed_base = [((p * pair + a) * blocks + c) * slot_count for a in range(pair)]
    live_end = L + 1 + count_ref[c]

    def start_of(j):
        return pl.multiple_of(rows_ref[base + j] * BS, BS)

    def keys(j):
        return kt_ref[pl.ds(start_of(j), BS), :]

    def values(j):
        return vt_ref[pl.ds(start_of(j), BS), :]

    def pick(parts, heads):
        out = parts[-1]
        for a in range(pair - 1):
            out = jnp.where(heads == a, parts[a], out)
        return out

    nt = (((1,), (1,)), ((), ()))
    f32 = jnp.float32
    m = [jnp.full((BS, BS), -jnp.inf, f32) for _ in range(pair)]
    q_stack = jnp.concatenate(q_parts, axis=0)
    g_stack = jnp.concatenate(g_parts, axis=0)
    for j in range(slot_count):
        k = keys(j)
        s_both = lax.dot_general(q_stack, k, nt, preferred_element_type=f32)
        for a in range(pair):
            s = s_both[a * BS : (a + 1) * BS]
            if j > L:
                s = jnp.where(j < live_end, s, MASKED)
            s_scr[a, j] = s
            m[a] = jnp.maximum(m[a], s)
    m = [jnp.max(x, axis=1, keepdims=True) for x in m]
    total = [jnp.zeros((BS, BS), f32) for _ in range(pair)]
    for j in range(slot_count):
        for a in range(pair):
            e = jnp.exp(s_scr[a, j] - m[a])
            s_scr[a, j] = e
            total[a] = total[a] + e
    inv = [1.0 / jnp.sum(x, axis=1, keepdims=True) for x in total]
    offs = (
        lax.broadcasted_iota(jnp.int32, (BS, BS), 0) * BS
        + lax.broadcasted_iota(jnp.int32, (BS, BS), 1)
    )
    acc_both = jnp.zeros((pair * BS, width), f32)
    for j in range(slot_count):
        v = values(j)
        drops = []
        for a in range(pair):
            att = s_scr[a, j] * inv[a]
            s_scr[a, j] = att
            word = seed_ref[seed_base[a] + j] * 40503 + offs
            word = word ^ srl(word, 15)
            word = word * 739982445
            word = word ^ srl(word, 12)
            word = word * 695872825
            word = word ^ srl(word, 15)
            keep = jnp.where((word & 1023) >= KEEP_LEVEL, KEEP_GAIN, 0.0).astype(f32)
            keep_scr[a, j] = keep
            dropped = (att * keep).astype(jnp.bfloat16)
            drop_scr[a, j] = dropped
            drops.append(dropped)
        acc_both = acc_both + jnp.dot(
            jnp.concatenate(drops, axis=0), v, preferred_element_type=f32
        )
    acc = [acc_both[a * BS : (a + 1) * BS] for a in range(pair)]
    attended = pick(acc, lane_head)
    att_ref[...] = attended.astype(att_ref.dtype)
    spread = g.astype(f32) * attended
    delta = [
        jnp.sum(jnp.where(lane_head == a, spread, 0.0), axis=1, keepdims=True) for a in range(pair)
    ]
    qacc_both = jnp.zeros((pair * BS, width), f32)
    for j in range(slot_count):
        k = keys(j)
        v = values(j)
        dg_both = lax.dot_general(g_stack, v, nt, preferred_element_type=f32)
        sgs = []
        for a in range(pair):
            dg = dg_both[a * BS : (a + 1) * BS]
            sgs.append((s_scr[a, j] * (dg * keep_scr[a, j] - delta[a])).astype(jnp.bfloat16))
        qacc_both = qacc_both + jnp.dot(
            jnp.concatenate(sgs, axis=0), k, preferred_element_type=f32
        )
        kp_both = jnp.dot(q_t, jnp.concatenate(sgs, axis=1), preferred_element_type=f32)
        vp_both = jnp.dot(
            g_t, jnp.concatenate([drop_scr[a, j] for a in range(pair)], axis=1),
            preferred_element_type=f32,
        )
        kp = pick([kp_both[:, a * BS : (a + 1) * BS] for a in range(pair)], row_head)
        vp = pick([vp_both[:, a * BS : (a + 1) * BS] for a in range(pair)], row_head)
        at = rows_ref[base + j]
        if j <= L:
            nk_ref[at] += kp
            nv_ref[at] += vp
        else:
            fk_ref[at - near_count] = kp.astype(fk_ref.dtype)
            fv_ref[at - near_count] = vp.astype(fv_ref.dtype)
    qacc = [qacc_both[a * BS : (a + 1) * BS] for a in range(pair)]
    qg_ref[...] = (pick(qacc, lane_head) * scale).astype(qg_ref.dtype)


def block_attention(rows, counts, seeds, q, g, kt, vt, *, near_count, far_count, scale, head_size):
    row_count, local_width = q.shape
    width = 2 * head_size
    groups = local_width // width
    blocks = row_count // BS
    slot_count = 1 + L + E
    kernel = functools.partial(
        attention_kernel, scale=scale, near_count=near_count, slot_count=slot_count,
        blocks=blocks, head_size=head_size,
    )
    q_spec = pl.BlockSpec((BS, width), lambda p, c, *_: (c, p))
    table_spec = pl.BlockSpec((kt.shape[0], width), lambda p, c, *_: (0, p))
    near_spec = pl.BlockSpec((near_count, width, BS), lambda p, c, *_: (0, p, 0))
    far_spec = pl.BlockSpec((far_count, width, BS), lambda p, c, *_: (0, p, 0))
    grid_spec = pltpu.PrefetchScalarGridSpec(
        num_scalar_prefetch=3,
        grid=(groups, blocks),
        in_specs=[q_spec, q_spec, table_spec, table_spec],
        out_specs=[q_spec, q_spec, near_spec, near_spec, far_spec, far_spec],
        scratch_shapes=[
            pltpu.VMEM((2, slot_count, BS, BS), jnp.float32),
            pltpu.VMEM((2, slot_count, BS, BS), jnp.float32),
            pltpu.VMEM((2, slot_count, BS, BS), jnp.bfloat16),
        ],
    )
    heads = local_width // head_size
    flops = 6 * 2 * heads * blocks * slot_count * BS * BS * width
    cost = pl.CostEstimate(
        flops=flops,
        transcendentals=heads * blocks * slot_count * BS * BS,
        bytes_accessed=2 * (q.size * 4 + kt.size * 2) + 4 * (near_count + far_count) * BS * local_width * 2,
    )
    return pl.pallas_call(
        kernel,
        grid_spec=grid_spec,
        out_shape=[
            jax.ShapeDtypeStruct(q.shape, jnp.bfloat16),
            jax.ShapeDtypeStruct(q.shape, jnp.bfloat16),
            jax.ShapeDtypeStruct((near_count, local_width, BS), jnp.float32),
            jax.ShapeDtypeStruct((near_count, local_width, BS), jnp.float32),
            jax.ShapeDtypeStruct((far_count, local_width, BS), jnp.bfloat16),
            jax.ShapeDtypeStruct((far_count, local_width, BS), jnp.bfloat16),
        ],
        compiler_params=pltpu.CompilerParams(
            dimension_semantics=("arbitrary", "arbitrary"), vmem_limit_bytes=48 * 1024 * 1024
        ),
        cost_estimate=cost,
    )(rows, counts, seeds, q, g, kt, vt)


def on_device(
    query_rows,
    key_rows,
    value_rows,
    out_grad,
    expander_device,
    expander_block,
    local_offset,
    live_count,
    drop_seed,
):
    head_count = lax.axis_size("head")
    head_index = lax.axis_index("head")
    share_rows = query_rows.shape[0]
    local_width = query_rows.shape[1] // head_count
    local_heads = drop_seed.shape[0]
    head_size = local_width // local_heads
    score_scale = head_size ** (-0.5)
    slot_count = 1 + L + E
    def to_columns(arrays):
        return lax.all_to_all(jnp.stack(arrays), "head", split_axis=2, concat_axis=1, tiled=True)

    key_local, value_local = to_columns([key_rows, value_rows])
    query_local, grad_local = to_columns([query_rows, out_grad])
    peer_count = lax.axis_size("blk")
    capacity = min(QB_DEV, max(2, (2 * QB_DEV * E + peer_count - 1) // peer_count))
    flat_device = expander_device.reshape(-1)
    matches = (flat_device[:, None] == jnp.arange(peer_count, dtype=jnp.int32)[None, :]).astype(
        jnp.int32
    )
    before = jnp.cumsum(matches, axis=0) - matches
    slot_rank = jnp.sum(before * matches, axis=1)
    far_position = flat_device * capacity + slot_rank
    far_live = jnp.arange(E, dtype=jnp.int32)[None, :] < live_count[:, None]
    asked_block = jnp.where(far_live, expander_block, -1)
    listing = lax.all_gather(
        jnp.stack([flat_device, asked_block.reshape(-1)]), "blk", axis=0, tiled=False
    )
    hit = (listing[:, 0] == lax.axis_index("blk")).astype(jnp.int32)
    hit_rank = jnp.cumsum(hit, axis=1) - hit
    wanted_here = jnp.stack(
        [
            jnp.sum(jnp.where((hit > 0) & (hit_rank == r), listing[:, 1] + 1, 0), axis=1) - 1
            for r in range(capacity)
        ],
        axis=1,
    )
    key_blocks = key_local.reshape(QB_DEV, BS, local_width)
    value_blocks = value_local.reshape(QB_DEV, BS, local_width)
    stacked = jnp.stack([key_blocks, value_blocks], axis=1)
    widened = padded(stacked, (("blk", 0),), W)
    wanted_flat = wanted_here.reshape(-1)
    chosen = jnp.clip(wanted_flat, 0, QB_DEV - 1)
    asked_mask = (wanted_flat >= 0)[:, None, None]
    zero_block = jnp.zeros((), jnp.bfloat16)
    reply_shape = (peer_count, capacity, BS, local_width)
    far_key, far_value = (
        lax.all_to_all(
            jnp.where(asked_mask, key_blocks[chosen], zero_block).reshape(reply_shape),
            "blk",
            split_axis=0,
            concat_axis=0,
            tiled=True,
        ),
        lax.all_to_all(
            jnp.where(asked_mask, value_blocks[chosen], zero_block).reshape(reply_shape),
            "blk",
            split_axis=0,
            concat_axis=0,
            tiled=True,
        ),
    )
    near_count = QB_DEV + 2 * W
    far_total_count = peer_count * capacity
    key_table = jnp.concatenate(
        [widened[:, 0], far_key.reshape(far_total_count, BS, local_width)], axis=0
    )
    value_table = jnp.concatenate(
        [widened[:, 1], far_value.reshape(far_total_count, BS, local_width)], axis=0
    )
    local_block = jnp.arange(QB_DEV, dtype=jnp.int32)[:, None]
    self_slot = local_block + W
    near_slot = local_block + W + local_offset
    far_slot = near_count + far_position.reshape(QB_DEV, E)
    table_rows = jnp.concatenate([self_slot, near_slot, far_slot], axis=1)
    slot_number = jnp.arange(slot_count, dtype=jnp.int32)[None, :]
    live_slots = (slot_number <= L) | (slot_number - 1 - L < live_count[:, None])
    slot_rows = table_rows.reshape(-1).astype(jnp.int32)
    seed_flat = drop_seed.reshape(-1).astype(jnp.int32)
    table_count = key_table.shape[0]

    att_out, qg_out, nk, nv, fk, fv = block_attention(
        slot_rows,
        live_count.astype(jnp.int32),
        seed_flat,
        query_local,
        grad_local,
        key_table.reshape(table_count * BS, local_width),
        value_table.reshape(table_count * BS, local_width),
        near_count=near_count,
        far_count=far_total_count,
        scale=score_scale,
        head_size=head_size,
    )
    outputs = (att_out, qg_out)
    column_shape = (peer_count, capacity, local_width, BS)
    back_key, back_value = (
        lax.all_to_all(fk.reshape(column_shape), "blk", split_axis=0, concat_axis=0, tiled=True),
        lax.all_to_all(fv.reshape(column_shape), "blk", split_axis=0, concat_axis=0, tiled=True),
    )
    owner_match = (
        jnp.arange(QB_DEV, dtype=jnp.int32)[:, None] == wanted_here.reshape(1, -1)
    ).astype(jnp.bfloat16)
    far_key_sum = jnp.dot(
        owner_match,
        back_key.reshape(far_total_count, BS * local_width),
        preferred_element_type=jnp.float32,
    ).reshape(QB_DEV, local_width, BS)
    far_value_sum = jnp.dot(
        owner_match,
        back_value.reshape(far_total_count, BS * local_width),
        preferred_element_type=jnp.float32,
    ).reshape(QB_DEV, local_width, BS)
    near_total = jnp.stack([nk, nv], axis=1)
    from_below = shifted(near_total[QB_DEV + W :].astype(jnp.bfloat16), "blk", 1).astype(
        jnp.float32
    )
    from_above = shifted(near_total[:W].astype(jnp.bfloat16), "blk", -1).astype(jnp.float32)
    own_total = near_total[W : W + QB_DEV]
    own_total = own_total.at[:W].add(from_below)
    own_total = own_total.at[QB_DEV - W :].add(from_above)
    block_rows = QB_DEV * BS
    key_grad = (own_total[:, 0] + far_key_sum).astype(jnp.bfloat16).transpose(0, 2, 1)
    value_grad = (own_total[:, 1] + far_value_sum).astype(jnp.bfloat16).transpose(0, 2, 1)
    def to_rows(arrays):
        return lax.all_to_all(jnp.stack(arrays), "head", split_axis=1, concat_axis=2, tiled=True)

    attended, query_grad = to_rows([
        outputs[0].reshape(block_rows, local_width),
        outputs[1].reshape(block_rows, local_width),
    ])
    key_grad, value_grad = to_rows([
        key_grad.reshape(block_rows, local_width),
        value_grad.reshape(block_rows, local_width),
    ])
    return attended, query_grad, key_grad, value_grad


def solution(mesh):
    in_specs = (
        P(("blk", "head"), None),
        P(("blk", "head"), None),
        P(("blk", "head"), None),
        P(("blk", "head"), None),
        P("blk", None),
        P("blk", None),
        P("blk", None),
        P("blk"),
        P("head", "blk", None),
    )
    out_specs = (
        P(("blk", "head"), None),
        P(("blk", "head"), None),
        P(("blk", "head"), None),
        P(("blk", "head"), None),
    )
    return jax.shard_map(
        on_device, mesh=mesh, in_specs=in_specs, out_specs=out_specs, check_vma=False
    )
```

```python
import functools

import jax
import jax.numpy as jnp
from jax import lax
from jax.experimental import pallas as pl
from jax.experimental.pallas import tpu as pltpu
from jax.sharding import PartitionSpec as P

BS = 128
QB_DEV = 8
L = 11
E = 4
W = 4


KEEP_LEVEL = 102
KEEP_GAIN = 1024.0 / 922.0
MASKED = -1e30


def padded(block, sides, width):
    for axis, dim in sides:
        count = lax.axis_size(axis)
        forward = [(i, i + 1) for i in range(count - 1)]
        forward.append((count - 1, 0))
        backward = [(target, source) for source, target in forward]
        low = lax.ppermute(
            lax.slice_in_dim(block, block.shape[dim] - width, None, axis=dim), axis, forward
        )
        high = lax.ppermute(lax.slice_in_dim(block, 0, width, axis=dim), axis, backward)
        block = jnp.concatenate([low, block, high], axis=dim)
    return block


def shifted(block, axis, distance):
    devices = range(lax.axis_size(axis))
    route = [((i - distance) % len(devices), i) for i in devices]
    return lax.ppermute(block, axis, route)


def logical_right(value, amount):
    return lax.shift_right_logical(value, jnp.full(value.shape, amount, jnp.int32))


def keep_weights(seed_row, block_size):
    row_index = jnp.arange(block_size, dtype=jnp.int32)[:, None, None]
    col_index = jnp.arange(block_size, dtype=jnp.int32)[None, None, :]
    offset = row_index * block_size + col_index
    hashed = seed_row[:, None, :, None] * 40503 + offset[None]
    hashed = hashed ^ logical_right(hashed, 15)
    hashed = hashed * 739982445
    hashed = hashed ^ logical_right(hashed, 12)
    hashed = hashed * 695872825
    hashed = hashed ^ logical_right(hashed, 15)
    keep_scale = jnp.where(hashed & 1023 >= KEEP_LEVEL, KEEP_GAIN, 0.0).astype(jnp.float32)
    return keep_scale.reshape(seed_row.shape[0], block_size, -1)


def unrolled(body, carry, first, last):
    for j in range(first, last):
        carry = body(j, carry)
    return carry


def srl(value, amount):
    return lax.shift_right_logical(value, jnp.full(value.shape, amount, jnp.int32))


def attention_kernel(
    rows_ref, count_ref, seed_ref, q_ref, g_ref, kt_ref, vt_ref,
    att_ref, qg_ref, nk_ref, nv_ref, fk_ref, fv_ref,
    s_scr, keep_scr, drop_scr,
    *, scale, near_count, slot_count, blocks, head_size,
):
    p = pl.program_id(0)
    c = pl.program_id(1)
    width = q_ref.shape[-1]
    pair = width // head_size

    @pl.when(c == 0)
    def _():
        nk_ref[...] = jnp.zeros_like(nk_ref)
        nv_ref[...] = jnp.zeros_like(nv_ref)
        fk_ref[...] = jnp.zeros_like(fk_ref)
        fv_ref[...] = jnp.zeros_like(fv_ref)

    q = q_ref[...] * jnp.asarray(scale, q_ref.dtype)
    g = g_ref[...]
    lane_head = lax.broadcasted_iota(jnp.int32, (BS, width), 1) // head_size
    row_head = lax.broadcasted_iota(jnp.int32, (width, BS), 0) // head_size
    zero = jnp.zeros((), q.dtype)
    q_parts = [jnp.where(lane_head == a, q, zero) for a in range(pair)]
    g_parts = [jnp.where(lane_head == a, g, zero) for a in range(pair)]
    q_t = q.T
    g_t = g.T
    base = c * slot_count
    seed_base = [((p * pair + a) * blocks + c) * slot_count for a in range(pair)]
    live_end = L + 1 + count_ref[c]

    def start_of(j):
        return pl.multiple_of(rows_ref[base + j] * BS, BS)

    def keys(j):
        return kt_ref[pl.ds(start_of(j), BS), :]

    def values(j):
        return vt_ref[pl.ds(start_of(j), BS), :]

    def pick(parts, heads):
        out = parts[-1]
        for a in range(pair - 1):
            out = jnp.where(heads == a, parts[a], out)
        return out

    nt = (((1,), (1,)), ((), ()))
    f32 = jnp.float32
    m = [jnp.full((BS, BS), -jnp.inf, f32) for _ in range(pair)]
    q_stack = jnp.concatenate(q_parts, axis=0)
    g_stack = jnp.concatenate(g_parts, axis=0)
    for j in range(slot_count):
        k = keys(j)
        s_both = lax.dot_general(q_stack, k, nt, preferred_element_type=f32)
        for a in range(pair):
            s = s_both[a * BS : (a + 1) * BS]
            if j > L:
                s = jnp.where(j < live_end, s, MASKED)
            s_scr[a, j] = s
            m[a] = jnp.maximum(m[a], s)
    m = [jnp.max(x, axis=1, keepdims=True) for x in m]
    total = [jnp.zeros((BS, BS), f32) for _ in range(pair)]
    for j in range(slot_count):
        for a in range(pair):
            e = jnp.exp(s_scr[a, j] - m[a])
            s_scr[a, j] = e
            total[a] = total[a] + e
    inv = [1.0 / jnp.sum(x, axis=1, keepdims=True) for x in total]
    offs = (
        lax.broadcasted_iota(jnp.int32, (BS, BS), 0) * BS
        + lax.broadcasted_iota(jnp.int32, (BS, BS), 1)
    )
    acc_both = jnp.zeros((pair * BS, width), f32)
    for j in range(slot_count):
        v = values(j)
        drops = []
        for a in range(pair):
            att = s_scr[a, j] * inv[a]
            s_scr[a, j] = att
            word = seed_ref[seed_base[a] + j] * 40503 + offs
            word = word ^ srl(word, 15)
            word = word * 739982445
            word = word ^ srl(word, 12)
            word = word * 695872825
            word = word ^ srl(word, 15)
            keep = jnp.where((word & 1023) >= KEEP_LEVEL, KEEP_GAIN, 0.0).astype(f32)
            keep_scr[a, j] = keep
            dropped = (att * keep).astype(jnp.bfloat16)
            drop_scr[a, j] = dropped
            drops.append(dropped)
        acc_both = acc_both + jnp.dot(
            jnp.concatenate(drops, axis=0), v, preferred_element_type=f32
        )
    acc = [acc_both[a * BS : (a + 1) * BS] for a in range(pair)]
    attended = pick(acc, lane_head)
    att_ref[...] = attended.astype(att_ref.dtype)
    spread = g.astype(f32) * attended
    delta = [
        jnp.sum(jnp.where(lane_head == a, spread, 0.0), axis=1, keepdims=True) for a in range(pair)
    ]
    qacc_both = jnp.zeros((pair * BS, width), f32)
    for j in range(slot_count):
        k = keys(j)
        v = values(j)
        dg_both = lax.dot_general(g_stack, v, nt, preferred_element_type=f32)
        sgs = []
        for a in range(pair):
            dg = dg_both[a * BS : (a + 1) * BS]
            sgs.append((s_scr[a, j] * (dg * keep_scr[a, j] - delta[a])).astype(jnp.bfloat16))
        qacc_both = qacc_both + jnp.dot(
            jnp.concatenate(sgs, axis=0), k, preferred_element_type=f32
        )
        kp_both = jnp.dot(q_t, jnp.concatenate(sgs, axis=1), preferred_element_type=f32)
        vp_both = jnp.dot(
            g_t, jnp.concatenate([drop_scr[a, j] for a in range(pair)], axis=1),
            preferred_element_type=f32,
        )
        kp = pick([kp_both[:, a * BS : (a + 1) * BS] for a in range(pair)], row_head)
        vp = pick([vp_both[:, a * BS : (a + 1) * BS] for a in range(pair)], row_head)
        at = rows_ref[base + j]
        if j <= L:
            nk_ref[at] += kp
            nv_ref[at] += vp
        else:
            fk_ref[at - near_count] = kp.astype(fk_ref.dtype)
            fv_ref[at - near_count] = vp.astype(fv_ref.dtype)
    qacc = [qacc_both[a * BS : (a + 1) * BS] for a in range(pair)]
    qg_ref[...] = (pick(qacc, lane_head) * scale).astype(qg_ref.dtype)


def block_attention(rows, counts, seeds, q, g, kt, vt, *, near_count, far_count, scale, head_size):
    row_count, local_width = q.shape
    width = 2 * head_size
    groups = local_width // width
    blocks = row_count // BS
    slot_count = 1 + L + E
    kernel = functools.partial(
        attention_kernel, scale=scale, near_count=near_count, slot_count=slot_count,
        blocks=blocks, head_size=head_size,
    )
    q_spec = pl.BlockSpec((BS, width), lambda p, c, *_: (c, p))
    table_spec = pl.BlockSpec((kt.shape[0], width), lambda p, c, *_: (0, p))
    near_spec = pl.BlockSpec((near_count, width, BS), lambda p, c, *_: (0, p, 0))
    far_spec = pl.BlockSpec((far_count, width, BS), lambda p, c, *_: (0, p, 0))
    grid_spec = pltpu.PrefetchScalarGridSpec(
        num_scalar_prefetch=3,
        grid=(groups, blocks),
        in_specs=[q_spec, q_spec, table_spec, table_spec],
        out_specs=[q_spec, q_spec, near_spec, near_spec, far_spec, far_spec],
        scratch_shapes=[
            pltpu.VMEM((2, slot_count, BS, BS), jnp.float32),
            pltpu.VMEM((2, slot_count, BS, BS), jnp.float32),
            pltpu.VMEM((2, slot_count, BS, BS), jnp.bfloat16),
        ],
    )
    heads = local_width // head_size
    flops = 6 * 2 * heads * blocks * slot_count * BS * BS * width
    cost = pl.CostEstimate(
        flops=flops,
        transcendentals=heads * blocks * slot_count * BS * BS,
        bytes_accessed=2 * (q.size * 4 + kt.size * 2) + 4 * (near_count + far_count) * BS * local_width * 2,
    )
    return pl.pallas_call(
        kernel,
        grid_spec=grid_spec,
        out_shape=[
            jax.ShapeDtypeStruct(q.shape, jnp.bfloat16),
            jax.ShapeDtypeStruct(q.shape, jnp.bfloat16),
            jax.ShapeDtypeStruct((near_count, local_width, BS), jnp.float32),
            jax.ShapeDtypeStruct((near_count, local_width, BS), jnp.float32),
            jax.ShapeDtypeStruct((far_count, local_width, BS), jnp.bfloat16),
            jax.ShapeDtypeStruct((far_count, local_width, BS), jnp.bfloat16),
        ],
        compiler_params=pltpu.CompilerParams(
            dimension_semantics=("arbitrary", "arbitrary"), vmem_limit_bytes=48 * 1024 * 1024
        ),
        cost_estimate=cost,
    )(rows, counts, seeds, q, g, kt, vt)


def on_device(
    query_rows,
    key_rows,
    value_rows,
    out_grad,
    expander_device,
    expander_block,
    local_offset,
    live_count,
    drop_seed,
):
    head_count = lax.axis_size("head")
    head_index = lax.axis_index("head")
    share_rows = query_rows.shape[0]
    local_width = query_rows.shape[1] // head_count
    local_heads = drop_seed.shape[0]
    head_size = local_width // local_heads
    score_scale = head_size ** (-0.5)
    slot_count = 1 + L + E
    def to_columns(arrays):
        return lax.all_to_all(jnp.stack(arrays), "head", split_axis=2, concat_axis=1, tiled=True)

    key_local, value_local, query_local, grad_local = to_columns(
        [key_rows, value_rows, query_rows, out_grad]
    )
    peer_count = lax.axis_size("blk")
    capacity = min(QB_DEV, max(2, (2 * QB_DEV * E + peer_count - 1) // peer_count))
    flat_device = expander_device.reshape(-1)
    matches = (flat_device[:, None] == jnp.arange(peer_count, dtype=jnp.int32)[None, :]).astype(
        jnp.int32
    )
    before = jnp.cumsum(matches, axis=0) - matches
    slot_rank = jnp.sum(before * matches, axis=1)
    far_position = flat_device * capacity + slot_rank
    far_live = jnp.arange(E, dtype=jnp.int32)[None, :] < live_count[:, None]
    asked_block = jnp.where(far_live, expander_block, -1)
    listing = lax.all_gather(
        jnp.stack([flat_device, asked_block.reshape(-1)]), "blk", axis=0, tiled=False
    )
    hit = (listing[:, 0] == lax.axis_index("blk")).astype(jnp.int32)
    hit_rank = jnp.cumsum(hit, axis=1) - hit
    wanted_here = jnp.stack(
        [
            jnp.sum(jnp.where((hit > 0) & (hit_rank == r), listing[:, 1] + 1, 0), axis=1) - 1
            for r in range(capacity)
        ],
        axis=1,
    )
    key_blocks = key_local.reshape(QB_DEV, BS, local_width)
    value_blocks = value_local.reshape(QB_DEV, BS, local_width)
    stacked = jnp.stack([key_blocks, value_blocks], axis=1)
    widened = padded(stacked, (("blk", 0),), W)
    wanted_flat = wanted_here.reshape(-1)
    chosen = jnp.clip(wanted_flat, 0, QB_DEV - 1)
    asked_mask = (wanted_flat >= 0)[:, None, None]
    zero_block = jnp.zeros((), jnp.bfloat16)
    reply_shape = (peer_count, capacity, BS, local_width)
    far_key, far_value = (
        lax.all_to_all(
            jnp.where(asked_mask, key_blocks[chosen], zero_block).reshape(reply_shape),
            "blk",
            split_axis=0,
            concat_axis=0,
            tiled=True,
        ),
        lax.all_to_all(
            jnp.where(asked_mask, value_blocks[chosen], zero_block).reshape(reply_shape),
            "blk",
            split_axis=0,
            concat_axis=0,
            tiled=True,
        ),
    )
    near_count = QB_DEV + 2 * W
    far_total_count = peer_count * capacity
    key_table = jnp.concatenate(
        [widened[:, 0], far_key.reshape(far_total_count, BS, local_width)], axis=0
    )
    value_table = jnp.concatenate(
        [widened[:, 1], far_value.reshape(far_total_count, BS, local_width)], axis=0
    )
    local_block = jnp.arange(QB_DEV, dtype=jnp.int32)[:, None]
    self_slot = local_block + W
    near_slot = local_block + W + local_offset
    far_slot = near_count + far_position.reshape(QB_DEV, E)
    table_rows = jnp.concatenate([self_slot, near_slot, far_slot], axis=1)
    slot_number = jnp.arange(slot_count, dtype=jnp.int32)[None, :]
    live_slots = (slot_number <= L) | (slot_number - 1 - L < live_count[:, None])
    slot_rows = table_rows.reshape(-1).astype(jnp.int32)
    seed_flat = drop_seed.reshape(-1).astype(jnp.int32)
    table_count = key_table.shape[0]

    att_out, qg_out, nk, nv, fk, fv = block_attention(
        slot_rows,
        live_count.astype(jnp.int32),
        seed_flat,
        query_local,
        grad_local,
        key_table.reshape(table_count * BS, local_width),
        value_table.reshape(table_count * BS, local_width),
        near_count=near_count,
        far_count=far_total_count,
        scale=score_scale,
        head_size=head_size,
    )
    outputs = (att_out, qg_out)
    column_shape = (peer_count, capacity, local_width, BS)
    back_key, back_value = (
        lax.all_to_all(fk.reshape(column_shape), "blk", split_axis=0, concat_axis=0, tiled=True),
        lax.all_to_all(fv.reshape(column_shape), "blk", split_axis=0, concat_axis=0, tiled=True),
    )
    owner_match = (
        jnp.arange(QB_DEV, dtype=jnp.int32)[:, None] == wanted_here.reshape(1, -1)
    ).astype(jnp.bfloat16)
    far_key_sum = jnp.dot(
        owner_match,
        back_key.reshape(far_total_count, BS * local_width),
        preferred_element_type=jnp.float32,
    ).reshape(QB_DEV, local_width, BS)
    far_value_sum = jnp.dot(
        owner_match,
        back_value.reshape(far_total_count, BS * local_width),
        preferred_element_type=jnp.float32,
    ).reshape(QB_DEV, local_width, BS)
    near_total = jnp.stack([nk, nv], axis=1)
    from_below = shifted(near_total[QB_DEV + W :].astype(jnp.bfloat16), "blk", 1).astype(
        jnp.float32
    )
    from_above = shifted(near_total[:W].astype(jnp.bfloat16), "blk", -1).astype(jnp.float32)
    own_total = near_total[W : W + QB_DEV]
    own_total = own_total.at[:W].add(from_below)
    own_total = own_total.at[QB_DEV - W :].add(from_above)
    block_rows = QB_DEV * BS
    key_grad = (own_total[:, 0] + far_key_sum).astype(jnp.bfloat16).transpose(0, 2, 1)
    value_grad = (own_total[:, 1] + far_value_sum).astype(jnp.bfloat16).transpose(0, 2, 1)
    def to_rows(arrays):
        return lax.all_to_all(jnp.stack(arrays), "head", split_axis=1, concat_axis=2, tiled=True)

    attended, query_grad = to_rows([
        outputs[0].reshape(block_rows, local_width),
        outputs[1].reshape(block_rows, local_width),
    ])
    key_grad, value_grad = to_rows([
        key_grad.reshape(block_rows, local_width),
        value_grad.reshape(block_rows, local_width),
    ])
    return attended, query_grad, key_grad, value_grad


def solution(mesh):
    in_specs = (
        P(("blk", "head"), None),
        P(("blk", "head"), None),
        P(("blk", "head"), None),
        P(("blk", "head"), None),
        P("blk", None),
        P("blk", None),
        P("blk", None),
        P("blk"),
        P("head", "blk", None),
    )
    out_specs = (
        P(("blk", "head"), None),
        P(("blk", "head"), None),
        P(("blk", "head"), None),
        P(("blk", "head"), None),
    )
    return jax.shard_map(
        on_device, mesh=mesh, in_specs=in_specs, out_specs=out_specs, check_vma=False
    )
```

```python
import functools

import jax
import jax.numpy as jnp
from jax import lax
from jax.experimental import pallas as pl
from jax.experimental.pallas import tpu as pltpu
from jax.sharding import PartitionSpec as P

BS = 128
QB_DEV = 8
L = 11
E = 4
W = 4


KEEP_LEVEL = 102
KEEP_GAIN = 1024.0 / 922.0
MASKED = -1e30


def padded(block, sides, width):
    for axis, dim in sides:
        count = lax.axis_size(axis)
        forward = [(i, i + 1) for i in range(count - 1)]
        forward.append((count - 1, 0))
        backward = [(target, source) for source, target in forward]
        low = lax.ppermute(
            lax.slice_in_dim(block, block.shape[dim] - width, None, axis=dim), axis, forward
        )
        high = lax.ppermute(lax.slice_in_dim(block, 0, width, axis=dim), axis, backward)
        block = jnp.concatenate([low, block, high], axis=dim)
    return block


def shifted(block, axis, distance):
    devices = range(lax.axis_size(axis))
    route = [((i - distance) % len(devices), i) for i in devices]
    return lax.ppermute(block, axis, route)


def logical_right(value, amount):
    return lax.shift_right_logical(value, jnp.full(value.shape, amount, jnp.int32))


def keep_weights(seed_row, block_size):
    row_index = jnp.arange(block_size, dtype=jnp.int32)[:, None, None]
    col_index = jnp.arange(block_size, dtype=jnp.int32)[None, None, :]
    offset = row_index * block_size + col_index
    hashed = seed_row[:, None, :, None] * 40503 + offset[None]
    hashed = hashed ^ logical_right(hashed, 15)
    hashed = hashed * 739982445
    hashed = hashed ^ logical_right(hashed, 12)
    hashed = hashed * 695872825
    hashed = hashed ^ logical_right(hashed, 15)
    keep_scale = jnp.where(hashed & 1023 >= KEEP_LEVEL, KEEP_GAIN, 0.0).astype(jnp.float32)
    return keep_scale.reshape(seed_row.shape[0], block_size, -1)


def unrolled(body, carry, first, last):
    for j in range(first, last):
        carry = body(j, carry)
    return carry


def srl(value, amount):
    return lax.shift_right_logical(value, jnp.full(value.shape, amount, jnp.int32))


def attention_kernel(
    rows_ref, count_ref, seed_ref, q_ref, g_ref, kt_ref, vt_ref,
    att_ref, qg_ref, nk_ref, nv_ref, fk_ref, fv_ref,
    s_scr, keep_scr, drop_scr,
    *, scale, near_count, slot_count, blocks, head_size,
):
    p = pl.program_id(0)
    c = pl.program_id(1)
    width = q_ref.shape[-1]
    pair = width // head_size

    @pl.when(c == 0)
    def _():
        nk_ref[...] = jnp.zeros_like(nk_ref)
        nv_ref[...] = jnp.zeros_like(nv_ref)
        fk_ref[...] = jnp.zeros_like(fk_ref)
        fv_ref[...] = jnp.zeros_like(fv_ref)

    q = q_ref[...] * jnp.asarray(scale, q_ref.dtype)
    g = g_ref[...]
    lane_head = lax.broadcasted_iota(jnp.int32, (BS, width), 1) // head_size
    row_head = lax.broadcasted_iota(jnp.int32, (width, BS), 0) // head_size
    zero = jnp.zeros((), q.dtype)
    q_parts = [jnp.where(lane_head == a, q, zero) for a in range(pair)]
    g_parts = [jnp.where(lane_head == a, g, zero) for a in range(pair)]
    q_t = q.T
    g_t = g.T
    base = c * slot_count
    seed_base = [((p * pair + a) * blocks + c) * slot_count for a in range(pair)]
    live_end = L + 1 + count_ref[c]

    def start_of(j):
        return pl.multiple_of(rows_ref[base + j] * BS, BS)

    def keys(j):
        return kt_ref[pl.ds(start_of(j), BS), :]

    def values(j):
        return vt_ref[pl.ds(start_of(j), BS), :]

    def pick(parts, heads):
        out = parts[-1]
        for a in range(pair - 1):
            out = jnp.where(heads == a, parts[a], out)
        return out

    nt = (((1,), (1,)), ((), ()))
    f32 = jnp.float32
    m = [jnp.full((BS, BS), -jnp.inf, f32) for _ in range(pair)]
    q_stack = jnp.concatenate(q_parts, axis=0)
    g_stack = jnp.concatenate(g_parts, axis=0)
    for j in range(slot_count):
        k = keys(j)
        s_both = lax.dot_general(q_stack, k, nt, preferred_element_type=f32)
        for a in range(pair):
            s = s_both[a * BS : (a + 1) * BS]
            if j > L:
                s = jnp.where(j < live_end, s, MASKED)
            s_scr[a, j] = s
            m[a] = jnp.maximum(m[a], s)
    m = [jnp.max(x, axis=1, keepdims=True) for x in m]
    total = [jnp.zeros((BS, BS), f32) for _ in range(pair)]
    for j in range(slot_count):
        for a in range(pair):
            e = jnp.exp(s_scr[a, j] - m[a])
            s_scr[a, j] = e
            total[a] = total[a] + e
    inv = [1.0 / jnp.sum(x, axis=1, keepdims=True) for x in total]
    offs = (
        lax.broadcasted_iota(jnp.int32, (BS, BS), 0) * BS
        + lax.broadcasted_iota(jnp.int32, (BS, BS), 1)
    )
    acc_both = jnp.zeros((pair * BS, width), f32)
    for j in range(slot_count):
        v = values(j)
        drops = []
        for a in range(pair):
            att = s_scr[a, j] * inv[a]
            s_scr[a, j] = att
            word = seed_ref[seed_base[a] + j] * 40503 + offs
            word = word ^ srl(word, 15)
            word = word * 739982445
            word = word ^ srl(word, 12)
            word = word * 695872825
            word = word ^ srl(word, 15)
            keep = jnp.where((word & 1023) >= KEEP_LEVEL, KEEP_GAIN, 0.0).astype(f32)
            keep_scr[a, j] = keep
            dropped = (att * keep).astype(jnp.bfloat16)
            drop_scr[a, j] = dropped
            drops.append(dropped)
        acc_both = acc_both + jnp.dot(
            jnp.concatenate(drops, axis=0), v, preferred_element_type=f32
        )
    acc = [acc_both[a * BS : (a + 1) * BS] for a in range(pair)]
    attended = pick(acc, lane_head)
    att_ref[...] = attended.astype(att_ref.dtype)
    spread = g.astype(f32) * attended
    delta = [
        jnp.sum(jnp.where(lane_head == a, spread, 0.0), axis=1, keepdims=True) for a in range(pair)
    ]
    qacc_both = jnp.zeros((pair * BS, width), f32)
    for j in range(slot_count):
        k = keys(j)
        v = values(j)
        dg_both = lax.dot_general(g_stack, v, nt, preferred_element_type=f32)
        sgs = []
        for a in range(pair):
            dg = dg_both[a * BS : (a + 1) * BS]
            sgs.append((s_scr[a, j] * (dg * keep_scr[a, j] - delta[a])).astype(jnp.bfloat16))
        qacc_both = qacc_both + jnp.dot(
            jnp.concatenate(sgs, axis=0), k, preferred_element_type=f32
        )
        kp_both = jnp.dot(q_t, jnp.concatenate(sgs, axis=1), preferred_element_type=f32)
        vp_both = jnp.dot(
            g_t, jnp.concatenate([drop_scr[a, j] for a in range(pair)], axis=1),
            preferred_element_type=f32,
        )
        kp = pick([kp_both[:, a * BS : (a + 1) * BS] for a in range(pair)], row_head)
        vp = pick([vp_both[:, a * BS : (a + 1) * BS] for a in range(pair)], row_head)
        at = rows_ref[base + j]
        if j <= L:
            nk_ref[at] += kp
            nv_ref[at] += vp
        else:
            fk_ref[at - near_count] = kp.astype(fk_ref.dtype)
            fv_ref[at - near_count] = vp.astype(fv_ref.dtype)
    qacc = [qacc_both[a * BS : (a + 1) * BS] for a in range(pair)]
    qg_ref[...] = (pick(qacc, lane_head) * scale).astype(qg_ref.dtype)


def block_attention(rows, counts, seeds, q, g, kt, vt, *, near_count, far_count, scale, head_size):
    row_count, local_width = q.shape
    width = 2 * head_size
    groups = local_width // width
    blocks = row_count // BS
    slot_count = 1 + L + E
    kernel = functools.partial(
        attention_kernel, scale=scale, near_count=near_count, slot_count=slot_count,
        blocks=blocks, head_size=head_size,
    )
    q_spec = pl.BlockSpec((BS, width), lambda p, c, *_: (c, p))
    table_spec = pl.BlockSpec((kt.shape[0], width), lambda p, c, *_: (0, p))
    near_spec = pl.BlockSpec((near_count, width, BS), lambda p, c, *_: (0, p, 0))
    far_spec = pl.BlockSpec((far_count, width, BS), lambda p, c, *_: (0, p, 0))
    grid_spec = pltpu.PrefetchScalarGridSpec(
        num_scalar_prefetch=3,
        grid=(groups, blocks),
        in_specs=[q_spec, q_spec, table_spec, table_spec],
        out_specs=[q_spec, q_spec, near_spec, near_spec, far_spec, far_spec],
        scratch_shapes=[
            pltpu.VMEM((2, slot_count, BS, BS), jnp.float32),
            pltpu.VMEM((2, slot_count, BS, BS), jnp.float32),
            pltpu.VMEM((2, slot_count, BS, BS), jnp.bfloat16),
        ],
    )
    heads = local_width // head_size
    flops = 6 * 2 * heads * blocks * slot_count * BS * BS * width
    cost = pl.CostEstimate(
        flops=flops,
        transcendentals=heads * blocks * slot_count * BS * BS,
        bytes_accessed=2 * (q.size * 4 + kt.size * 2) + 4 * (near_count + far_count) * BS * local_width * 2,
    )
    return pl.pallas_call(
        kernel,
        grid_spec=grid_spec,
        out_shape=[
            jax.ShapeDtypeStruct(q.shape, jnp.bfloat16),
            jax.ShapeDtypeStruct(q.shape, jnp.bfloat16),
            jax.ShapeDtypeStruct((near_count, local_width, BS), jnp.float32),
            jax.ShapeDtypeStruct((near_count, local_width, BS), jnp.float32),
            jax.ShapeDtypeStruct((far_count, local_width, BS), jnp.bfloat16),
            jax.ShapeDtypeStruct((far_count, local_width, BS), jnp.bfloat16),
        ],
        compiler_params=pltpu.CompilerParams(
            dimension_semantics=("arbitrary", "arbitrary"), vmem_limit_bytes=48 * 1024 * 1024
        ),
        cost_estimate=cost,
    )(rows, counts, seeds, q, g, kt, vt)


def on_device(
    query_rows,
    key_rows,
    value_rows,
    out_grad,
    expander_device,
    expander_block,
    local_offset,
    live_count,
    drop_seed,
):
    head_count = lax.axis_size("head")
    head_index = lax.axis_index("head")
    share_rows = query_rows.shape[0]
    local_width = query_rows.shape[1] // head_count
    local_heads = drop_seed.shape[0]
    head_size = local_width // local_heads
    score_scale = head_size ** (-0.5)
    slot_count = 1 + L + E
    def to_columns(arrays):
        return lax.all_to_all(jnp.stack(arrays), "head", split_axis=2, concat_axis=1, tiled=True)

    key_local, value_local = to_columns([key_rows, value_rows])
    first_col = head_index * local_width
    query_local, grad_local = [
        lax.dynamic_slice_in_dim(
            lax.all_gather(member, "head", axis=0, tiled=True), first_col, local_width, 1
        )
        for member in (query_rows, out_grad)
    ]
    peer_count = lax.axis_size("blk")
    capacity = min(QB_DEV, max(2, (2 * QB_DEV * E + peer_count - 1) // peer_count))
    flat_device = expander_device.reshape(-1)
    matches = (flat_device[:, None] == jnp.arange(peer_count, dtype=jnp.int32)[None, :]).astype(
        jnp.int32
    )
    before = jnp.cumsum(matches, axis=0) - matches
    slot_rank = jnp.sum(before * matches, axis=1)
    far_position = flat_device * capacity + slot_rank
    far_live = jnp.arange(E, dtype=jnp.int32)[None, :] < live_count[:, None]
    asked_block = jnp.where(far_live, expander_block, -1)
    listing = lax.all_gather(
        jnp.stack([flat_device, asked_block.reshape(-1)]), "blk", axis=0, tiled=False
    )
    hit = (listing[:, 0] == lax.axis_index("blk")).astype(jnp.int32)
    hit_rank = jnp.cumsum(hit, axis=1) - hit
    wanted_here = jnp.stack(
        [
            jnp.sum(jnp.where((hit > 0) & (hit_rank == r), listing[:, 1] + 1, 0), axis=1) - 1
            for r in range(capacity)
        ],
        axis=1,
    )
    key_blocks = key_local.reshape(QB_DEV, BS, local_width)
    value_blocks = value_local.reshape(QB_DEV, BS, local_width)
    stacked = jnp.stack([key_blocks, value_blocks], axis=1)
    widened = padded(stacked, (("blk", 0),), W)
    wanted_flat = wanted_here.reshape(-1)
    chosen = jnp.clip(wanted_flat, 0, QB_DEV - 1)
    asked_mask = (wanted_flat >= 0)[:, None, None]
    zero_block = jnp.zeros((), jnp.bfloat16)
    reply_shape = (peer_count, capacity, BS, local_width)
    far_key, far_value = (
        lax.all_to_all(
            jnp.where(asked_mask, key_blocks[chosen], zero_block).reshape(reply_shape),
            "blk",
            split_axis=0,
            concat_axis=0,
            tiled=True,
        ),
        lax.all_to_all(
            jnp.where(asked_mask, value_blocks[chosen], zero_block).reshape(reply_shape),
            "blk",
            split_axis=0,
            concat_axis=0,
            tiled=True,
        ),
    )
    near_count = QB_DEV + 2 * W
    far_total_count = peer_count * capacity
    key_table = jnp.concatenate(
        [widened[:, 0], far_key.reshape(far_total_count, BS, local_width)], axis=0
    )
    value_table = jnp.concatenate(
        [widened[:, 1], far_value.reshape(far_total_count, BS, local_width)], axis=0
    )
    local_block = jnp.arange(QB_DEV, dtype=jnp.int32)[:, None]
    self_slot = local_block + W
    near_slot = local_block + W + local_offset
    far_slot = near_count + far_position.reshape(QB_DEV, E)
    table_rows = jnp.concatenate([self_slot, near_slot, far_slot], axis=1)
    slot_number = jnp.arange(slot_count, dtype=jnp.int32)[None, :]
    live_slots = (slot_number <= L) | (slot_number - 1 - L < live_count[:, None])
    slot_rows = table_rows.reshape(-1).astype(jnp.int32)
    seed_flat = drop_seed.reshape(-1).astype(jnp.int32)
    table_count = key_table.shape[0]

    att_out, qg_out, nk, nv, fk, fv = block_attention(
        slot_rows,
        live_count.astype(jnp.int32),
        seed_flat,
        query_local,
        grad_local,
        key_table.reshape(table_count * BS, local_width),
        value_table.reshape(table_count * BS, local_width),
        near_count=near_count,
        far_count=far_total_count,
        scale=score_scale,
        head_size=head_size,
    )
    outputs = (att_out, qg_out)
    column_shape = (peer_count, capacity, local_width, BS)
    back_key, back_value = (
        lax.all_to_all(fk.reshape(column_shape), "blk", split_axis=0, concat_axis=0, tiled=True),
        lax.all_to_all(fv.reshape(column_shape), "blk", split_axis=0, concat_axis=0, tiled=True),
    )
    owner_match = (
        jnp.arange(QB_DEV, dtype=jnp.int32)[:, None] == wanted_here.reshape(1, -1)
    ).astype(jnp.bfloat16)
    far_key_sum = jnp.dot(
        owner_match,
        back_key.reshape(far_total_count, BS * local_width),
        preferred_element_type=jnp.float32,
    ).reshape(QB_DEV, local_width, BS)
    far_value_sum = jnp.dot(
        owner_match,
        back_value.reshape(far_total_count, BS * local_width),
        preferred_element_type=jnp.float32,
    ).reshape(QB_DEV, local_width, BS)
    near_total = jnp.stack([nk, nv], axis=1)
    from_below = shifted(near_total[QB_DEV + W :].astype(jnp.bfloat16), "blk", 1).astype(
        jnp.float32
    )
    from_above = shifted(near_total[:W].astype(jnp.bfloat16), "blk", -1).astype(jnp.float32)
    own_total = near_total[W : W + QB_DEV]
    own_total = own_total.at[:W].add(from_below)
    own_total = own_total.at[QB_DEV - W :].add(from_above)
    block_rows = QB_DEV * BS
    key_grad = (own_total[:, 0] + far_key_sum).astype(jnp.bfloat16).transpose(0, 2, 1)
    value_grad = (own_total[:, 1] + far_value_sum).astype(jnp.bfloat16).transpose(0, 2, 1)
    def to_rows(arrays):
        return lax.all_to_all(jnp.stack(arrays), "head", split_axis=1, concat_axis=2, tiled=True)

    first_row = head_index * share_rows
    attended, query_grad = [
        lax.dynamic_slice_in_dim(
            lax.all_gather(member.reshape(block_rows, local_width), "head", axis=1, tiled=True),
            first_row,
            share_rows,
            0,
        )
        for member in outputs
    ]
    key_grad, value_grad = to_rows([
        key_grad.reshape(block_rows, local_width),
        value_grad.reshape(block_rows, local_width),
    ])
    return attended, query_grad, key_grad, value_grad


def solution(mesh):
    in_specs = (
        P(("blk", "head"), None),
        P(("blk", "head"), None),
        P(("blk", "head"), None),
        P(("blk", "head"), None),
        P("blk", None),
        P("blk", None),
        P("blk", None),
        P("blk"),
        P("head", "blk", None),
    )
    out_specs = (
        P(("blk", "head"), None),
        P(("blk", "head"), None),
        P(("blk", "head"), None),
        P(("blk", "head"), None),
    )
    return jax.shard_map(
        on_device, mesh=mesh, in_specs=in_specs, out_specs=out_specs, check_vma=False
    )
```

```python
import functools

import jax
import jax.numpy as jnp
from jax import lax
from jax.experimental import pallas as pl
from jax.experimental.pallas import tpu as pltpu
from jax.sharding import PartitionSpec as P

BS = 128
QB_DEV = 8
L = 11
E = 4
W = 4


KEEP_LEVEL = 102
KEEP_GAIN = 1024.0 / 922.0
MASKED = -1e30


def padded(block, sides, width):
    for axis, dim in sides:
        count = lax.axis_size(axis)
        forward = [(i, i + 1) for i in range(count - 1)]
        forward.append((count - 1, 0))
        backward = [(target, source) for source, target in forward]
        low = lax.ppermute(
            lax.slice_in_dim(block, block.shape[dim] - width, None, axis=dim), axis, forward
        )
        high = lax.ppermute(lax.slice_in_dim(block, 0, width, axis=dim), axis, backward)
        block = jnp.concatenate([low, block, high], axis=dim)
    return block


def shifted(block, axis, distance):
    devices = range(lax.axis_size(axis))
    route = [((i - distance) % len(devices), i) for i in devices]
    return lax.ppermute(block, axis, route)


def logical_right(value, amount):
    return lax.shift_right_logical(value, jnp.full(value.shape, amount, jnp.int32))


def keep_weights(seed_row, block_size):
    row_index = jnp.arange(block_size, dtype=jnp.int32)[:, None, None]
    col_index = jnp.arange(block_size, dtype=jnp.int32)[None, None, :]
    offset = row_index * block_size + col_index
    hashed = seed_row[:, None, :, None] * 40503 + offset[None]
    hashed = hashed ^ logical_right(hashed, 15)
    hashed = hashed * 739982445
    hashed = hashed ^ logical_right(hashed, 12)
    hashed = hashed * 695872825
    hashed = hashed ^ logical_right(hashed, 15)
    keep_scale = jnp.where(hashed & 1023 >= KEEP_LEVEL, KEEP_GAIN, 0.0).astype(jnp.float32)
    return keep_scale.reshape(seed_row.shape[0], block_size, -1)


def unrolled(body, carry, first, last):
    for j in range(first, last):
        carry = body(j, carry)
    return carry


def srl(value, amount):
    return lax.shift_right_logical(value, jnp.full(value.shape, amount, jnp.int32))


def attention_kernel(
    rows_ref, count_ref, seed_ref, q_ref, g_ref, kt_ref, vt_ref,
    att_ref, qg_ref, nk_ref, nv_ref, fk_ref, fv_ref,
    s_scr, keep_scr, drop_scr,
    *, scale, near_count, slot_count, blocks, head_size,
):
    p = pl.program_id(0)
    c = pl.program_id(1)
    width = q_ref.shape[-1]
    pair = width // head_size

    @pl.when(c == 0)
    def _():
        nk_ref[...] = jnp.zeros_like(nk_ref)
        nv_ref[...] = jnp.zeros_like(nv_ref)
        fk_ref[...] = jnp.zeros_like(fk_ref)
        fv_ref[...] = jnp.zeros_like(fv_ref)

    q = q_ref[...] * jnp.asarray(scale, q_ref.dtype)
    g = g_ref[...]
    lane_head = lax.broadcasted_iota(jnp.int32, (BS, width), 1) // head_size
    row_head = lax.broadcasted_iota(jnp.int32, (width, BS), 0) // head_size
    zero = jnp.zeros((), q.dtype)
    q_parts = [jnp.where(lane_head == a, q, zero) for a in range(pair)]
    g_parts = [jnp.where(lane_head == a, g, zero) for a in range(pair)]
    q_t = q.T
    g_t = g.T
    base = c * slot_count
    seed_base = [((p * pair + a) * blocks + c) * slot_count for a in range(pair)]
    live_end = L + 1 + count_ref[c]

    def start_of(j):
        return pl.multiple_of(rows_ref[base + j] * BS, BS)

    def keys(j):
        return kt_ref[pl.ds(start_of(j), BS), :]

    def values(j):
        return vt_ref[pl.ds(start_of(j), BS), :]

    def pick(parts, heads):
        out = parts[-1]
        for a in range(pair - 1):
            out = jnp.where(heads == a, parts[a], out)
        return out

    nt = (((1,), (1,)), ((), ()))
    f32 = jnp.float32
    m = [jnp.full((BS, BS), -jnp.inf, f32) for _ in range(pair)]
    q_stack = jnp.concatenate(q_parts, axis=0)
    g_stack = jnp.concatenate(g_parts, axis=0)
    for j in range(slot_count):
        k = keys(j)
        s_both = lax.dot_general(q_stack, k, nt, preferred_element_type=f32)
        for a in range(pair):
            s = s_both[a * BS : (a + 1) * BS]
            if j > L:
                s = jnp.where(j < live_end, s, MASKED)
            s_scr[a, j] = s
            m[a] = jnp.maximum(m[a], s)
    m = [jnp.max(x, axis=1, keepdims=True) for x in m]
    total = [jnp.zeros((BS, BS), f32) for _ in range(pair)]
    for j in range(slot_count):
        for a in range(pair):
            e = jnp.exp(s_scr[a, j] - m[a])
            s_scr[a, j] = e
            total[a] = total[a] + e
    inv = [1.0 / jnp.sum(x, axis=1, keepdims=True) for x in total]
    offs = (
        lax.broadcasted_iota(jnp.int32, (BS, BS), 0) * BS
        + lax.broadcasted_iota(jnp.int32, (BS, BS), 1)
    )
    acc_both = jnp.zeros((pair * BS, width), f32)
    for j in range(slot_count):
        v = values(j)
        drops = []
        for a in range(pair):
            att = s_scr[a, j] * inv[a]
            s_scr[a, j] = att
            word = seed_ref[seed_base[a] + j] * 40503 + offs
            word = word ^ srl(word, 15)
            word = word * 739982445
            word = word ^ srl(word, 12)
            word = word * 695872825
            word = word ^ srl(word, 15)
            keep = jnp.where((word & 1023) >= KEEP_LEVEL, KEEP_GAIN, 0.0).astype(f32)
            keep_scr[a, j] = keep
            dropped = (att * keep).astype(jnp.bfloat16)
            drop_scr[a, j] = dropped
            drops.append(dropped)
        acc_both = acc_both + jnp.dot(
            jnp.concatenate(drops, axis=0), v, preferred_element_type=f32
        )
    acc = [acc_both[a * BS : (a + 1) * BS] for a in range(pair)]
    attended = pick(acc, lane_head)
    att_ref[...] = attended.astype(att_ref.dtype)
    spread = g.astype(f32) * attended
    delta = [
        jnp.sum(jnp.where(lane_head == a, spread, 0.0), axis=1, keepdims=True) for a in range(pair)
    ]
    qacc_both = jnp.zeros((pair * BS, width), f32)
    for j in range(slot_count):
        k = keys(j)
        v = values(j)
        dg_both = lax.dot_general(g_stack, v, nt, preferred_element_type=f32)
        sgs = []
        for a in range(pair):
            dg = dg_both[a * BS : (a + 1) * BS]
            sgs.append((s_scr[a, j] * (dg * keep_scr[a, j] - delta[a])).astype(jnp.bfloat16))
        qacc_both = qacc_both + jnp.dot(
            jnp.concatenate(sgs, axis=0), k, preferred_element_type=f32
        )
        kp_both = jnp.dot(q_t, jnp.concatenate(sgs, axis=1), preferred_element_type=f32)
        vp_both = jnp.dot(
            g_t, jnp.concatenate([drop_scr[a, j] for a in range(pair)], axis=1),
            preferred_element_type=f32,
        )
        kp = pick([kp_both[:, a * BS : (a + 1) * BS] for a in range(pair)], row_head)
        vp = pick([vp_both[:, a * BS : (a + 1) * BS] for a in range(pair)], row_head)
        at = rows_ref[base + j]
        if j <= L:
            nk_ref[at] += kp
            nv_ref[at] += vp
        else:
            fk_ref[at - near_count] = kp.astype(fk_ref.dtype)
            fv_ref[at - near_count] = vp.astype(fv_ref.dtype)
    qacc = [qacc_both[a * BS : (a + 1) * BS] for a in range(pair)]
    qg_ref[...] = (pick(qacc, lane_head) * scale).astype(qg_ref.dtype)


def block_attention(rows, counts, seeds, q, g, kt, vt, *, near_count, far_count, scale, head_size):
    row_count, local_width = q.shape
    width = 2 * head_size
    groups = local_width // width
    blocks = row_count // BS
    slot_count = 1 + L + E
    kernel = functools.partial(
        attention_kernel, scale=scale, near_count=near_count, slot_count=slot_count,
        blocks=blocks, head_size=head_size,
    )
    q_spec = pl.BlockSpec((BS, width), lambda p, c, *_: (c, p))
    table_spec = pl.BlockSpec((kt.shape[0], width), lambda p, c, *_: (0, p))
    near_spec = pl.BlockSpec((near_count, width, BS), lambda p, c, *_: (0, p, 0))
    far_spec = pl.BlockSpec((far_count, width, BS), lambda p, c, *_: (0, p, 0))
    grid_spec = pltpu.PrefetchScalarGridSpec(
        num_scalar_prefetch=3,
        grid=(groups, blocks),
        in_specs=[q_spec, q_spec, table_spec, table_spec],
        out_specs=[q_spec, q_spec, near_spec, near_spec, far_spec, far_spec],
        scratch_shapes=[
            pltpu.VMEM((2, slot_count, BS, BS), jnp.float32),
            pltpu.VMEM((2, slot_count, BS, BS), jnp.float32),
            pltpu.VMEM((2, slot_count, BS, BS), jnp.bfloat16),
        ],
    )
    heads = local_width // head_size
    flops = 6 * 2 * heads * blocks * slot_count * BS * BS * width
    cost = pl.CostEstimate(
        flops=flops,
        transcendentals=heads * blocks * slot_count * BS * BS,
        bytes_accessed=2 * (q.size * 4 + kt.size * 2) + 4 * (near_count + far_count) * BS * local_width * 2,
    )
    return pl.pallas_call(
        kernel,
        grid_spec=grid_spec,
        out_shape=[
            jax.ShapeDtypeStruct(q.shape, jnp.bfloat16),
            jax.ShapeDtypeStruct(q.shape, jnp.bfloat16),
            jax.ShapeDtypeStruct((near_count, local_width, BS), jnp.float32),
            jax.ShapeDtypeStruct((near_count, local_width, BS), jnp.float32),
            jax.ShapeDtypeStruct((far_count, local_width, BS), jnp.bfloat16),
            jax.ShapeDtypeStruct((far_count, local_width, BS), jnp.bfloat16),
        ],
        compiler_params=pltpu.CompilerParams(
            dimension_semantics=("arbitrary", "arbitrary"), vmem_limit_bytes=48 * 1024 * 1024
        ),
        cost_estimate=cost,
    )(rows, counts, seeds, q, g, kt, vt)


def on_device(
    query_rows,
    key_rows,
    value_rows,
    out_grad,
    expander_device,
    expander_block,
    local_offset,
    live_count,
    drop_seed,
):
    head_count = lax.axis_size("head")
    head_index = lax.axis_index("head")
    share_rows = query_rows.shape[0]
    local_width = query_rows.shape[1] // head_count
    local_heads = drop_seed.shape[0]
    head_size = local_width // local_heads
    score_scale = head_size ** (-0.5)
    slot_count = 1 + L + E
    def to_columns(arrays):
        return lax.all_to_all(jnp.stack(arrays), "head", split_axis=2, concat_axis=1, tiled=True)

    key_local, value_local, query_local, grad_local = to_columns(
        [key_rows, value_rows, query_rows, out_grad]
    )
    peer_count = lax.axis_size("blk")
    capacity = min(QB_DEV, max(2, (2 * QB_DEV * E + peer_count - 1) // peer_count))
    flat_device = expander_device.reshape(-1)
    matches = (flat_device[:, None] == jnp.arange(peer_count, dtype=jnp.int32)[None, :]).astype(
        jnp.int32
    )
    before = jnp.cumsum(matches, axis=0) - matches
    slot_rank = jnp.sum(before * matches, axis=1)
    far_position = flat_device * capacity + slot_rank
    far_live = jnp.arange(E, dtype=jnp.int32)[None, :] < live_count[:, None]
    asked_block = jnp.where(far_live, expander_block, -1)
    listing = lax.all_gather(
        jnp.stack([flat_device, asked_block.reshape(-1)]), "blk", axis=0, tiled=False
    )
    hit = (listing[:, 0] == lax.axis_index("blk")).astype(jnp.int32)
    hit_rank = jnp.cumsum(hit, axis=1) - hit
    wanted_here = jnp.stack(
        [
            jnp.sum(jnp.where((hit > 0) & (hit_rank == r), listing[:, 1] + 1, 0), axis=1) - 1
            for r in range(capacity)
        ],
        axis=1,
    )
    key_blocks = key_local.reshape(QB_DEV, BS, local_width)
    value_blocks = value_local.reshape(QB_DEV, BS, local_width)
    stacked = jnp.stack([key_blocks, value_blocks], axis=1)
    widened = padded(stacked, (("blk", 0),), W)
    wanted_flat = wanted_here.reshape(-1)
    chosen = jnp.clip(wanted_flat, 0, QB_DEV - 1)
    asked_mask = (wanted_flat >= 0)[:, None, None]
    zero_block = jnp.zeros((), jnp.bfloat16)
    selection = (
        wanted_flat[:, None] == jnp.arange(QB_DEV, dtype=jnp.int32)[None, :]
    ).astype(jnp.bfloat16)

    def asked_of(blocks):
        return jnp.dot(
            selection, blocks.reshape(QB_DEV, -1), preferred_element_type=jnp.float32
        ).astype(jnp.bfloat16)
    reply_shape = (peer_count, capacity, BS, local_width)
    far_key, far_value = (
        lax.all_to_all(
            asked_of(key_blocks).reshape(reply_shape),
            "blk",
            split_axis=0,
            concat_axis=0,
            tiled=True,
        ),
        lax.all_to_all(
            asked_of(value_blocks).reshape(reply_shape),
            "blk",
            split_axis=0,
            concat_axis=0,
            tiled=True,
        ),
    )
    near_count = QB_DEV + 2 * W
    far_total_count = peer_count * capacity
    key_table = jnp.concatenate(
        [widened[:, 0], far_key.reshape(far_total_count, BS, local_width)], axis=0
    )
    value_table = jnp.concatenate(
        [widened[:, 1], far_value.reshape(far_total_count, BS, local_width)], axis=0
    )
    local_block = jnp.arange(QB_DEV, dtype=jnp.int32)[:, None]
    self_slot = local_block + W
    near_slot = local_block + W + local_offset
    far_slot = near_count + far_position.reshape(QB_DEV, E)
    table_rows = jnp.concatenate([self_slot, near_slot, far_slot], axis=1)
    slot_number = jnp.arange(slot_count, dtype=jnp.int32)[None, :]
    live_slots = (slot_number <= L) | (slot_number - 1 - L < live_count[:, None])
    slot_rows = table_rows.reshape(-1).astype(jnp.int32)
    seed_flat = drop_seed.reshape(-1).astype(jnp.int32)
    table_count = key_table.shape[0]

    att_out, qg_out, nk, nv, fk, fv = block_attention(
        slot_rows,
        live_count.astype(jnp.int32),
        seed_flat,
        query_local,
        grad_local,
        key_table.reshape(table_count * BS, local_width),
        value_table.reshape(table_count * BS, local_width),
        near_count=near_count,
        far_count=far_total_count,
        scale=score_scale,
        head_size=head_size,
    )
    outputs = (att_out, qg_out)
    column_shape = (peer_count, capacity, local_width, BS)
    back_key, back_value = (
        lax.all_to_all(fk.reshape(column_shape), "blk", split_axis=0, concat_axis=0, tiled=True),
        lax.all_to_all(fv.reshape(column_shape), "blk", split_axis=0, concat_axis=0, tiled=True),
    )
    owner_match = (
        jnp.arange(QB_DEV, dtype=jnp.int32)[:, None] == wanted_here.reshape(1, -1)
    ).astype(jnp.bfloat16)
    far_key_sum = jnp.dot(
        owner_match,
        back_key.reshape(far_total_count, BS * local_width),
        preferred_element_type=jnp.float32,
    ).reshape(QB_DEV, local_width, BS)
    far_value_sum = jnp.dot(
        owner_match,
        back_value.reshape(far_total_count, BS * local_width),
        preferred_element_type=jnp.float32,
    ).reshape(QB_DEV, local_width, BS)
    near_total = jnp.stack([nk, nv], axis=1)
    from_below = shifted(near_total[QB_DEV + W :].astype(jnp.bfloat16), "blk", 1).astype(
        jnp.float32
    )
    from_above = shifted(near_total[:W].astype(jnp.bfloat16), "blk", -1).astype(jnp.float32)
    own_total = near_total[W : W + QB_DEV]
    own_total = own_total.at[:W].add(from_below)
    own_total = own_total.at[QB_DEV - W :].add(from_above)
    block_rows = QB_DEV * BS
    key_grad = (own_total[:, 0] + far_key_sum).astype(jnp.bfloat16).transpose(0, 2, 1)
    value_grad = (own_total[:, 1] + far_value_sum).astype(jnp.bfloat16).transpose(0, 2, 1)
    def to_rows(arrays):
        return lax.all_to_all(jnp.stack(arrays), "head", split_axis=1, concat_axis=2, tiled=True)

    attended, query_grad = to_rows([
        outputs[0].reshape(block_rows, local_width),
        outputs[1].reshape(block_rows, local_width),
    ])
    key_grad, value_grad = to_rows([
        key_grad.reshape(block_rows, local_width),
        value_grad.reshape(block_rows, local_width),
    ])
    return attended, query_grad, key_grad, value_grad


def solution(mesh):
    in_specs = (
        P(("blk", "head"), None),
        P(("blk", "head"), None),
        P(("blk", "head"), None),
        P(("blk", "head"), None),
        P("blk", None),
        P("blk", None),
        P("blk", None),
        P("blk"),
        P("head", "blk", None),
    )
    out_specs = (
        P(("blk", "head"), None),
        P(("blk", "head"), None),
        P(("blk", "head"), None),
        P(("blk", "head"), None),
    )
    return jax.shard_map(
        on_device, mesh=mesh, in_specs=in_specs, out_specs=out_specs, check_vma=False
    )
```

```python
import functools

import jax
import jax.numpy as jnp
from jax import lax
from jax.experimental import pallas as pl
from jax.experimental.pallas import tpu as pltpu
from jax.sharding import PartitionSpec as P

BS = 128
QB_DEV = 8
L = 11
E = 4
W = 4


KEEP_LEVEL = 102
KEEP_GAIN = 1024.0 / 922.0
MASKED = -1e30


def padded(block, sides, width):
    for axis, dim in sides:
        count = lax.axis_size(axis)
        forward = [(i, i + 1) for i in range(count - 1)]
        forward.append((count - 1, 0))
        backward = [(target, source) for source, target in forward]
        low = lax.ppermute(
            lax.slice_in_dim(block, block.shape[dim] - width, None, axis=dim), axis, forward
        )
        high = lax.ppermute(lax.slice_in_dim(block, 0, width, axis=dim), axis, backward)
        block = jnp.concatenate([low, block, high], axis=dim)
    return block


def shifted(block, axis, distance):
    devices = range(lax.axis_size(axis))
    route = [((i - distance) % len(devices), i) for i in devices]
    return lax.ppermute(block, axis, route)


def logical_right(value, amount):
    return lax.shift_right_logical(value, jnp.full(value.shape, amount, jnp.int32))


def keep_weights(seed_row, block_size):
    row_index = jnp.arange(block_size, dtype=jnp.int32)[:, None, None]
    col_index = jnp.arange(block_size, dtype=jnp.int32)[None, None, :]
    offset = row_index * block_size + col_index
    hashed = seed_row[:, None, :, None] * 40503 + offset[None]
    hashed = hashed ^ logical_right(hashed, 15)
    hashed = hashed * 739982445
    hashed = hashed ^ logical_right(hashed, 12)
    hashed = hashed * 695872825
    hashed = hashed ^ logical_right(hashed, 15)
    keep_scale = jnp.where(hashed & 1023 >= KEEP_LEVEL, KEEP_GAIN, 0.0).astype(jnp.float32)
    return keep_scale.reshape(seed_row.shape[0], block_size, -1)


def unrolled(body, carry, first, last):
    for j in range(first, last):
        carry = body(j, carry)
    return carry


def srl(value, amount):
    return lax.shift_right_logical(value, jnp.full(value.shape, amount, jnp.int32))


def attention_kernel(
    rows_ref, count_ref, seed_ref, q_ref, g_ref, kt_ref, vt_ref, kf_ref, vf_ref,
    att_ref, qg_ref, nk_ref, nv_ref, fk_ref, fv_ref,
    s_scr, keep_scr, drop_scr,
    *, scale, near_count, slot_count, blocks, head_size,
):
    p = pl.program_id(0)
    c = pl.program_id(1)
    width = q_ref.shape[-1]
    pair = width // head_size

    @pl.when(c == 0)
    def _():
        nk_ref[...] = jnp.zeros_like(nk_ref)
        nv_ref[...] = jnp.zeros_like(nv_ref)
        fk_ref[...] = jnp.zeros_like(fk_ref)
        fv_ref[...] = jnp.zeros_like(fv_ref)

    q = q_ref[...] * jnp.asarray(scale, q_ref.dtype)
    g = g_ref[...]
    lane_head = lax.broadcasted_iota(jnp.int32, (BS, width), 1) // head_size
    row_head = lax.broadcasted_iota(jnp.int32, (width, BS), 0) // head_size
    zero = jnp.zeros((), q.dtype)
    q_parts = [jnp.where(lane_head == a, q, zero) for a in range(pair)]
    g_parts = [jnp.where(lane_head == a, g, zero) for a in range(pair)]
    q_t = q.T
    g_t = g.T
    base = c * slot_count
    seed_base = [((p * pair + a) * blocks + c) * slot_count for a in range(pair)]
    live_end = L + 1 + count_ref[c]

    def start_of(j):
        return pl.multiple_of(rows_ref[base + j] * BS, BS)

    def keys(j):
        if j <= L:
            return kt_ref[pl.ds(start_of(j), BS), :]
        return kf_ref[pl.ds(pl.multiple_of(start_of(j) - near_count * BS, BS), BS), :]

    def values(j):
        if j <= L:
            return vt_ref[pl.ds(start_of(j), BS), :]
        return vf_ref[pl.ds(pl.multiple_of(start_of(j) - near_count * BS, BS), BS), :]

    def pick(parts, heads):
        out = parts[-1]
        for a in range(pair - 1):
            out = jnp.where(heads == a, parts[a], out)
        return out

    nt = (((1,), (1,)), ((), ()))
    f32 = jnp.float32
    m = [jnp.full((BS, BS), -jnp.inf, f32) for _ in range(pair)]
    q_stack = jnp.concatenate(q_parts, axis=0)
    g_stack = jnp.concatenate(g_parts, axis=0)
    for j in range(slot_count):
        k = keys(j)
        s_both = lax.dot_general(q_stack, k, nt, preferred_element_type=f32)
        for a in range(pair):
            s = s_both[a * BS : (a + 1) * BS]
            if j > L:
                s = jnp.where(j < live_end, s, MASKED)
            s_scr[a, j] = s
            m[a] = jnp.maximum(m[a], s)
    m = [jnp.max(x, axis=1, keepdims=True) for x in m]
    total = [jnp.zeros((BS, BS), f32) for _ in range(pair)]
    for j in range(slot_count):
        for a in range(pair):
            e = jnp.exp(s_scr[a, j] - m[a])
            s_scr[a, j] = e
            total[a] = total[a] + e
    inv = [1.0 / jnp.sum(x, axis=1, keepdims=True) for x in total]
    offs = (
        lax.broadcasted_iota(jnp.int32, (BS, BS), 0) * BS
        + lax.broadcasted_iota(jnp.int32, (BS, BS), 1)
    )
    acc_both = jnp.zeros((pair * BS, width), f32)
    for j in range(slot_count):
        v = values(j)
        drops = []
        for a in range(pair):
            att = s_scr[a, j] * inv[a]
            s_scr[a, j] = att
            word = seed_ref[seed_base[a] + j] * 40503 + offs
            word = word ^ srl(word, 15)
            word = word * 739982445
            word = word ^ srl(word, 12)
            word = word * 695872825
            word = word ^ srl(word, 15)
            keep = jnp.where((word & 1023) >= KEEP_LEVEL, KEEP_GAIN, 0.0).astype(f32)
            keep_scr[a, j] = keep
            dropped = (att * keep).astype(jnp.bfloat16)
            drop_scr[a, j] = dropped
            drops.append(dropped)
        acc_both = acc_both + jnp.dot(
            jnp.concatenate(drops, axis=0), v, preferred_element_type=f32
        )
    acc = [acc_both[a * BS : (a + 1) * BS] for a in range(pair)]
    attended = pick(acc, lane_head)
    att_ref[...] = attended.astype(att_ref.dtype)
    spread = g.astype(f32) * attended
    delta = [
        jnp.sum(jnp.where(lane_head == a, spread, 0.0), axis=1, keepdims=True) for a in range(pair)
    ]
    qacc_both = jnp.zeros((pair * BS, width), f32)
    for j in range(slot_count):
        k = keys(j)
        v = values(j)
        dg_both = lax.dot_general(g_stack, v, nt, preferred_element_type=f32)
        sgs = []
        for a in range(pair):
            dg = dg_both[a * BS : (a + 1) * BS]
            sgs.append((s_scr[a, j] * (dg * keep_scr[a, j] - delta[a])).astype(jnp.bfloat16))
        qacc_both = qacc_both + jnp.dot(
            jnp.concatenate(sgs, axis=0), k, preferred_element_type=f32
        )
        kp_both = jnp.dot(q_t, jnp.concatenate(sgs, axis=1), preferred_element_type=f32)
        vp_both = jnp.dot(
            g_t, jnp.concatenate([drop_scr[a, j] for a in range(pair)], axis=1),
            preferred_element_type=f32,
        )
        kp = pick([kp_both[:, a * BS : (a + 1) * BS] for a in range(pair)], row_head)
        vp = pick([vp_both[:, a * BS : (a + 1) * BS] for a in range(pair)], row_head)
        at = rows_ref[base + j]
        if j <= L:
            nk_ref[at] += kp
            nv_ref[at] += vp
        else:
            fk_ref[at - near_count] = kp.astype(fk_ref.dtype)
            fv_ref[at - near_count] = vp.astype(fv_ref.dtype)
    qacc = [qacc_both[a * BS : (a + 1) * BS] for a in range(pair)]
    qg_ref[...] = (pick(qacc, lane_head) * scale).astype(qg_ref.dtype)


def block_attention(rows, counts, seeds, q, g, kt, vt, kf, vf, *, near_count, far_count, scale, head_size):
    row_count, local_width = q.shape
    width = 2 * head_size
    groups = local_width // width
    blocks = row_count // BS
    slot_count = 1 + L + E
    kernel = functools.partial(
        attention_kernel, scale=scale, near_count=near_count, slot_count=slot_count,
        blocks=blocks, head_size=head_size,
    )
    q_spec = pl.BlockSpec((BS, width), lambda p, c, *_: (c, p))
    table_spec = pl.BlockSpec((kt.shape[0], width), lambda p, c, *_: (0, p))
    far_table_spec = pl.BlockSpec((kf.shape[0], width), lambda p, c, *_: (0, p))
    near_spec = pl.BlockSpec((near_count, width, BS), lambda p, c, *_: (0, p, 0))
    far_spec = pl.BlockSpec((far_count, width, BS), lambda p, c, *_: (0, p, 0))
    grid_spec = pltpu.PrefetchScalarGridSpec(
        num_scalar_prefetch=3,
        grid=(groups, blocks),
        in_specs=[q_spec, q_spec, table_spec, table_spec, far_table_spec, far_table_spec],
        out_specs=[q_spec, q_spec, near_spec, near_spec, far_spec, far_spec],
        scratch_shapes=[
            pltpu.VMEM((2, slot_count, BS, BS), jnp.float32),
            pltpu.VMEM((2, slot_count, BS, BS), jnp.float32),
            pltpu.VMEM((2, slot_count, BS, BS), jnp.bfloat16),
        ],
    )
    heads = local_width // head_size
    flops = 6 * 2 * heads * blocks * slot_count * BS * BS * width
    cost = pl.CostEstimate(
        flops=flops,
        transcendentals=heads * blocks * slot_count * BS * BS,
        bytes_accessed=2 * (q.size * 4 + kt.size * 2) + 4 * (near_count + far_count) * BS * local_width * 2,
    )
    return pl.pallas_call(
        kernel,
        grid_spec=grid_spec,
        out_shape=[
            jax.ShapeDtypeStruct(q.shape, jnp.bfloat16),
            jax.ShapeDtypeStruct(q.shape, jnp.bfloat16),
            jax.ShapeDtypeStruct((near_count, local_width, BS), jnp.float32),
            jax.ShapeDtypeStruct((near_count, local_width, BS), jnp.float32),
            jax.ShapeDtypeStruct((far_count, local_width, BS), jnp.bfloat16),
            jax.ShapeDtypeStruct((far_count, local_width, BS), jnp.bfloat16),
        ],
        compiler_params=pltpu.CompilerParams(
            dimension_semantics=("arbitrary", "arbitrary"), vmem_limit_bytes=48 * 1024 * 1024
        ),
        cost_estimate=cost,
    )(rows, counts, seeds, q, g, kt, vt, kf, vf)


def on_device(
    query_rows,
    key_rows,
    value_rows,
    out_grad,
    expander_device,
    expander_block,
    local_offset,
    live_count,
    drop_seed,
):
    head_count = lax.axis_size("head")
    head_index = lax.axis_index("head")
    share_rows = query_rows.shape[0]
    local_width = query_rows.shape[1] // head_count
    local_heads = drop_seed.shape[0]
    head_size = local_width // local_heads
    score_scale = head_size ** (-0.5)
    slot_count = 1 + L + E
    def to_columns(arrays):
        return lax.all_to_all(jnp.stack(arrays), "head", split_axis=2, concat_axis=1, tiled=True)

    key_local, value_local, query_local, grad_local = to_columns(
        [key_rows, value_rows, query_rows, out_grad]
    )
    peer_count = lax.axis_size("blk")
    capacity = min(QB_DEV, max(2, (2 * QB_DEV * E + peer_count - 1) // peer_count))
    flat_device = expander_device.reshape(-1)
    matches = (flat_device[:, None] == jnp.arange(peer_count, dtype=jnp.int32)[None, :]).astype(
        jnp.int32
    )
    before = jnp.cumsum(matches, axis=0) - matches
    slot_rank = jnp.sum(before * matches, axis=1)
    far_position = flat_device * capacity + slot_rank
    far_live = jnp.arange(E, dtype=jnp.int32)[None, :] < live_count[:, None]
    asked_block = jnp.where(far_live, expander_block, -1)
    listing = lax.all_gather(
        jnp.stack([flat_device, asked_block.reshape(-1)]), "blk", axis=0, tiled=False
    )
    hit = (listing[:, 0] == lax.axis_index("blk")).astype(jnp.int32)
    hit_rank = jnp.cumsum(hit, axis=1) - hit
    wanted_here = jnp.stack(
        [
            jnp.sum(jnp.where((hit > 0) & (hit_rank == r), listing[:, 1] + 1, 0), axis=1) - 1
            for r in range(capacity)
        ],
        axis=1,
    )
    key_blocks = key_local.reshape(QB_DEV, BS, local_width)
    value_blocks = value_local.reshape(QB_DEV, BS, local_width)
    stacked = jnp.stack([key_blocks, value_blocks], axis=1)
    widened = padded(stacked, (("blk", 0),), W)
    wanted_flat = wanted_here.reshape(-1)
    chosen = jnp.clip(wanted_flat, 0, QB_DEV - 1)
    asked_mask = (wanted_flat >= 0)[:, None, None]
    zero_block = jnp.zeros((), jnp.bfloat16)
    selection = (
        wanted_flat[:, None] == jnp.arange(QB_DEV, dtype=jnp.int32)[None, :]
    ).astype(jnp.bfloat16)

    def asked_of(blocks):
        return jnp.dot(
            selection, blocks.reshape(QB_DEV, -1), preferred_element_type=jnp.float32
        ).astype(jnp.bfloat16)
    reply_shape = (peer_count, capacity, BS, local_width)
    far_key, far_value = (
        lax.all_to_all(
            asked_of(key_blocks).reshape(reply_shape),
            "blk",
            split_axis=0,
            concat_axis=0,
            tiled=True,
        ),
        lax.all_to_all(
            asked_of(value_blocks).reshape(reply_shape),
            "blk",
            split_axis=0,
            concat_axis=0,
            tiled=True,
        ),
    )
    near_count = QB_DEV + 2 * W
    far_total_count = peer_count * capacity
    local_block = jnp.arange(QB_DEV, dtype=jnp.int32)[:, None]
    self_slot = local_block + W
    near_slot = local_block + W + local_offset
    far_slot = near_count + far_position.reshape(QB_DEV, E)
    table_rows = jnp.concatenate([self_slot, near_slot, far_slot], axis=1)
    slot_number = jnp.arange(slot_count, dtype=jnp.int32)[None, :]
    live_slots = (slot_number <= L) | (slot_number - 1 - L < live_count[:, None])
    slot_rows = table_rows.reshape(-1).astype(jnp.int32)
    seed_flat = drop_seed.reshape(-1).astype(jnp.int32)

    att_out, qg_out, nk, nv, fk, fv = block_attention(
        slot_rows,
        live_count.astype(jnp.int32),
        seed_flat,
        query_local,
        grad_local,
        widened[:, 0].reshape(near_count * BS, local_width),
        widened[:, 1].reshape(near_count * BS, local_width),
        far_key.reshape(far_total_count * BS, local_width),
        far_value.reshape(far_total_count * BS, local_width),
        near_count=near_count,
        far_count=far_total_count,
        scale=score_scale,
        head_size=head_size,
    )
    outputs = (att_out, qg_out)
    column_shape = (peer_count, capacity, local_width, BS)
    back_key, back_value = (
        lax.all_to_all(fk.reshape(column_shape), "blk", split_axis=0, concat_axis=0, tiled=True),
        lax.all_to_all(fv.reshape(column_shape), "blk", split_axis=0, concat_axis=0, tiled=True),
    )
    owner_match = (
        jnp.arange(QB_DEV, dtype=jnp.int32)[:, None] == wanted_here.reshape(1, -1)
    ).astype(jnp.bfloat16)
    far_key_sum = jnp.dot(
        owner_match,
        back_key.reshape(far_total_count, BS * local_width),
        preferred_element_type=jnp.float32,
    ).reshape(QB_DEV, local_width, BS)
    far_value_sum = jnp.dot(
        owner_match,
        back_value.reshape(far_total_count, BS * local_width),
        preferred_element_type=jnp.float32,
    ).reshape(QB_DEV, local_width, BS)
    near_total = jnp.stack([nk, nv], axis=1)
    from_below = shifted(near_total[QB_DEV + W :].astype(jnp.bfloat16), "blk", 1).astype(
        jnp.float32
    )
    from_above = shifted(near_total[:W].astype(jnp.bfloat16), "blk", -1).astype(jnp.float32)
    own_total = near_total[W : W + QB_DEV]
    own_total = own_total.at[:W].add(from_below)
    own_total = own_total.at[QB_DEV - W :].add(from_above)
    block_rows = QB_DEV * BS
    key_grad = (own_total[:, 0] + far_key_sum).astype(jnp.bfloat16).transpose(0, 2, 1)
    value_grad = (own_total[:, 1] + far_value_sum).astype(jnp.bfloat16).transpose(0, 2, 1)
    def to_rows(arrays):
        return lax.all_to_all(jnp.stack(arrays), "head", split_axis=1, concat_axis=2, tiled=True)

    attended, query_grad = to_rows([
        outputs[0].reshape(block_rows, local_width),
        outputs[1].reshape(block_rows, local_width),
    ])
    key_grad, value_grad = to_rows([
        key_grad.reshape(block_rows, local_width),
        value_grad.reshape(block_rows, local_width),
    ])
    return attended, query_grad, key_grad, value_grad


def solution(mesh):
    in_specs = (
        P(("blk", "head"), None),
        P(("blk", "head"), None),
        P(("blk", "head"), None),
        P(("blk", "head"), None),
        P("blk", None),
        P("blk", None),
        P("blk", None),
        P("blk"),
        P("head", "blk", None),
    )
    out_specs = (
        P(("blk", "head"), None),
        P(("blk", "head"), None),
        P(("blk", "head"), None),
        P(("blk", "head"), None),
    )
    return jax.shard_map(
        on_device, mesh=mesh, in_specs=in_specs, out_specs=out_specs, check_vma=False
    )
```

```python
import functools

import jax
import jax.numpy as jnp
from jax import lax
from jax.experimental import pallas as pl
from jax.experimental.pallas import tpu as pltpu
from jax.sharding import PartitionSpec as P

BS = 128
QB_DEV = 8
L = 11
E = 4
W = 4


KEEP_LEVEL = 102
KEEP_GAIN = 1024.0 / 922.0
MASKED = -1e30


def padded(block, sides, width):
    for axis, dim in sides:
        count = lax.axis_size(axis)
        forward = [(i, i + 1) for i in range(count - 1)]
        forward.append((count - 1, 0))
        backward = [(target, source) for source, target in forward]
        low = lax.ppermute(
            lax.slice_in_dim(block, block.shape[dim] - width, None, axis=dim), axis, forward
        )
        high = lax.ppermute(lax.slice_in_dim(block, 0, width, axis=dim), axis, backward)
        block = jnp.concatenate([low, block, high], axis=dim)
    return block


def shifted(block, axis, distance):
    devices = range(lax.axis_size(axis))
    route = [((i - distance) % len(devices), i) for i in devices]
    return lax.ppermute(block, axis, route)


def logical_right(value, amount):
    return lax.shift_right_logical(value, jnp.full(value.shape, amount, jnp.int32))


def keep_weights(seed_row, block_size):
    row_index = jnp.arange(block_size, dtype=jnp.int32)[:, None, None]
    col_index = jnp.arange(block_size, dtype=jnp.int32)[None, None, :]
    offset = row_index * block_size + col_index
    hashed = seed_row[:, None, :, None] * 40503 + offset[None]
    hashed = hashed ^ logical_right(hashed, 15)
    hashed = hashed * 739982445
    hashed = hashed ^ logical_right(hashed, 12)
    hashed = hashed * 695872825
    hashed = hashed ^ logical_right(hashed, 15)
    keep_scale = jnp.where(hashed & 1023 >= KEEP_LEVEL, KEEP_GAIN, 0.0).astype(jnp.float32)
    return keep_scale.reshape(seed_row.shape[0], block_size, -1)


def unrolled(body, carry, first, last):
    for j in range(first, last):
        carry = body(j, carry)
    return carry


def srl(value, amount):
    return lax.shift_right_logical(value, jnp.full(value.shape, amount, jnp.int32))


def attention_kernel(
    rows_ref, count_ref, seed_ref, q_ref, g_ref, kt_ref, vt_ref, kf_ref, vf_ref,
    att_ref, qg_ref, nk_ref, nv_ref, fk_ref, fv_ref,
    s_scr, keep_scr, drop_scr,
    *, scale, near_count, slot_count, blocks, head_size,
):
    p = pl.program_id(0)
    c = pl.program_id(1)
    width = q_ref.shape[-1]
    pair = width // head_size

    @pl.when(c == 0)
    def _():
        nk_ref[...] = jnp.zeros_like(nk_ref)
        nv_ref[...] = jnp.zeros_like(nv_ref)
        fk_ref[...] = jnp.zeros_like(fk_ref)
        fv_ref[...] = jnp.zeros_like(fv_ref)

    q = q_ref[...] * jnp.asarray(scale, q_ref.dtype)
    g = g_ref[...]
    lane_head = lax.broadcasted_iota(jnp.int32, (BS, width), 1) // head_size
    row_head = lax.broadcasted_iota(jnp.int32, (width, BS), 0) // head_size
    zero = jnp.zeros((), q.dtype)
    q_parts = [jnp.where(lane_head == a, q, zero) for a in range(pair)]
    g_parts = [jnp.where(lane_head == a, g, zero) for a in range(pair)]
    q_t = q.T
    g_t = g.T
    base = c * slot_count
    seed_base = [((p * pair + a) * blocks + c) * slot_count for a in range(pair)]
    live_end = L + 1 + count_ref[c]

    def start_of(j):
        return pl.multiple_of(rows_ref[base + j] * BS, BS)

    def keys(j):
        if j <= L:
            return kt_ref[pl.ds(pl.multiple_of(rows_ref[base + j] * (2 * BS), BS), BS), :]
        return kf_ref[pl.ds(pl.multiple_of(start_of(j) - near_count * BS, BS), BS), :]

    def values(j):
        if j <= L:
            return kt_ref[pl.ds(pl.multiple_of(rows_ref[base + j] * (2 * BS) + BS, BS), BS), :]
        return vf_ref[pl.ds(pl.multiple_of(start_of(j) - near_count * BS, BS), BS), :]

    def pick(parts, heads):
        out = parts[-1]
        for a in range(pair - 1):
            out = jnp.where(heads == a, parts[a], out)
        return out

    nt = (((1,), (1,)), ((), ()))
    f32 = jnp.float32
    m = [jnp.full((BS, BS), -jnp.inf, f32) for _ in range(pair)]
    q_stack = jnp.concatenate(q_parts, axis=0)
    g_stack = jnp.concatenate(g_parts, axis=0)
    for j in range(slot_count):
        k = keys(j)
        s_both = lax.dot_general(q_stack, k, nt, preferred_element_type=f32)
        for a in range(pair):
            s = s_both[a * BS : (a + 1) * BS]
            if j > L:
                s = jnp.where(j < live_end, s, MASKED)
            s_scr[a, j] = s
            m[a] = jnp.maximum(m[a], s)
    m = [jnp.max(x, axis=1, keepdims=True) for x in m]
    total = [jnp.zeros((BS, BS), f32) for _ in range(pair)]
    for j in range(slot_count):
        for a in range(pair):
            e = jnp.exp(s_scr[a, j] - m[a])
            s_scr[a, j] = e
            total[a] = total[a] + e
    inv = [1.0 / jnp.sum(x, axis=1, keepdims=True) for x in total]
    offs = (
        lax.broadcasted_iota(jnp.int32, (BS, BS), 0) * BS
        + lax.broadcasted_iota(jnp.int32, (BS, BS), 1)
    )
    acc_both = jnp.zeros((pair * BS, width), f32)
    for j in range(slot_count):
        v = values(j)
        drops = []
        for a in range(pair):
            att = s_scr[a, j] * inv[a]
            s_scr[a, j] = att
            word = seed_ref[seed_base[a] + j] * 40503 + offs
            word = word ^ srl(word, 15)
            word = word * 739982445
            word = word ^ srl(word, 12)
            word = word * 695872825
            word = word ^ srl(word, 15)
            keep = jnp.where((word & 1023) >= KEEP_LEVEL, KEEP_GAIN, 0.0).astype(f32)
            keep_scr[a, j] = keep
            dropped = (att * keep).astype(jnp.bfloat16)
            drop_scr[a, j] = dropped
            drops.append(dropped)
        acc_both = acc_both + jnp.dot(
            jnp.concatenate(drops, axis=0), v, preferred_element_type=f32
        )
    acc = [acc_both[a * BS : (a + 1) * BS] for a in range(pair)]
    attended = pick(acc, lane_head)
    att_ref[...] = attended.astype(att_ref.dtype)
    spread = g.astype(f32) * attended
    delta = [
        jnp.sum(jnp.where(lane_head == a, spread, 0.0), axis=1, keepdims=True) for a in range(pair)
    ]
    qacc_both = jnp.zeros((pair * BS, width), f32)
    for j in range(slot_count):
        k = keys(j)
        v = values(j)
        dg_both = lax.dot_general(g_stack, v, nt, preferred_element_type=f32)
        sgs = []
        for a in range(pair):
            dg = dg_both[a * BS : (a + 1) * BS]
            sgs.append((s_scr[a, j] * (dg * keep_scr[a, j] - delta[a])).astype(jnp.bfloat16))
        qacc_both = qacc_both + jnp.dot(
            jnp.concatenate(sgs, axis=0), k, preferred_element_type=f32
        )
        kp_both = jnp.dot(q_t, jnp.concatenate(sgs, axis=1), preferred_element_type=f32)
        vp_both = jnp.dot(
            g_t, jnp.concatenate([drop_scr[a, j] for a in range(pair)], axis=1),
            preferred_element_type=f32,
        )
        kp = pick([kp_both[:, a * BS : (a + 1) * BS] for a in range(pair)], row_head)
        vp = pick([vp_both[:, a * BS : (a + 1) * BS] for a in range(pair)], row_head)
        at = rows_ref[base + j]
        if j <= L:
            nk_ref[at] += kp
            nv_ref[at] += vp
        else:
            fk_ref[at - near_count] = kp.astype(fk_ref.dtype)
            fv_ref[at - near_count] = vp.astype(fv_ref.dtype)
    qacc = [qacc_both[a * BS : (a + 1) * BS] for a in range(pair)]
    qg_ref[...] = (pick(qacc, lane_head) * scale).astype(qg_ref.dtype)


def block_attention(rows, counts, seeds, q, g, kt, vt, kf, vf, *, near_count, far_count, scale, head_size):
    row_count, local_width = q.shape
    width = 2 * head_size
    groups = local_width // width
    blocks = row_count // BS
    slot_count = 1 + L + E
    kernel = functools.partial(
        attention_kernel, scale=scale, near_count=near_count, slot_count=slot_count,
        blocks=blocks, head_size=head_size,
    )
    q_spec = pl.BlockSpec((BS, width), lambda p, c, *_: (c, p))
    table_spec = pl.BlockSpec((kt.shape[0], width), lambda p, c, *_: (0, p))
    far_table_spec = pl.BlockSpec((kf.shape[0], width), lambda p, c, *_: (0, p))
    near_spec = pl.BlockSpec((near_count, width, BS), lambda p, c, *_: (0, p, 0))
    far_spec = pl.BlockSpec((far_count, width, BS), lambda p, c, *_: (0, p, 0))
    grid_spec = pltpu.PrefetchScalarGridSpec(
        num_scalar_prefetch=3,
        grid=(groups, blocks),
        in_specs=[q_spec, q_spec, table_spec, table_spec, far_table_spec, far_table_spec],
        out_specs=[q_spec, q_spec, near_spec, near_spec, far_spec, far_spec],
        scratch_shapes=[
            pltpu.VMEM((2, slot_count, BS, BS), jnp.float32),
            pltpu.VMEM((2, slot_count, BS, BS), jnp.float32),
            pltpu.VMEM((2, slot_count, BS, BS), jnp.bfloat16),
        ],
    )
    heads = local_width // head_size
    flops = 6 * 2 * heads * blocks * slot_count * BS * BS * width
    cost = pl.CostEstimate(
        flops=flops,
        transcendentals=heads * blocks * slot_count * BS * BS,
        bytes_accessed=2 * (q.size * 4 + kt.size * 2) + 4 * (near_count + far_count) * BS * local_width * 2,
    )
    return pl.pallas_call(
        kernel,
        grid_spec=grid_spec,
        out_shape=[
            jax.ShapeDtypeStruct(q.shape, jnp.bfloat16),
            jax.ShapeDtypeStruct(q.shape, jnp.bfloat16),
            jax.ShapeDtypeStruct((near_count, local_width, BS), jnp.float32),
            jax.ShapeDtypeStruct((near_count, local_width, BS), jnp.float32),
            jax.ShapeDtypeStruct((far_count, local_width, BS), jnp.bfloat16),
            jax.ShapeDtypeStruct((far_count, local_width, BS), jnp.bfloat16),
        ],
        compiler_params=pltpu.CompilerParams(
            dimension_semantics=("arbitrary", "arbitrary"), vmem_limit_bytes=48 * 1024 * 1024
        ),
        cost_estimate=cost,
    )(rows, counts, seeds, q, g, kt, vt, kf, vf)


def on_device(
    query_rows,
    key_rows,
    value_rows,
    out_grad,
    expander_device,
    expander_block,
    local_offset,
    live_count,
    drop_seed,
):
    head_count = lax.axis_size("head")
    head_index = lax.axis_index("head")
    share_rows = query_rows.shape[0]
    local_width = query_rows.shape[1] // head_count
    local_heads = drop_seed.shape[0]
    head_size = local_width // local_heads
    score_scale = head_size ** (-0.5)
    slot_count = 1 + L + E
    def to_columns(arrays):
        return lax.all_to_all(jnp.stack(arrays), "head", split_axis=2, concat_axis=1, tiled=True)

    key_local, value_local, query_local, grad_local = to_columns(
        [key_rows, value_rows, query_rows, out_grad]
    )
    peer_count = lax.axis_size("blk")
    capacity = min(QB_DEV, max(2, (2 * QB_DEV * E + peer_count - 1) // peer_count))
    flat_device = expander_device.reshape(-1)
    matches = (flat_device[:, None] == jnp.arange(peer_count, dtype=jnp.int32)[None, :]).astype(
        jnp.int32
    )
    before = jnp.cumsum(matches, axis=0) - matches
    slot_rank = jnp.sum(before * matches, axis=1)
    far_position = flat_device * capacity + slot_rank
    far_live = jnp.arange(E, dtype=jnp.int32)[None, :] < live_count[:, None]
    asked_block = jnp.where(far_live, expander_block, -1)
    listing = lax.all_gather(
        jnp.stack([flat_device, asked_block.reshape(-1)]), "blk", axis=0, tiled=False
    )
    hit = (listing[:, 0] == lax.axis_index("blk")).astype(jnp.int32)
    hit_rank = jnp.cumsum(hit, axis=1) - hit
    wanted_here = jnp.stack(
        [
            jnp.sum(jnp.where((hit > 0) & (hit_rank == r), listing[:, 1] + 1, 0), axis=1) - 1
            for r in range(capacity)
        ],
        axis=1,
    )
    key_blocks = key_local.reshape(QB_DEV, BS, local_width)
    value_blocks = value_local.reshape(QB_DEV, BS, local_width)
    stacked = jnp.stack([key_blocks, value_blocks], axis=1)
    widened = padded(stacked, (("blk", 0),), W)
    wanted_flat = wanted_here.reshape(-1)
    chosen = jnp.clip(wanted_flat, 0, QB_DEV - 1)
    asked_mask = (wanted_flat >= 0)[:, None, None]
    zero_block = jnp.zeros((), jnp.bfloat16)
    selection = (
        wanted_flat[:, None] == jnp.arange(QB_DEV, dtype=jnp.int32)[None, :]
    ).astype(jnp.bfloat16)

    def asked_of(blocks):
        return jnp.dot(
            selection, blocks.reshape(QB_DEV, -1), preferred_element_type=jnp.float32
        ).astype(jnp.bfloat16)
    reply_shape = (peer_count, capacity, BS, local_width)
    far_key, far_value = (
        lax.all_to_all(
            asked_of(key_blocks).reshape(reply_shape),
            "blk",
            split_axis=0,
            concat_axis=0,
            tiled=True,
        ),
        lax.all_to_all(
            asked_of(value_blocks).reshape(reply_shape),
            "blk",
            split_axis=0,
            concat_axis=0,
            tiled=True,
        ),
    )
    near_count = QB_DEV + 2 * W
    far_total_count = peer_count * capacity
    local_block = jnp.arange(QB_DEV, dtype=jnp.int32)[:, None]
    self_slot = local_block + W
    near_slot = local_block + W + local_offset
    far_slot = near_count + far_position.reshape(QB_DEV, E)
    table_rows = jnp.concatenate([self_slot, near_slot, far_slot], axis=1)
    slot_number = jnp.arange(slot_count, dtype=jnp.int32)[None, :]
    live_slots = (slot_number <= L) | (slot_number - 1 - L < live_count[:, None])
    slot_rows = table_rows.reshape(-1).astype(jnp.int32)
    seed_flat = drop_seed.reshape(-1).astype(jnp.int32)

    att_out, qg_out, nk, nv, fk, fv = block_attention(
        slot_rows,
        live_count.astype(jnp.int32),
        seed_flat,
        query_local,
        grad_local,
        widened.reshape(near_count * 2 * BS, local_width),
        widened.reshape(near_count * 2 * BS, local_width),
        far_key.reshape(far_total_count * BS, local_width),
        far_value.reshape(far_total_count * BS, local_width),
        near_count=near_count,
        far_count=far_total_count,
        scale=score_scale,
        head_size=head_size,
    )
    outputs = (att_out, qg_out)
    column_shape = (peer_count, capacity, local_width, BS)
    back_key, back_value = (
        lax.all_to_all(fk.reshape(column_shape), "blk", split_axis=0, concat_axis=0, tiled=True),
        lax.all_to_all(fv.reshape(column_shape), "blk", split_axis=0, concat_axis=0, tiled=True),
    )
    owner_match = (
        jnp.arange(QB_DEV, dtype=jnp.int32)[:, None] == wanted_here.reshape(1, -1)
    ).astype(jnp.bfloat16)
    far_key_sum = jnp.dot(
        owner_match,
        back_key.reshape(far_total_count, BS * local_width),
        preferred_element_type=jnp.float32,
    ).reshape(QB_DEV, local_width, BS)
    far_value_sum = jnp.dot(
        owner_match,
        back_value.reshape(far_total_count, BS * local_width),
        preferred_element_type=jnp.float32,
    ).reshape(QB_DEV, local_width, BS)
    near_total = jnp.stack([nk, nv], axis=1)
    from_below = shifted(near_total[QB_DEV + W :].astype(jnp.bfloat16), "blk", 1).astype(
        jnp.float32
    )
    from_above = shifted(near_total[:W].astype(jnp.bfloat16), "blk", -1).astype(jnp.float32)
    own_total = near_total[W : W + QB_DEV]
    own_total = own_total.at[:W].add(from_below)
    own_total = own_total.at[QB_DEV - W :].add(from_above)
    block_rows = QB_DEV * BS
    key_grad = (own_total[:, 0] + far_key_sum).astype(jnp.bfloat16).transpose(0, 2, 1)
    value_grad = (own_total[:, 1] + far_value_sum).astype(jnp.bfloat16).transpose(0, 2, 1)
    def to_rows(arrays):
        return lax.all_to_all(jnp.stack(arrays), "head", split_axis=1, concat_axis=2, tiled=True)

    attended, query_grad = to_rows([
        outputs[0].reshape(block_rows, local_width),
        outputs[1].reshape(block_rows, local_width),
    ])
    key_grad, value_grad = to_rows([
        key_grad.reshape(block_rows, local_width),
        value_grad.reshape(block_rows, local_width),
    ])
    return attended, query_grad, key_grad, value_grad


def solution(mesh):
    in_specs = (
        P(("blk", "head"), None),
        P(("blk", "head"), None),
        P(("blk", "head"), None),
        P(("blk", "head"), None),
        P("blk", None),
        P("blk", None),
        P("blk", None),
        P("blk"),
        P("head", "blk", None),
    )
    out_specs = (
        P(("blk", "head"), None),
        P(("blk", "head"), None),
        P(("blk", "head"), None),
        P(("blk", "head"), None),
    )
    return jax.shard_map(
        on_device, mesh=mesh, in_specs=in_specs, out_specs=out_specs, check_vma=False
    )
```

```python
import functools

import jax
import jax.numpy as jnp
from jax import lax
from jax.experimental import pallas as pl
from jax.experimental.pallas import tpu as pltpu
from jax.sharding import PartitionSpec as P

BS = 128
QB_DEV = 8
L = 11
E = 4
W = 4


KEEP_LEVEL = 102
KEEP_GAIN = 1024.0 / 922.0
MASKED = -1e30


def padded(block, sides, width):
    for axis, dim in sides:
        count = lax.axis_size(axis)
        forward = [(i, i + 1) for i in range(count - 1)]
        forward.append((count - 1, 0))
        backward = [(target, source) for source, target in forward]
        low = lax.ppermute(
            lax.slice_in_dim(block, block.shape[dim] - width, None, axis=dim), axis, forward
        )
        high = lax.ppermute(lax.slice_in_dim(block, 0, width, axis=dim), axis, backward)
        block = jnp.concatenate([low, block, high], axis=dim)
    return block


def shifted(block, axis, distance):
    devices = range(lax.axis_size(axis))
    route = [((i - distance) % len(devices), i) for i in devices]
    return lax.ppermute(block, axis, route)


def logical_right(value, amount):
    return lax.shift_right_logical(value, jnp.full(value.shape, amount, jnp.int32))


def keep_weights(seed_row, block_size):
    row_index = jnp.arange(block_size, dtype=jnp.int32)[:, None, None]
    col_index = jnp.arange(block_size, dtype=jnp.int32)[None, None, :]
    offset = row_index * block_size + col_index
    hashed = seed_row[:, None, :, None] * 40503 + offset[None]
    hashed = hashed ^ logical_right(hashed, 15)
    hashed = hashed * 739982445
    hashed = hashed ^ logical_right(hashed, 12)
    hashed = hashed * 695872825
    hashed = hashed ^ logical_right(hashed, 15)
    keep_scale = jnp.where(hashed & 1023 >= KEEP_LEVEL, KEEP_GAIN, 0.0).astype(jnp.float32)
    return keep_scale.reshape(seed_row.shape[0], block_size, -1)


def unrolled(body, carry, first, last):
    for j in range(first, last):
        carry = body(j, carry)
    return carry


def srl(value, amount):
    return lax.shift_right_logical(value, jnp.full(value.shape, amount, jnp.int32))


def attention_kernel(
    rows_ref, count_ref, seed_ref, q_ref, g_ref, kt_ref, vt_ref, kf_ref, vf_ref,
    pair_out_ref, nk_ref, nv_ref, fk_ref, fv_ref,
    s_scr, keep_scr, drop_scr,
    *, scale, near_count, slot_count, blocks, head_size,
):
    p = pl.program_id(0)
    c = pl.program_id(1)
    width = q_ref.shape[-1]
    pair = width // head_size

    @pl.when(c == 0)
    def _():
        nk_ref[...] = jnp.zeros_like(nk_ref)
        nv_ref[...] = jnp.zeros_like(nv_ref)
        fk_ref[...] = jnp.zeros_like(fk_ref)
        fv_ref[...] = jnp.zeros_like(fv_ref)

    q = q_ref[...] * jnp.asarray(scale, q_ref.dtype)
    g = g_ref[...]
    lane_head = lax.broadcasted_iota(jnp.int32, (BS, width), 1) // head_size
    row_head = lax.broadcasted_iota(jnp.int32, (width, BS), 0) // head_size
    zero = jnp.zeros((), q.dtype)
    q_parts = [jnp.where(lane_head == a, q, zero) for a in range(pair)]
    g_parts = [jnp.where(lane_head == a, g, zero) for a in range(pair)]
    q_t = q.T
    g_t = g.T
    base = c * slot_count
    seed_base = [((p * pair + a) * blocks + c) * slot_count for a in range(pair)]
    live_end = L + 1 + count_ref[c]

    def start_of(j):
        return pl.multiple_of(rows_ref[base + j] * BS, BS)

    def keys(j):
        if j <= L:
            return kt_ref[pl.ds(start_of(j), BS), :]
        return kf_ref[pl.ds(pl.multiple_of(start_of(j) - near_count * BS, BS), BS), :]

    def values(j):
        if j <= L:
            return vt_ref[pl.ds(start_of(j), BS), :]
        return vf_ref[pl.ds(pl.multiple_of(start_of(j) - near_count * BS, BS), BS), :]

    def pick(parts, heads):
        out = parts[-1]
        for a in range(pair - 1):
            out = jnp.where(heads == a, parts[a], out)
        return out

    nt = (((1,), (1,)), ((), ()))
    f32 = jnp.float32
    m = [jnp.full((BS, BS), -jnp.inf, f32) for _ in range(pair)]
    q_stack = jnp.concatenate(q_parts, axis=0)
    g_stack = jnp.concatenate(g_parts, axis=0)
    for j in range(slot_count):
        k = keys(j)
        s_both = lax.dot_general(q_stack, k, nt, preferred_element_type=f32)
        for a in range(pair):
            s = s_both[a * BS : (a + 1) * BS]
            if j > L:
                s = jnp.where(j < live_end, s, MASKED)
            s_scr[a, j] = s
            m[a] = jnp.maximum(m[a], s)
    m = [jnp.max(x, axis=1, keepdims=True) for x in m]
    total = [jnp.zeros((BS, BS), f32) for _ in range(pair)]
    for j in range(slot_count):
        for a in range(pair):
            e = jnp.exp(s_scr[a, j] - m[a])
            s_scr[a, j] = e
            total[a] = total[a] + e
    inv = [1.0 / jnp.sum(x, axis=1, keepdims=True) for x in total]
    offs = (
        lax.broadcasted_iota(jnp.int32, (BS, BS), 0) * BS
        + lax.broadcasted_iota(jnp.int32, (BS, BS), 1)
    )
    acc_both = jnp.zeros((pair * BS, width), f32)
    for j in range(slot_count):
        v = values(j)
        drops = []
        for a in range(pair):
            att = s_scr[a, j] * inv[a]
            s_scr[a, j] = att
            word = seed_ref[seed_base[a] + j] * 40503 + offs
            word = word ^ srl(word, 15)
            word = word * 739982445
            word = word ^ srl(word, 12)
            word = word * 695872825
            word = word ^ srl(word, 15)
            keep = jnp.where((word & 1023) >= KEEP_LEVEL, KEEP_GAIN, 0.0).astype(f32)
            keep_scr[a, j] = keep
            dropped = (att * keep).astype(jnp.bfloat16)
            drop_scr[a, j] = dropped
            drops.append(dropped)
        acc_both = acc_both + jnp.dot(
            jnp.concatenate(drops, axis=0), v, preferred_element_type=f32
        )
    acc = [acc_both[a * BS : (a + 1) * BS] for a in range(pair)]
    attended = pick(acc, lane_head)
    pair_out_ref[0] = attended.astype(pair_out_ref.dtype)
    spread = g.astype(f32) * attended
    delta = [
        jnp.sum(jnp.where(lane_head == a, spread, 0.0), axis=1, keepdims=True) for a in range(pair)
    ]
    qacc_both = jnp.zeros((pair * BS, width), f32)
    for j in range(slot_count):
        k = keys(j)
        v = values(j)
        dg_both = lax.dot_general(g_stack, v, nt, preferred_element_type=f32)
        sgs = []
        for a in range(pair):
            dg = dg_both[a * BS : (a + 1) * BS]
            sgs.append((s_scr[a, j] * (dg * keep_scr[a, j] - delta[a])).astype(jnp.bfloat16))
        qacc_both = qacc_both + jnp.dot(
            jnp.concatenate(sgs, axis=0), k, preferred_element_type=f32
        )
        kp_both = jnp.dot(q_t, jnp.concatenate(sgs, axis=1), preferred_element_type=f32)
        vp_both = jnp.dot(
            g_t, jnp.concatenate([drop_scr[a, j] for a in range(pair)], axis=1),
            preferred_element_type=f32,
        )
        kp = pick([kp_both[:, a * BS : (a + 1) * BS] for a in range(pair)], row_head)
        vp = pick([vp_both[:, a * BS : (a + 1) * BS] for a in range(pair)], row_head)
        at = rows_ref[base + j]
        if j <= L:
            nk_ref[at] += kp
            nv_ref[at] += vp
        else:
            fk_ref[at - near_count] = kp.astype(fk_ref.dtype)
            fv_ref[at - near_count] = vp.astype(fv_ref.dtype)
    qacc = [qacc_both[a * BS : (a + 1) * BS] for a in range(pair)]
    pair_out_ref[1] = (pick(qacc, lane_head) * scale).astype(pair_out_ref.dtype)


def block_attention(rows, counts, seeds, q, g, kt, vt, kf, vf, *, near_count, far_count, scale, head_size):
    row_count, local_width = q.shape
    width = 2 * head_size
    groups = local_width // width
    blocks = row_count // BS
    slot_count = 1 + L + E
    kernel = functools.partial(
        attention_kernel, scale=scale, near_count=near_count, slot_count=slot_count,
        blocks=blocks, head_size=head_size,
    )
    q_spec = pl.BlockSpec((BS, width), lambda p, c, *_: (c, p))
    pair_spec = pl.BlockSpec((2, BS, width), lambda p, c, *_: (0, c, p))
    table_spec = pl.BlockSpec((kt.shape[0], width), lambda p, c, *_: (0, p))
    far_table_spec = pl.BlockSpec((kf.shape[0], width), lambda p, c, *_: (0, p))
    near_spec = pl.BlockSpec((near_count, width, BS), lambda p, c, *_: (0, p, 0))
    far_spec = pl.BlockSpec((far_count, width, BS), lambda p, c, *_: (0, p, 0))
    grid_spec = pltpu.PrefetchScalarGridSpec(
        num_scalar_prefetch=3,
        grid=(groups, blocks),
        in_specs=[q_spec, q_spec, table_spec, table_spec, far_table_spec, far_table_spec],
        out_specs=[pair_spec, near_spec, near_spec, far_spec, far_spec],
        scratch_shapes=[
            pltpu.VMEM((2, slot_count, BS, BS), jnp.float32),
            pltpu.VMEM((2, slot_count, BS, BS), jnp.float32),
            pltpu.VMEM((2, slot_count, BS, BS), jnp.bfloat16),
        ],
    )
    heads = local_width // head_size
    flops = 6 * 2 * heads * blocks * slot_count * BS * BS * width
    cost = pl.CostEstimate(
        flops=flops,
        transcendentals=heads * blocks * slot_count * BS * BS,
        bytes_accessed=2 * (q.size * 4 + kt.size * 2) + 4 * (near_count + far_count) * BS * local_width * 2,
    )
    return pl.pallas_call(
        kernel,
        grid_spec=grid_spec,
        out_shape=[
            jax.ShapeDtypeStruct((2,) + q.shape, jnp.bfloat16),
            jax.ShapeDtypeStruct((near_count, local_width, BS), jnp.float32),
            jax.ShapeDtypeStruct((near_count, local_width, BS), jnp.float32),
            jax.ShapeDtypeStruct((far_count, local_width, BS), jnp.bfloat16),
            jax.ShapeDtypeStruct((far_count, local_width, BS), jnp.bfloat16),
        ],
        compiler_params=pltpu.CompilerParams(
            dimension_semantics=("arbitrary", "arbitrary"), vmem_limit_bytes=48 * 1024 * 1024
        ),
        cost_estimate=cost,
    )(rows, counts, seeds, q, g, kt, vt, kf, vf)


def on_device(
    query_rows,
    key_rows,
    value_rows,
    out_grad,
    expander_device,
    expander_block,
    local_offset,
    live_count,
    drop_seed,
):
    head_count = lax.axis_size("head")
    head_index = lax.axis_index("head")
    share_rows = query_rows.shape[0]
    local_width = query_rows.shape[1] // head_count
    local_heads = drop_seed.shape[0]
    head_size = local_width // local_heads
    score_scale = head_size ** (-0.5)
    slot_count = 1 + L + E
    def to_columns(arrays):
        return lax.all_to_all(jnp.stack(arrays), "head", split_axis=2, concat_axis=1, tiled=True)

    key_local, value_local, query_local, grad_local = to_columns(
        [key_rows, value_rows, query_rows, out_grad]
    )
    peer_count = lax.axis_size("blk")
    capacity = min(QB_DEV, max(2, (2 * QB_DEV * E + peer_count - 1) // peer_count))
    flat_device = expander_device.reshape(-1)
    matches = (flat_device[:, None] == jnp.arange(peer_count, dtype=jnp.int32)[None, :]).astype(
        jnp.int32
    )
    before = jnp.cumsum(matches, axis=0) - matches
    slot_rank = jnp.sum(before * matches, axis=1)
    far_position = flat_device * capacity + slot_rank
    far_live = jnp.arange(E, dtype=jnp.int32)[None, :] < live_count[:, None]
    asked_block = jnp.where(far_live, expander_block, -1)
    listing = lax.all_gather(
        jnp.stack([flat_device, asked_block.reshape(-1)]), "blk", axis=0, tiled=False
    )
    hit = (listing[:, 0] == lax.axis_index("blk")).astype(jnp.int32)
    hit_rank = jnp.cumsum(hit, axis=1) - hit
    wanted_here = jnp.stack(
        [
            jnp.sum(jnp.where((hit > 0) & (hit_rank == r), listing[:, 1] + 1, 0), axis=1) - 1
            for r in range(capacity)
        ],
        axis=1,
    )
    key_blocks = key_local.reshape(QB_DEV, BS, local_width)
    value_blocks = value_local.reshape(QB_DEV, BS, local_width)
    stacked = jnp.stack([key_blocks, value_blocks], axis=1)
    widened = padded(stacked, (("blk", 0),), W)
    wanted_flat = wanted_here.reshape(-1)
    chosen = jnp.clip(wanted_flat, 0, QB_DEV - 1)
    asked_mask = (wanted_flat >= 0)[:, None, None]
    zero_block = jnp.zeros((), jnp.bfloat16)
    selection = (
        wanted_flat[:, None] == jnp.arange(QB_DEV, dtype=jnp.int32)[None, :]
    ).astype(jnp.bfloat16)

    def asked_of(blocks):
        return jnp.dot(
            selection, blocks.reshape(QB_DEV, -1), preferred_element_type=jnp.float32
        ).astype(jnp.bfloat16)
    reply_shape = (peer_count, capacity, BS, local_width)
    far_key, far_value = (
        lax.all_to_all(
            asked_of(key_blocks).reshape(reply_shape),
            "blk",
            split_axis=0,
            concat_axis=0,
            tiled=True,
        ),
        lax.all_to_all(
            asked_of(value_blocks).reshape(reply_shape),
            "blk",
            split_axis=0,
            concat_axis=0,
            tiled=True,
        ),
    )
    near_count = QB_DEV + 2 * W
    far_total_count = peer_count * capacity
    local_block = jnp.arange(QB_DEV, dtype=jnp.int32)[:, None]
    self_slot = local_block + W
    near_slot = local_block + W + local_offset
    far_slot = near_count + far_position.reshape(QB_DEV, E)
    table_rows = jnp.concatenate([self_slot, near_slot, far_slot], axis=1)
    slot_number = jnp.arange(slot_count, dtype=jnp.int32)[None, :]
    live_slots = (slot_number <= L) | (slot_number - 1 - L < live_count[:, None])
    slot_rows = table_rows.reshape(-1).astype(jnp.int32)
    seed_flat = drop_seed.reshape(-1).astype(jnp.int32)

    pair_out, nk, nv, fk, fv = block_attention(
        slot_rows,
        live_count.astype(jnp.int32),
        seed_flat,
        query_local,
        grad_local,
        widened[:, 0].reshape(near_count * BS, local_width),
        widened[:, 1].reshape(near_count * BS, local_width),
        far_key.reshape(far_total_count * BS, local_width),
        far_value.reshape(far_total_count * BS, local_width),
        near_count=near_count,
        far_count=far_total_count,
        scale=score_scale,
        head_size=head_size,
    )
    column_shape = (peer_count, capacity, local_width, BS)
    back_key, back_value = (
        lax.all_to_all(fk.reshape(column_shape), "blk", split_axis=0, concat_axis=0, tiled=True),
        lax.all_to_all(fv.reshape(column_shape), "blk", split_axis=0, concat_axis=0, tiled=True),
    )
    owner_match = (
        jnp.arange(QB_DEV, dtype=jnp.int32)[:, None] == wanted_here.reshape(1, -1)
    ).astype(jnp.bfloat16)
    far_key_sum = jnp.dot(
        owner_match,
        back_key.reshape(far_total_count, BS * local_width),
        preferred_element_type=jnp.float32,
    ).reshape(QB_DEV, local_width, BS)
    far_value_sum = jnp.dot(
        owner_match,
        back_value.reshape(far_total_count, BS * local_width),
        preferred_element_type=jnp.float32,
    ).reshape(QB_DEV, local_width, BS)
    near_total = jnp.stack([nk, nv], axis=1)
    from_below = shifted(near_total[QB_DEV + W :].astype(jnp.bfloat16), "blk", 1).astype(
        jnp.float32
    )
    from_above = shifted(near_total[:W].astype(jnp.bfloat16), "blk", -1).astype(jnp.float32)
    own_total = near_total[W : W + QB_DEV]
    own_total = own_total.at[:W].add(from_below)
    own_total = own_total.at[QB_DEV - W :].add(from_above)
    block_rows = QB_DEV * BS
    key_grad = (own_total[:, 0] + far_key_sum).astype(jnp.bfloat16).transpose(0, 2, 1)
    value_grad = (own_total[:, 1] + far_value_sum).astype(jnp.bfloat16).transpose(0, 2, 1)
    def to_rows(arrays):
        return lax.all_to_all(jnp.stack(arrays), "head", split_axis=1, concat_axis=2, tiled=True)

    pair_back = lax.all_to_all(pair_out, "head", split_axis=1, concat_axis=2, tiled=True)
    attended, query_grad = pair_back[0], pair_back[1]
    key_grad, value_grad = to_rows([
        key_grad.reshape(block_rows, local_width),
        value_grad.reshape(block_rows, local_width),
    ])
    return attended, query_grad, key_grad, value_grad


def solution(mesh):
    in_specs = (
        P(("blk", "head"), None),
        P(("blk", "head"), None),
        P(("blk", "head"), None),
        P(("blk", "head"), None),
        P("blk", None),
        P("blk", None),
        P("blk", None),
        P("blk"),
        P("head", "blk", None),
    )
    out_specs = (
        P(("blk", "head"), None),
        P(("blk", "head"), None),
        P(("blk", "head"), None),
        P(("blk", "head"), None),
    )
    return jax.shard_map(
        on_device, mesh=mesh, in_specs=in_specs, out_specs=out_specs, check_vma=False
    )
```
